128 devices in a mesh: bx: 16 (over z, y), by: 8 (over x, core).
Axes of the slice: x: 4, y: 4, z: 4, core: 2. Of those that a mesh axis runs over, the one named last changes fastest.
Arguments:
- views: bfloat16 [4, 1024, 512, 128], P(None, ('bx', 'by')), may hold values from 0.25 to 4
- offsets: int32 [4, 2], replicated, may hold values from -16 to 16, as said below
- background: float32 [4], replicated, may hold values from 0.5 to 2
- psf_x: float32 [4, 9], replicated, may hold values from 0.1 to 1
- psf_y: float32 [4, 9], replicated, may hold values from 0.1 to 1
- psf_z: float32 [4, 21], replicated, may hold values from 0.1 to 1
- start: float32 [1024, 512, 128], P('bx', 'by'), may hold values from 0.5 to 2
Outputs:
- estimate: float32 [1024, 512, 128], P('bx', 'by')
The draws below stay inside these ranges and needn't reach their ends.
Inputs may be any that keep to these rules, and one draw needn't show every extreme that they name: Every offset is nonzero; view 0 has offsets (-16, -16), view 3 has (16, 16), view 1 has a positive first and a negative second offset, view 2 the reverse.
All inputs are finite; a program needn't handle non-finite values.
Results may differ from the reference program's by a relative error of at most 0.0003.
Values may be sent and summed in bfloat16 or wider, within the bound.
No kernel may reach another device: no remote copies, remote signals or barrier semaphores. Data moves between devices by JAX's collectives and lax.ppermute only.
A program may use at most 128 MiB of HBM per device.

```python
import math
import jax
import jax.numpy as jnp
from jax import lax

V = 4
SHIFT = 16
KXY = 9
KZ = 21
ITERS = 2
NZ = 128
NX = 1024
NY = 512


def draw_offsets(key, part):
    magnitudes = jax.random.randint(key, (V, 2), 1, SHIFT + 1).astype(jnp.int32)
    magnitudes = magnitudes.at[0].set(SHIFT).at[3].set(SHIFT)
    signs = jnp.array([[-1, -1], [1, -1], [-1, 1], [1, 1]], jnp.int32)
    return (magnitudes * signs).astype(jnp.int32)


def shard_levels(key, shape, split, least, top_value):
    def one(axis_at, shards_of):
        steps = jax.random.uniform(jax.random.fold_in(jax.random.fold_in(key, 6), axis_at), (shards_of,), jnp.float32, least / len(split), top_value / len(split))
        return jnp.repeat(jnp.exp(steps), shape[axis_at] // shards_of).reshape((-1,) + (1,) * (len(shape) - axis_at - 1))

    factor_of = one(*split[0])
    for cut in split[1:]:
        factor_of = factor_of * one(*cut)
    return factor_of


def setup_inputs(seed: int = 0) -> dict:
    arg_keys = jax.random.split(jax.random.key(seed), 8)
    return {
        "views": jnp.clip(jnp.exp(math.log(4.0) - 2.7725887 * jax.random.uniform(arg_keys[0], (V, NX, NY, NZ), jnp.float32) ** shard_levels(arg_keys[0], (V, NX, NY, NZ), ((1, 128),), -0.2, 0.2)), 0.25, 4.0).astype(jnp.bfloat16),
        "offsets": draw_offsets(jax.random.fold_in(arg_keys[7], 71), 0),
        "background": jnp.clip(jnp.exp(jax.random.uniform(arg_keys[2], (V,), jnp.float32, math.log(0.5), math.log(2.0))), 0.5, 2.0),
        "psf_x": jnp.clip(jnp.exp(jax.random.uniform(arg_keys[3], (V, KXY), jnp.float32, math.log(0.1), math.log(1.0))), 0.1, 1.0),
        "psf_y": jnp.clip(jnp.exp(jax.random.uniform(arg_keys[4], (V, KXY), jnp.float32, math.log(0.1), math.log(1.0))), 0.1, 1.0),
        "psf_z": jnp.clip(jnp.exp(jax.random.uniform(arg_keys[5], (V, KZ), jnp.float32, math.log(0.1), math.log(1.0))), 0.1, 1.0),
        "start": jnp.clip(jnp.exp(math.log(2.0) - 1.3862944 * jax.random.uniform(arg_keys[6], (NX, NY, NZ), jnp.float32) ** shard_levels(arg_keys[6], (NX, NY, NZ), ((0, 16), (1, 8)), -0.2, 0.2)), 0.5, 2.0),
    }


def depth_band(tap_row, extent):
    length = tap_row.shape[0]
    middle = (length - 1) // 2
    distance = jnp.arange(extent)[:, None] - jnp.arange(extent)[None, :] + middle
    picked = distance[:, :, None] == jnp.arange(length)[None, None, :]
    return jnp.sum(jnp.where(picked, tap_row[None, None, :], 0.0), axis=2)


def along(field, tap_row, axis):
    length = tap_row.shape[0]
    middle = (length - 1) // 2
    extent = field.shape[axis]
    widths = [(0, 0), (0, 0), (0, 0)]
    widths[axis] = (middle, middle)
    padded = jnp.pad(field, widths)
    result = jnp.zeros_like(field)
    for lag_index in range(length):
        result = result + tap_row[lag_index] * lax.slice_in_dim(padded, lag_index, lag_index + extent, axis=axis)
    return result


def forward(field, taps_x, taps_y, taps_z):
    result = along(along(field, taps_x, 0), taps_y, 1)
    return jnp.einsum('xyj,ji->xyi', result, depth_band(taps_z, result.shape[2]), precision=lax.Precision.HIGHEST)


def reference(views, offsets, background, psf_x, psf_y, psf_z, start):
    coord_x = jnp.arange(NX)
    coord_y = jnp.arange(NY)
    weight = jnp.zeros(start.shape, jnp.float32)
    kernels = []
    registered = []
    for which in range(V):
        taps_x = psf_x[which] / jnp.sum(psf_x[which])
        taps_y = psf_y[which] / jnp.sum(psf_y[which])
        taps_z = psf_z[which] / jnp.sum(psf_z[which])
        kernels.append((taps_x, taps_y, taps_z))
        padded = jnp.pad(views[which], ((SHIFT, SHIFT), (SHIFT, SHIFT), (0, 0)))
        moved = lax.dynamic_slice(padded, (SHIFT + offsets[which, 0], SHIFT + offsets[which, 1], jnp.int32(0)), (NX, NY, NZ))
        registered.append(moved)
        inside_x = ((coord_x + offsets[which, 0] >= 0) & (coord_x + offsets[which, 0] < NX)).astype(jnp.float32)
        inside_y = ((coord_y + offsets[which, 1] >= 0) & (coord_y + offsets[which, 1] < NY)).astype(jnp.float32)
        cover = jnp.broadcast_to((inside_x[:, None] * inside_y[None, :])[:, :, None], (NX, NY, NZ))
        weight = weight + forward(cover, taps_x[::-1], taps_y[::-1], taps_z[::-1])
    estimate = start
    for sweep in range(ITERS):
        summed = jnp.zeros(start.shape, jnp.float32)
        for which in range(V):
            taps_x, taps_y, taps_z = kernels[which]
            blurred = forward(estimate, taps_x, taps_y, taps_z)
            ratios = registered[which].astype(jnp.float32) / (blurred + background[which])
            summed = summed + forward(ratios, taps_x[::-1], taps_y[::-1], taps_z[::-1])
        estimate = estimate * summed / weight
    return estimate
```

```python
import jax
import jax.numpy as jnp
from jax import lax
from jax.sharding import PartitionSpec as P

V = 4
SHIFT = 16
ITERS = 2
HIGHEST = lax.Precision.HIGHEST


def shift_pairs(count, step):
    if step > 0:
        return [(i, i + step) for i in range(count - step)]
    return [(i - step, i) for i in range(count + step)]


def halo_2d(block, width):
    nx = lax.axis_size("bx")
    ny = lax.axis_size("by")
    low = block.astype(jnp.bfloat16)
    w = width
    up = lax.ppermute(low[-w:], "bx", shift_pairs(nx, 1))
    down = lax.ppermute(low[:w], "bx", shift_pairs(nx, -1))
    left = lax.ppermute(low[:, -w:], "by", shift_pairs(ny, 1))
    right = lax.ppermute(low[:, :w], "by", shift_pairs(ny, -1))

    def corner(part, dx, dy):
        pairs = []
        for i in range(nx):
            for j in range(ny):
                ti, tj = i + dx, j + dy
                if 0 <= ti < nx and 0 <= tj < ny:
                    pairs.append((i * ny + j, ti * ny + tj))
        return lax.ppermute(part, ("bx", "by"), pairs)

    up_left = corner(low[-w:, -w:], 1, 1)
    up_right = corner(low[-w:, :w], 1, -1)
    down_left = corner(low[:w, -w:], -1, 1)
    down_right = corner(low[:w, :w], -1, -1)
    f = block.dtype
    top = jnp.concatenate([up_left, up, up_right], axis=1).astype(f)
    mid = jnp.concatenate([left.astype(f), block, right.astype(f)], axis=1)
    bottom = jnp.concatenate([down_left, down, down_right], axis=1).astype(f)
    return jnp.concatenate([top, mid, bottom], axis=0)


def band_rows(taps, extent):
    length = taps.shape[1]
    distance = jnp.arange(extent + length - 1)[None, :] - jnp.arange(extent)[:, None]
    picked = distance[:, :, None] == jnp.arange(length)[None, None, :]
    return jnp.sum(jnp.where(picked[None], taps[:, None, None, :], 0.0), axis=3)


def depth_band(taps, extent):
    length = taps.shape[1]
    middle = (length - 1) // 2
    distance = jnp.arange(extent)[:, None] - jnp.arange(extent)[None, :] + middle
    picked = distance[:, :, None] == jnp.arange(length)[None, None, :]
    return jnp.sum(jnp.where(picked[None], taps[:, None, None, :], 0.0), axis=3)


def local(views, offsets, background, psf_x, psf_y, psf_z, start):
    rows_x, rows_y, depth = start.shape
    nx = lax.axis_size("bx")
    ny = lax.axis_size("by")
    full_x = rows_x * nx
    full_y = rows_y * ny
    middle = (psf_x.shape[1] - 1) // 2
    h = middle
    ix = lax.axis_index("bx")
    iy = lax.axis_index("by")

    padded_start = halo_2d(start, 2 * h)

    pad_y = SHIFT + h
    vpad = jnp.pad(views, ((0, 0), (0, 0), (pad_y, pad_y), (0, 0)))
    cols = full_y + 2 * h
    shifted = jnp.stack(
        [
            lax.dynamic_slice_in_dim(vpad[w], SHIFT + offsets[w, 1], cols, axis=1)
            for w in range(V)
        ]
    )
    chunks = jnp.concatenate(
        [shifted[:, :, k * rows_y : k * rows_y + rows_y + 2 * h] for k in range(ny)], axis=2
    )
    routed = lax.all_to_all(chunks, "by", split_axis=2, concat_axis=1, tiled=True)

    reach = SHIFT + h
    prev_rows = (reach, h, reach, 0)
    next_rows = (0, reach, h, reach)
    prev_send = jnp.concatenate(
        [routed[w, rows_x - prev_rows[w] :] for w in range(V) if prev_rows[w]], axis=0
    )
    next_send = jnp.concatenate(
        [routed[w, : next_rows[w]] for w in range(V) if next_rows[w]], axis=0
    )
    prev_got = lax.ppermute(prev_send, "bx", shift_pairs(nx, 1))
    next_got = lax.ppermute(next_send, "bx", shift_pairs(nx, -1))

    base_x = ix * rows_x - h + jnp.arange(rows_x + 2 * h, dtype=jnp.int32)
    base_y = iy * rows_y - h + jnp.arange(rows_y + 2 * h, dtype=jnp.int32)
    inside_x = (base_x >= 0) & (base_x < full_x)
    inside_y = (base_y >= 0) & (base_y < full_y)
    inside = inside_x[:, None] & inside_y[None, :]

    registered = []
    at_prev = 0
    at_next = 0
    for w in range(V):
        parts = []
        if prev_rows[w]:
            parts.append(prev_got[at_prev : at_prev + prev_rows[w]])
            at_prev += prev_rows[w]
        parts.append(routed[w])
        if next_rows[w]:
            parts.append(next_got[at_next : at_next + next_rows[w]])
            at_next += next_rows[w]
        ext = jnp.concatenate(parts, axis=0)
        moved = lax.dynamic_slice_in_dim(
            ext, prev_rows[w] - h + offsets[w, 0], rows_x + 2 * h, axis=0
        )
        registered.append(jnp.where(inside[:, :, None], moved, jnp.zeros((), moved.dtype)))
    registered = jnp.stack(registered)

    taps_x = psf_x / jnp.sum(psf_x, axis=1, keepdims=True)
    taps_y = psf_y / jnp.sum(psf_y, axis=1, keepdims=True)
    taps_z = psf_z / jnp.sum(psf_z, axis=1, keepdims=True)
    fwd_x = band_rows(taps_x, rows_x + 2 * h)
    fwd_y = band_rows(taps_y, rows_y + 2 * h)
    fwd_z = depth_band(taps_z, depth)
    adj_x = band_rows(taps_x[:, ::-1], rows_x)
    adj_y = band_rows(taps_y[:, ::-1], rows_y)
    adj_z = jnp.swapaxes(fwd_z, 1, 2)

    cover_x = (
        (base_x[None, :] + offsets[:, 0:1] >= 0) & (base_x[None, :] + offsets[:, 0:1] < full_x)
    ) & inside_x[None, :]
    cover_y = (
        (base_y[None, :] + offsets[:, 1:2] >= 0) & (base_y[None, :] + offsets[:, 1:2] < full_y)
    ) & inside_y[None, :]
    weight_x = jnp.einsum("vij,vj->vi", adj_x, cover_x.astype(jnp.float32), precision=HIGHEST)
    weight_y = jnp.einsum("vij,vj->vi", adj_y, cover_y.astype(jnp.float32), precision=HIGHEST)
    weight_z = jnp.sum(adj_z, axis=1)
    weight = jnp.einsum("vx,vy,vz->xyz", weight_x, weight_y, weight_z, precision=HIGHEST)

    bg = background[:, None, None, None]
    estimate = start
    for sweep in range(ITERS):
        field = padded_start if sweep == 0 else halo_2d(estimate, 2 * h)
        first = jnp.einsum("vij,jyz->viyz", fwd_x, field, precision=HIGHEST)
        second = jnp.einsum("vij,vxjz->vxiz", fwd_y, first, precision=HIGHEST)
        blurred = jnp.einsum("vxyj,vji->vxyi", second, fwd_z, precision=HIGHEST)
        ratio = registered.astype(jnp.float32) / (blurred + bg)
        back_x = jnp.einsum("vij,vjyz->viyz", adj_x, ratio, precision=HIGHEST)
        back_y = jnp.einsum("vij,vxjz->vxiz", adj_y, back_x, precision=HIGHEST)
        summed = jnp.einsum("vxyj,vji->xyi", back_y, adj_z, precision=HIGHEST)
        estimate = estimate * summed / weight
    return estimate


def solution(mesh):
    return jax.shard_map(
        local,
        mesh=mesh,
        in_specs=(P(None, ("bx", "by"), None, None), P(), P(), P(), P(), P(), P("bx", "by", None)),
        out_specs=P("bx", "by", None),
        check_vma=False,
    )
```

```python
import jax
import jax.numpy as jnp
from jax import lax
from jax.sharding import PartitionSpec as P
from jax.experimental import pallas as pl
from jax.experimental.pallas import tpu as pltpu

V = 4
SHIFT = 16
ITERS = 2
HIGHEST = lax.Precision.HIGHEST


def shift_pairs(count, step):
    if step > 0:
        return [(i, i + step) for i in range(count - step)]
    return [(i - step, i) for i in range(count + step)]


def halo_2d(block, width):
    nx = lax.axis_size("bx")
    ny = lax.axis_size("by")
    low = block.astype(jnp.bfloat16)
    w = width
    up = lax.ppermute(low[-w:], "bx", shift_pairs(nx, 1))
    down = lax.ppermute(low[:w], "bx", shift_pairs(nx, -1))
    left = lax.ppermute(low[:, -w:], "by", shift_pairs(ny, 1))
    right = lax.ppermute(low[:, :w], "by", shift_pairs(ny, -1))

    def corner(part, dx, dy):
        pairs = []
        for i in range(nx):
            for j in range(ny):
                ti, tj = i + dx, j + dy
                if 0 <= ti < nx and 0 <= tj < ny:
                    pairs.append((i * ny + j, ti * ny + tj))
        return lax.ppermute(part, ("bx", "by"), pairs)

    up_left = corner(low[-w:, -w:], 1, 1)
    up_right = corner(low[-w:, :w], 1, -1)
    down_left = corner(low[:w, -w:], -1, 1)
    down_right = corner(low[:w, :w], -1, -1)
    f = block.dtype
    top = jnp.concatenate([up_left, up, up_right], axis=1).astype(f)
    mid = jnp.concatenate([left.astype(f), block, right.astype(f)], axis=1)
    bottom = jnp.concatenate([down_left, down, down_right], axis=1).astype(f)
    return jnp.concatenate([top, mid, bottom], axis=0)


def band_rows(taps, extent):
    length = taps.shape[1]
    distance = jnp.arange(extent + length - 1)[None, :] - jnp.arange(extent)[:, None]
    picked = distance[:, :, None] == jnp.arange(length)[None, None, :]
    return jnp.sum(jnp.where(picked[None], taps[:, None, None, :], 0.0), axis=3)


def depth_band(taps, extent):
    length = taps.shape[1]
    middle = (length - 1) // 2
    distance = jnp.arange(extent)[:, None] - jnp.arange(extent)[None, :] + middle
    picked = distance[:, :, None] == jnp.arange(length)[None, None, :]
    return jnp.sum(jnp.where(picked[None], taps[:, None, None, :], 0.0), axis=3)


def rl_step(field, registered, estimate, weight, taps_x, taps_y, bg, fwd_z, adj_z):
    views, rows_r, cols_r, depth = registered.shape
    rows, cols = estimate.shape[:2]
    rows_f, cols_f = field.shape[:2]
    taps = taps_x.shape[1]
    chunk = 4
    f32 = jnp.float32

    def kernel(tx_ref, ty_ref, bg_ref, field_ref, reg_ref, est_ref, w_ref, fz_ref, az_ref,
               out_ref, q_ref, t1_ref, t2_ref, s_ref):
        v = pl.program_id(0)

        def forward_rows(c, carry):
            r0 = pl.multiple_of(c * chunk, chunk)
            acc = tx_ref[v, 0] * field_ref[pl.ds(r0, chunk)]
            for a in range(1, taps):
                acc = acc + tx_ref[v, a] * field_ref[pl.ds(r0 + a, chunk)]
            t1_ref[...] = acc
            acc2 = ty_ref[v, 0] * t1_ref[:, pl.ds(0, cols_r), :]
            for b in range(1, taps):
                acc2 = acc2 + ty_ref[v, b] * t1_ref[:, pl.ds(b, cols_r), :]
            blurred = jnp.dot(acc2.reshape(chunk * cols_r, depth), fz_ref[0],
                              precision=HIGHEST, preferred_element_type=f32)
            reg = reg_ref[0, pl.ds(r0, chunk)].astype(f32).reshape(chunk * cols_r, depth)
            ratio = reg / (blurred + bg_ref[v])
            back = jnp.dot(ratio, az_ref[0], precision=HIGHEST, preferred_element_type=f32)
            q_ref[pl.ds(r0, chunk)] = back.reshape(chunk, cols_r, depth)
            return carry

        lax.fori_loop(0, rows_r // chunk, forward_rows, 0)

        def adjoint_rows(c, carry):
            r0 = pl.multiple_of(c * chunk, chunk)
            acc = tx_ref[v, taps - 1] * q_ref[pl.ds(r0, chunk)]
            for a in range(1, taps):
                acc = acc + tx_ref[v, taps - 1 - a] * q_ref[pl.ds(r0 + a, chunk)]
            t2_ref[...] = acc
            acc2 = ty_ref[v, taps - 1] * t2_ref[:, pl.ds(0, cols), :]
            for b in range(1, taps):
                acc2 = acc2 + ty_ref[v, taps - 1 - b] * t2_ref[:, pl.ds(b, cols), :]
            rs = pl.ds(r0, chunk)

            @pl.when(v == 0)
            def _():
                s_ref[rs] = acc2

            @pl.when((v > 0) & (v < views - 1))
            def _():
                s_ref[rs] = s_ref[rs] + acc2

            @pl.when(v == views - 1)
            def _():
                out_ref[rs] = est_ref[rs] * (s_ref[rs] + acc2) / w_ref[rs]

            return carry

        lax.fori_loop(0, rows // chunk, adjoint_rows, 0)

    smem = pl.BlockSpec(memory_space=pltpu.SMEM)
    whole3 = lambda shape: pl.BlockSpec(shape, lambda v: (0, 0, 0))
    return pl.pallas_call(
        kernel,
        grid=(views,),
        in_specs=[
            smem,
            smem,
            smem,
            whole3(field.shape),
            pl.BlockSpec((1, rows_r, cols_r, depth), lambda v: (v, 0, 0, 0)),
            whole3(estimate.shape),
            whole3(weight.shape),
            pl.BlockSpec((1, depth, depth), lambda v: (v, 0, 0)),
            pl.BlockSpec((1, depth, depth), lambda v: (v, 0, 0)),
        ],
        out_specs=whole3(estimate.shape),
        out_shape=jax.ShapeDtypeStruct(estimate.shape, f32),
        scratch_shapes=[
            pltpu.VMEM((rows_r, cols_r, depth), f32),
            pltpu.VMEM((chunk, cols_f, depth), f32),
            pltpu.VMEM((chunk, cols_r, depth), f32),
            pltpu.VMEM((rows, cols, depth), f32),
        ],
        compiler_params=pltpu.CompilerParams(dimension_semantics=("arbitrary",)),
    )(taps_x, taps_y, bg, field, registered, estimate, weight, fwd_z, adj_z)


def local(views, offsets, background, psf_x, psf_y, psf_z, start):
    rows_x, rows_y, depth = start.shape
    nx = lax.axis_size("bx")
    ny = lax.axis_size("by")
    full_x = rows_x * nx
    full_y = rows_y * ny
    middle = (psf_x.shape[1] - 1) // 2
    h = middle
    ix = lax.axis_index("bx")
    iy = lax.axis_index("by")

    padded_start = halo_2d(start, 2 * h)

    pad_y = SHIFT + h
    vpad = jnp.pad(views, ((0, 0), (0, 0), (pad_y, pad_y), (0, 0)))
    cols = full_y + 2 * h
    shifted = jnp.stack(
        [
            lax.dynamic_slice_in_dim(vpad[w], SHIFT + offsets[w, 1], cols, axis=1)
            for w in range(V)
        ]
    )
    chunks = jnp.concatenate(
        [shifted[:, :, k * rows_y : k * rows_y + rows_y + 2 * h] for k in range(ny)], axis=2
    )
    routed = lax.all_to_all(chunks, "by", split_axis=2, concat_axis=1, tiled=True)

    reach = SHIFT + h
    prev_rows = (reach, h, reach, 0)
    next_rows = (0, reach, h, reach)
    prev_send = jnp.concatenate(
        [routed[w, rows_x - prev_rows[w] :] for w in range(V) if prev_rows[w]], axis=0
    )
    next_send = jnp.concatenate(
        [routed[w, : next_rows[w]] for w in range(V) if next_rows[w]], axis=0
    )
    prev_got = lax.ppermute(prev_send, "bx", shift_pairs(nx, 1))
    next_got = lax.ppermute(next_send, "bx", shift_pairs(nx, -1))

    base_x = ix * rows_x - h + jnp.arange(rows_x + 2 * h, dtype=jnp.int32)
    base_y = iy * rows_y - h + jnp.arange(rows_y + 2 * h, dtype=jnp.int32)
    inside_x = (base_x >= 0) & (base_x < full_x)
    inside_y = (base_y >= 0) & (base_y < full_y)
    inside = inside_x[:, None] & inside_y[None, :]

    registered = []
    at_prev = 0
    at_next = 0
    for w in range(V):
        parts = []
        if prev_rows[w]:
            parts.append(prev_got[at_prev : at_prev + prev_rows[w]])
            at_prev += prev_rows[w]
        parts.append(routed[w])
        if next_rows[w]:
            parts.append(next_got[at_next : at_next + next_rows[w]])
            at_next += next_rows[w]
        ext = jnp.concatenate(parts, axis=0)
        moved = lax.dynamic_slice_in_dim(
            ext, prev_rows[w] - h + offsets[w, 0], rows_x + 2 * h, axis=0
        )
        registered.append(jnp.where(inside[:, :, None], moved, jnp.zeros((), moved.dtype)))
    registered = jnp.stack(registered)

    taps_x = psf_x / jnp.sum(psf_x, axis=1, keepdims=True)
    taps_y = psf_y / jnp.sum(psf_y, axis=1, keepdims=True)
    taps_z = psf_z / jnp.sum(psf_z, axis=1, keepdims=True)
    fwd_x = band_rows(taps_x, rows_x + 2 * h)
    fwd_y = band_rows(taps_y, rows_y + 2 * h)
    fwd_z = depth_band(taps_z, depth)
    adj_x = band_rows(taps_x[:, ::-1], rows_x)
    adj_y = band_rows(taps_y[:, ::-1], rows_y)
    adj_z = jnp.swapaxes(fwd_z, 1, 2)

    cover_x = (
        (base_x[None, :] + offsets[:, 0:1] >= 0) & (base_x[None, :] + offsets[:, 0:1] < full_x)
    ) & inside_x[None, :]
    cover_y = (
        (base_y[None, :] + offsets[:, 1:2] >= 0) & (base_y[None, :] + offsets[:, 1:2] < full_y)
    ) & inside_y[None, :]
    weight_x = jnp.einsum("vij,vj->vi", adj_x, cover_x.astype(jnp.float32), precision=HIGHEST)
    weight_y = jnp.einsum("vij,vj->vi", adj_y, cover_y.astype(jnp.float32), precision=HIGHEST)
    weight_z = jnp.sum(adj_z, axis=1)
    weight = jnp.einsum("vx,vy,vz->xyz", weight_x, weight_y, weight_z, precision=HIGHEST)

    estimate = start
    for sweep in range(ITERS):
        field = padded_start if sweep == 0 else halo_2d(estimate, 2 * h)
        estimate = rl_step(field, registered, estimate, weight, taps_x, taps_y, background,
                           fwd_z, adj_z)
    return estimate


def solution(mesh):
    return jax.shard_map(
        local,
        mesh=mesh,
        in_specs=(P(None, ("bx", "by"), None, None), P(), P(), P(), P(), P(), P("bx", "by", None)),
        out_specs=P("bx", "by", None),
        check_vma=False,
    )
```

```python
import jax
import jax.numpy as jnp
from jax import lax
from jax.sharding import PartitionSpec as P
from jax.experimental import pallas as pl
from jax.experimental.pallas import tpu as pltpu

V = 4
SHIFT = 16
ITERS = 2
HIGHEST = lax.Precision.HIGHEST
MATMUL = lax.Precision.HIGH
DEEP = 36


def shift_pairs(count, step):
    if step > 0:
        return [(i, i + step) for i in range(count - step)]
    return [(i - step, i) for i in range(count + step)]


def halo_2d(block, width):
    nx = lax.axis_size("bx")
    ny = lax.axis_size("by")
    low = block.astype(jnp.bfloat16)
    w = width
    up = lax.ppermute(low[-w:], "bx", shift_pairs(nx, 1))
    down = lax.ppermute(low[:w], "bx", shift_pairs(nx, -1))
    left = lax.ppermute(low[:, -w:], "by", shift_pairs(ny, 1))
    right = lax.ppermute(low[:, :w], "by", shift_pairs(ny, -1))

    def corner(part, dx, dy):
        pairs = []
        for i in range(nx):
            for j in range(ny):
                ti, tj = i + dx, j + dy
                if 0 <= ti < nx and 0 <= tj < ny:
                    pairs.append((i * ny + j, ti * ny + tj))
        return lax.ppermute(part, ("bx", "by"), pairs)

    up_left = corner(low[-w:, -w:], 1, 1)
    up_right = corner(low[-w:, :w], 1, -1)
    down_left = corner(low[:w, -w:], -1, 1)
    down_right = corner(low[:w, :w], -1, -1)
    f = block.dtype
    top = jnp.concatenate([up_left, up, up_right], axis=1).astype(f)
    mid = jnp.concatenate([left.astype(f), block, right.astype(f)], axis=1)
    bottom = jnp.concatenate([down_left, down, down_right], axis=1).astype(f)
    return jnp.concatenate([top, mid, bottom], axis=0)


def band_rows(taps, extent):
    length = taps.shape[1]
    distance = jnp.arange(extent + length - 1)[None, :] - jnp.arange(extent)[:, None]
    picked = distance[:, :, None] == jnp.arange(length)[None, None, :]
    return jnp.sum(jnp.where(picked[None], taps[:, None, None, :], 0.0), axis=3)


def depth_band(taps, extent):
    length = taps.shape[1]
    middle = (length - 1) // 2
    distance = jnp.arange(extent)[:, None] - jnp.arange(extent)[None, :] + middle
    picked = distance[:, :, None] == jnp.arange(length)[None, None, :]
    return jnp.sum(jnp.where(picked[None], taps[:, None, None, :], 0.0), axis=3)


def rl_step(field, registered, estimate, weight, taps_x, taps_y, bg, fwd_z, adj_z):
    views, rows_r, cols_r, depth = registered.shape
    rows, cols = estimate.shape[:2]
    rows_f, cols_f = field.shape[:2]
    taps = taps_x.shape[1]
    chunk = 4
    deep = DEEP
    f32 = jnp.float32

    def kernel(tx_ref, ty_ref, bg_ref, field_ref, reg_ref, est_ref, w_ref, fz_ref, az_ref,
               out_ref, q_ref, t1_ref, t2_ref, s_ref):
        v = pl.program_id(0)

        def forward_rows(c, carry):
            r0 = pl.multiple_of(c * chunk, chunk)
            acc = tx_ref[v, 0] * field_ref[pl.ds(r0, chunk)]
            for a in range(1, taps):
                acc = acc + tx_ref[v, a] * field_ref[pl.ds(r0 + a, chunk)]
            t1_ref[...] = acc
            acc2 = ty_ref[v, 0] * t1_ref[:, pl.ds(0, cols_r), :]
            for b in range(1, taps):
                acc2 = acc2 + ty_ref[v, b] * t1_ref[:, pl.ds(b, cols_r), :]
            q_ref[pl.ds(r0, chunk)] = acc2
            return carry

        lax.fori_loop(0, rows_r // chunk, forward_rows, 0)

        def depth_rows(c, carry):
            r0 = pl.multiple_of(c * deep, deep)
            flat = q_ref[pl.ds(r0, deep)].reshape(deep * cols_r, depth)
            blurred = jnp.dot(flat, fz_ref[0], precision=MATMUL, preferred_element_type=f32)
            reg = reg_ref[0, pl.ds(r0, deep)].astype(f32).reshape(deep * cols_r, depth)
            ratio = reg / (blurred + bg_ref[v])
            back = jnp.dot(ratio, az_ref[0], precision=MATMUL, preferred_element_type=f32)
            q_ref[pl.ds(r0, deep)] = back.reshape(deep, cols_r, depth)
            return carry

        lax.fori_loop(0, rows_r // deep, depth_rows, 0)

        def adjoint_rows(c, carry):
            r0 = pl.multiple_of(c * chunk, chunk)
            acc = tx_ref[v, taps - 1] * q_ref[pl.ds(r0, chunk)]
            for a in range(1, taps):
                acc = acc + tx_ref[v, taps - 1 - a] * q_ref[pl.ds(r0 + a, chunk)]
            t2_ref[...] = acc
            acc2 = ty_ref[v, taps - 1] * t2_ref[:, pl.ds(0, cols), :]
            for b in range(1, taps):
                acc2 = acc2 + ty_ref[v, taps - 1 - b] * t2_ref[:, pl.ds(b, cols), :]
            rs = pl.ds(r0, chunk)

            @pl.when(v == 0)
            def _():
                s_ref[rs] = acc2

            @pl.when((v > 0) & (v < views - 1))
            def _():
                s_ref[rs] = s_ref[rs] + acc2

            @pl.when(v == views - 1)
            def _():
                out_ref[rs] = est_ref[rs] * (s_ref[rs] + acc2) / w_ref[rs]

            return carry

        lax.fori_loop(0, rows // chunk, adjoint_rows, 0)

    smem = pl.BlockSpec(memory_space=pltpu.SMEM)
    whole3 = lambda shape: pl.BlockSpec(shape, lambda v: (0, 0, 0))
    return pl.pallas_call(
        kernel,
        grid=(views,),
        in_specs=[
            smem,
            smem,
            smem,
            whole3(field.shape),
            pl.BlockSpec((1, rows_r, cols_r, depth), lambda v: (v, 0, 0, 0)),
            whole3(estimate.shape),
            whole3(weight.shape),
            pl.BlockSpec((1, depth, depth), lambda v: (v, 0, 0)),
            pl.BlockSpec((1, depth, depth), lambda v: (v, 0, 0)),
        ],
        out_specs=whole3(estimate.shape),
        out_shape=jax.ShapeDtypeStruct(estimate.shape, f32),
        scratch_shapes=[
            pltpu.VMEM((rows_r, cols_r, depth), f32),
            pltpu.VMEM((chunk, cols_f, depth), f32),
            pltpu.VMEM((chunk, cols_r, depth), f32),
            pltpu.VMEM((rows, cols, depth), f32),
        ],
        compiler_params=pltpu.CompilerParams(dimension_semantics=("arbitrary",)),
    )(taps_x, taps_y, bg, field, registered, estimate, weight, fwd_z, adj_z)


def local(views, offsets, background, psf_x, psf_y, psf_z, start):
    rows_x, rows_y, depth = start.shape
    nx = lax.axis_size("bx")
    ny = lax.axis_size("by")
    full_x = rows_x * nx
    full_y = rows_y * ny
    middle = (psf_x.shape[1] - 1) // 2
    h = middle
    ix = lax.axis_index("bx")
    iy = lax.axis_index("by")

    padded_start = halo_2d(start, 2 * h)

    pad_y = SHIFT + h
    vpad = jnp.pad(views, ((0, 0), (0, 0), (pad_y, pad_y), (0, 0)))
    cols = full_y + 2 * h
    shifted = jnp.stack(
        [
            lax.dynamic_slice_in_dim(vpad[w], SHIFT + offsets[w, 1], cols, axis=1)
            for w in range(V)
        ]
    )
    chunks = jnp.concatenate(
        [shifted[:, :, k * rows_y : k * rows_y + rows_y + 2 * h] for k in range(ny)], axis=2
    )
    routed = lax.all_to_all(chunks, "by", split_axis=2, concat_axis=1, tiled=True)

    reach = SHIFT + h
    prev_rows = (reach, h, reach, 0)
    next_rows = (0, reach, h, reach)
    prev_send = jnp.concatenate(
        [routed[w, rows_x - prev_rows[w] :] for w in range(V) if prev_rows[w]], axis=0
    )
    next_send = jnp.concatenate(
        [routed[w, : next_rows[w]] for w in range(V) if next_rows[w]], axis=0
    )
    prev_got = lax.ppermute(prev_send, "bx", shift_pairs(nx, 1))
    next_got = lax.ppermute(next_send, "bx", shift_pairs(nx, -1))

    base_x = ix * rows_x - h + jnp.arange(rows_x + 2 * h, dtype=jnp.int32)
    base_y = iy * rows_y - h + jnp.arange(rows_y + 2 * h, dtype=jnp.int32)
    inside_x = (base_x >= 0) & (base_x < full_x)
    inside_y = (base_y >= 0) & (base_y < full_y)
    inside = inside_x[:, None] & inside_y[None, :]

    registered = []
    at_prev = 0
    at_next = 0
    for w in range(V):
        parts = []
        if prev_rows[w]:
            parts.append(prev_got[at_prev : at_prev + prev_rows[w]])
            at_prev += prev_rows[w]
        parts.append(routed[w])
        if next_rows[w]:
            parts.append(next_got[at_next : at_next + next_rows[w]])
            at_next += next_rows[w]
        ext = jnp.concatenate(parts, axis=0)
        moved = lax.dynamic_slice_in_dim(
            ext, prev_rows[w] - h + offsets[w, 0], rows_x + 2 * h, axis=0
        )
        registered.append(jnp.where(inside[:, :, None], moved, jnp.zeros((), moved.dtype)))
    registered = jnp.stack(registered)

    taps_x = psf_x / jnp.sum(psf_x, axis=1, keepdims=True)
    taps_y = psf_y / jnp.sum(psf_y, axis=1, keepdims=True)
    taps_z = psf_z / jnp.sum(psf_z, axis=1, keepdims=True)
    fwd_x = band_rows(taps_x, rows_x + 2 * h)
    fwd_y = band_rows(taps_y, rows_y + 2 * h)
    fwd_z = depth_band(taps_z, depth)
    adj_x = band_rows(taps_x[:, ::-1], rows_x)
    adj_y = band_rows(taps_y[:, ::-1], rows_y)
    adj_z = jnp.swapaxes(fwd_z, 1, 2)

    cover_x = (
        (base_x[None, :] + offsets[:, 0:1] >= 0) & (base_x[None, :] + offsets[:, 0:1] < full_x)
    ) & inside_x[None, :]
    cover_y = (
        (base_y[None, :] + offsets[:, 1:2] >= 0) & (base_y[None, :] + offsets[:, 1:2] < full_y)
    ) & inside_y[None, :]
    weight_x = jnp.einsum("vij,vj->vi", adj_x, cover_x.astype(jnp.float32), precision=HIGHEST)
    weight_y = jnp.einsum("vij,vj->vi", adj_y, cover_y.astype(jnp.float32), precision=HIGHEST)
    weight_z = jnp.sum(adj_z, axis=1)
    weight = jnp.einsum("vx,vy,vz->xyz", weight_x, weight_y, weight_z, precision=HIGHEST)

    estimate = start
    for sweep in range(ITERS):
        field = padded_start if sweep == 0 else halo_2d(estimate, 2 * h)
        estimate = rl_step(field, registered, estimate, weight, taps_x, taps_y, background,
                           fwd_z, adj_z)
    return estimate


def solution(mesh):
    return jax.shard_map(
        local,
        mesh=mesh,
        in_specs=(P(None, ("bx", "by"), None, None), P(), P(), P(), P(), P(), P("bx", "by", None)),
        out_specs=P("bx", "by", None),
        check_vma=False,
    )
```

```python
import jax
import jax.numpy as jnp
from jax import lax
from jax.sharding import PartitionSpec as P
from jax.experimental import pallas as pl
from jax.experimental.pallas import tpu as pltpu

V = 4
SHIFT = 16
ITERS = 2
HIGHEST = lax.Precision.HIGHEST
MATMUL = lax.Precision.HIGH
DEEP = 36


def shift_pairs(count, step):
    if step > 0:
        return [(i, i + step) for i in range(count - step)]
    return [(i - step, i) for i in range(count + step)]


def halo_2d(block, width):
    nx = lax.axis_size("bx")
    ny = lax.axis_size("by")
    low = block.astype(jnp.bfloat16)
    w = width
    up = lax.ppermute(low[-w:], "bx", shift_pairs(nx, 1))
    down = lax.ppermute(low[:w], "bx", shift_pairs(nx, -1))
    left = lax.ppermute(low[:, -w:], "by", shift_pairs(ny, 1))
    right = lax.ppermute(low[:, :w], "by", shift_pairs(ny, -1))

    def corner(part, dx, dy):
        pairs = []
        for i in range(nx):
            for j in range(ny):
                ti, tj = i + dx, j + dy
                if 0 <= ti < nx and 0 <= tj < ny:
                    pairs.append((i * ny + j, ti * ny + tj))
        return lax.ppermute(part, ("bx", "by"), pairs)

    up_left = corner(low[-w:, -w:], 1, 1)
    up_right = corner(low[-w:, :w], 1, -1)
    down_left = corner(low[:w, -w:], -1, 1)
    down_right = corner(low[:w, :w], -1, -1)
    f = block.dtype
    top = jnp.concatenate([up_left, up, up_right], axis=1).astype(f)
    mid = jnp.concatenate([left.astype(f), block, right.astype(f)], axis=1)
    bottom = jnp.concatenate([down_left, down, down_right], axis=1).astype(f)
    return jnp.concatenate([top, mid, bottom], axis=0)


def band_rows(taps, extent):
    length = taps.shape[1]
    distance = jnp.arange(extent + length - 1)[None, :] - jnp.arange(extent)[:, None]
    picked = distance[:, :, None] == jnp.arange(length)[None, None, :]
    return jnp.sum(jnp.where(picked[None], taps[:, None, None, :], 0.0), axis=3)


def depth_band(taps, extent):
    length = taps.shape[1]
    middle = (length - 1) // 2
    distance = jnp.arange(extent)[:, None] - jnp.arange(extent)[None, :] + middle
    picked = distance[:, :, None] == jnp.arange(length)[None, None, :]
    return jnp.sum(jnp.where(picked[None], taps[:, None, None, :], 0.0), axis=3)


def conv_xy(src_ref, t_ref, dst_ref, tx_ref, ty_ref, v, flip, count, chunk, taps, cols_out,
            finish=None):
    def tap(ref, k):
        return ref[v, taps - 1 - k] if flip else ref[v, k]

    def rows(c, carry):
        r0 = pl.multiple_of(c * chunk, chunk)
        acc = tap(tx_ref, 0) * src_ref[pl.ds(r0, chunk)]
        for a in range(1, taps):
            acc = acc + tap(tx_ref, a) * src_ref[pl.ds(r0 + a, chunk)]
        t_ref[...] = acc
        acc2 = tap(ty_ref, 0) * t_ref[:, pl.ds(0, cols_out), :]
        for b in range(1, taps):
            acc2 = acc2 + tap(ty_ref, b) * t_ref[:, pl.ds(b, cols_out), :]
        if finish is None:
            dst_ref[pl.ds(r0, chunk)] = acc2
        else:
            finish(pl.ds(r0, chunk), acc2)
        return carry

    lax.fori_loop(0, count // chunk, rows, 0)


def blur_views(field, taps_x, taps_y, fwd_z, views):
    rows_f, cols_f, depth = field.shape
    taps = taps_x.shape[1]
    rows_r = rows_f - (taps - 1)
    cols_r = cols_f - (taps - 1)
    chunk = 4
    deep = DEEP
    f32 = jnp.float32

    def kernel(tx_ref, ty_ref, field_ref, fz_ref, out_ref, q_ref, t1_ref):
        v = pl.program_id(0)
        conv_xy(field_ref, t1_ref, q_ref, tx_ref, ty_ref, v, False, rows_r, chunk, taps, cols_r)

        def depth_rows(c, carry):
            r0 = pl.multiple_of(c * deep, deep)
            flat = q_ref[pl.ds(r0, deep)].reshape(deep * cols_r, depth)
            blurred = jnp.dot(flat, fz_ref[0], precision=MATMUL, preferred_element_type=f32)
            out_ref[0, pl.ds(r0, deep)] = blurred.reshape(deep, cols_r, depth)
            return carry

        lax.fori_loop(0, rows_r // deep, depth_rows, 0)

    smem = pl.BlockSpec(memory_space=pltpu.SMEM)
    return pl.pallas_call(
        kernel,
        grid=(views,),
        in_specs=[
            smem,
            smem,
            pl.BlockSpec(field.shape, lambda v: (0, 0, 0)),
            pl.BlockSpec((1, depth, depth), lambda v: (v, 0, 0)),
        ],
        out_specs=pl.BlockSpec((1, rows_r, cols_r, depth), lambda v: (v, 0, 0, 0)),
        out_shape=jax.ShapeDtypeStruct((views, rows_r, cols_r, depth), f32),
        scratch_shapes=[
            pltpu.VMEM((rows_r, cols_r, depth), f32),
            pltpu.VMEM((chunk, cols_f, depth), f32),
        ],
        compiler_params=pltpu.CompilerParams(dimension_semantics=("arbitrary",)),
    )(taps_x, taps_y, field, fwd_z)


def rl_step(source, registered, estimate, weight, taps_x, taps_y, bg, fwd_z, adj_z, given):
    views, rows_r, cols_r, depth = registered.shape
    rows, cols = estimate.shape[:2]
    taps = taps_x.shape[1]
    cols_f = cols_r + taps - 1
    chunk = 4
    deep = DEEP
    f32 = jnp.float32

    def kernel(tx_ref, ty_ref, bg_ref, src_ref, reg_ref, est_ref, w_ref, fz_ref, az_ref,
               out_ref, q_ref, t1_ref, t2_ref, s_ref):
        v = pl.program_id(0)
        if not given:
            conv_xy(src_ref, t1_ref, q_ref, tx_ref, ty_ref, v, False, rows_r, chunk, taps, cols_r)

        def depth_rows(c, carry):
            r0 = pl.multiple_of(c * deep, deep)
            if given:
                blurred = src_ref[0, pl.ds(r0, deep)].reshape(deep * cols_r, depth)
            else:
                flat = q_ref[pl.ds(r0, deep)].reshape(deep * cols_r, depth)
                blurred = jnp.dot(flat, fz_ref[0], precision=MATMUL, preferred_element_type=f32)
            reg = reg_ref[0, pl.ds(r0, deep)].astype(f32).reshape(deep * cols_r, depth)
            ratio = reg / (blurred + bg_ref[v])
            back = jnp.dot(ratio, az_ref[0], precision=MATMUL, preferred_element_type=f32)
            q_ref[pl.ds(r0, deep)] = back.reshape(deep, cols_r, depth)
            return carry

        lax.fori_loop(0, rows_r // deep, depth_rows, 0)

        def finish(rs, acc2):
            @pl.when(v == 0)
            def _():
                s_ref[rs] = acc2

            @pl.when((v > 0) & (v < views - 1))
            def _():
                s_ref[rs] = s_ref[rs] + acc2

            @pl.when(v == views - 1)
            def _():
                out_ref[rs] = est_ref[rs] * (s_ref[rs] + acc2) / w_ref[rs]

        conv_xy(q_ref, t2_ref, None, tx_ref, ty_ref, v, True, rows, chunk, taps, cols, finish)

    smem = pl.BlockSpec(memory_space=pltpu.SMEM)
    whole3 = lambda shape: pl.BlockSpec(shape, lambda v: (0, 0, 0))
    per_view = pl.BlockSpec((1, rows_r, cols_r, depth), lambda v: (v, 0, 0, 0))
    return pl.pallas_call(
        kernel,
        grid=(views,),
        in_specs=[
            smem,
            smem,
            smem,
            per_view if given else whole3(source.shape),
            per_view,
            whole3(estimate.shape),
            whole3(weight.shape),
            pl.BlockSpec((1, depth, depth), lambda v: (v, 0, 0)),
            pl.BlockSpec((1, depth, depth), lambda v: (v, 0, 0)),
        ],
        out_specs=whole3(estimate.shape),
        out_shape=jax.ShapeDtypeStruct(estimate.shape, f32),
        scratch_shapes=[
            pltpu.VMEM((rows_r, cols_r, depth), f32),
            pltpu.VMEM((chunk, cols_f, depth), f32),
            pltpu.VMEM((chunk, cols_r, depth), f32),
            pltpu.VMEM((rows, cols, depth), f32),
        ],
        compiler_params=pltpu.CompilerParams(dimension_semantics=("arbitrary",)),
    )(taps_x, taps_y, bg, source, registered, estimate, weight, fwd_z, adj_z)


def local(views, offsets, background, psf_x, psf_y, psf_z, start):
    rows_x, rows_y, depth = start.shape
    nx = lax.axis_size("bx")
    ny = lax.axis_size("by")
    full_x = rows_x * nx
    full_y = rows_y * ny
    middle = (psf_x.shape[1] - 1) // 2
    h = middle
    ix = lax.axis_index("bx")
    iy = lax.axis_index("by")

    padded_start = halo_2d(start, 2 * h)

    taps_x = psf_x / jnp.sum(psf_x, axis=1, keepdims=True)
    taps_y = psf_y / jnp.sum(psf_y, axis=1, keepdims=True)
    taps_z = psf_z / jnp.sum(psf_z, axis=1, keepdims=True)
    fwd_x = band_rows(taps_x, rows_x + 2 * h)
    fwd_y = band_rows(taps_y, rows_y + 2 * h)
    fwd_z = depth_band(taps_z, depth)
    adj_x = band_rows(taps_x[:, ::-1], rows_x)
    adj_y = band_rows(taps_y[:, ::-1], rows_y)
    adj_z = jnp.swapaxes(fwd_z, 1, 2)

    pad_y = SHIFT + h
    vpad = jnp.pad(views, ((0, 0), (0, 0), (pad_y, pad_y), (0, 0)))
    cols = full_y + 2 * h
    shifted = jnp.stack(
        [
            lax.dynamic_slice_in_dim(vpad[w], SHIFT + offsets[w, 1], cols, axis=1)
            for w in range(V)
        ]
    )
    chunks = jnp.concatenate(
        [shifted[:, :, k * rows_y : k * rows_y + rows_y + 2 * h] for k in range(ny)], axis=2
    )
    routed = lax.all_to_all(chunks, "by", split_axis=2, concat_axis=1, tiled=True)
    blurred = blur_views(padded_start, taps_x, taps_y, fwd_z, V)
    blurred, routed = lax.optimization_barrier((blurred, routed))

    reach = SHIFT + h
    prev_rows = (reach, h, reach, 0)
    next_rows = (0, reach, h, reach)
    prev_send = jnp.concatenate(
        [routed[w, rows_x - prev_rows[w] :] for w in range(V) if prev_rows[w]], axis=0
    )
    next_send = jnp.concatenate(
        [routed[w, : next_rows[w]] for w in range(V) if next_rows[w]], axis=0
    )
    prev_got = lax.ppermute(prev_send, "bx", shift_pairs(nx, 1))
    next_got = lax.ppermute(next_send, "bx", shift_pairs(nx, -1))

    base_x = ix * rows_x - h + jnp.arange(rows_x + 2 * h, dtype=jnp.int32)
    base_y = iy * rows_y - h + jnp.arange(rows_y + 2 * h, dtype=jnp.int32)
    inside_x = (base_x >= 0) & (base_x < full_x)
    inside_y = (base_y >= 0) & (base_y < full_y)
    inside = inside_x[:, None] & inside_y[None, :]

    registered = []
    at_prev = 0
    at_next = 0
    for w in range(V):
        parts = []
        if prev_rows[w]:
            parts.append(prev_got[at_prev : at_prev + prev_rows[w]])
            at_prev += prev_rows[w]
        parts.append(routed[w])
        if next_rows[w]:
            parts.append(next_got[at_next : at_next + next_rows[w]])
            at_next += next_rows[w]
        ext = jnp.concatenate(parts, axis=0)
        moved = lax.dynamic_slice_in_dim(
            ext, prev_rows[w] - h + offsets[w, 0], rows_x + 2 * h, axis=0
        )
        registered.append(jnp.where(inside[:, :, None], moved, jnp.zeros((), moved.dtype)))
    registered = jnp.stack(registered)

    cover_x = (
        (base_x[None, :] + offsets[:, 0:1] >= 0) & (base_x[None, :] + offsets[:, 0:1] < full_x)
    ) & inside_x[None, :]
    cover_y = (
        (base_y[None, :] + offsets[:, 1:2] >= 0) & (base_y[None, :] + offsets[:, 1:2] < full_y)
    ) & inside_y[None, :]
    weight_x = jnp.einsum("vij,vj->vi", adj_x, cover_x.astype(jnp.float32), precision=HIGHEST)
    weight_y = jnp.einsum("vij,vj->vi", adj_y, cover_y.astype(jnp.float32), precision=HIGHEST)
    weight_z = jnp.sum(adj_z, axis=1)
    weight = jnp.einsum("vx,vy,vz->xyz", weight_x, weight_y, weight_z, precision=HIGHEST)

    estimate = start
    for sweep in range(ITERS):
        if sweep == 0:
            source = blurred
        else:
            source = halo_2d(estimate, 2 * h)
        estimate = rl_step(source, registered, estimate, weight, taps_x, taps_y, background,
                           fwd_z, adj_z, sweep == 0)
    return estimate


def solution(mesh):
    return jax.shard_map(
        local,
        mesh=mesh,
        in_specs=(P(None, ("bx", "by"), None, None), P(), P(), P(), P(), P(), P("bx", "by", None)),
        out_specs=P("bx", "by", None),
        check_vma=False,
    )
```

```python
import jax
import jax.numpy as jnp
from jax import lax
from jax.sharding import PartitionSpec as P
from jax.experimental import pallas as pl
from jax.experimental.pallas import tpu as pltpu

V = 4
SHIFT = 16
ITERS = 2
HIGHEST = lax.Precision.HIGHEST
MATMUL = lax.Precision.HIGH
DEEP = 36


def shift_pairs(count, step):
    if step > 0:
        return [(i, i + step) for i in range(count - step)]
    return [(i - step, i) for i in range(count + step)]


def halo_2d(block, width):
    nx = lax.axis_size("bx")
    ny = lax.axis_size("by")
    low = block.astype(jnp.bfloat16)
    w = width
    up = lax.ppermute(low[-w:], "bx", shift_pairs(nx, 1))
    down = lax.ppermute(low[:w], "bx", shift_pairs(nx, -1))
    left = lax.ppermute(low[:, -w:], "by", shift_pairs(ny, 1))
    right = lax.ppermute(low[:, :w], "by", shift_pairs(ny, -1))

    def corner(part, dx, dy):
        pairs = []
        for i in range(nx):
            for j in range(ny):
                ti, tj = i + dx, j + dy
                if 0 <= ti < nx and 0 <= tj < ny:
                    pairs.append((i * ny + j, ti * ny + tj))
        return lax.ppermute(part, ("bx", "by"), pairs)

    up_left = corner(low[-w:, -w:], 1, 1)
    up_right = corner(low[-w:, :w], 1, -1)
    down_left = corner(low[:w, -w:], -1, 1)
    down_right = corner(low[:w, :w], -1, -1)
    f = block.dtype
    top = jnp.concatenate([up_left, up, up_right], axis=1).astype(f)
    mid = jnp.concatenate([left.astype(f), block, right.astype(f)], axis=1)
    bottom = jnp.concatenate([down_left, down, down_right], axis=1).astype(f)
    return jnp.concatenate([top, mid, bottom], axis=0)


def band_rows(taps, extent):
    length = taps.shape[1]
    distance = jnp.arange(extent + length - 1)[None, :] - jnp.arange(extent)[:, None]
    picked = distance[:, :, None] == jnp.arange(length)[None, None, :]
    return jnp.sum(jnp.where(picked[None], taps[:, None, None, :], 0.0), axis=3)


def depth_band(taps, extent):
    length = taps.shape[1]
    middle = (length - 1) // 2
    distance = jnp.arange(extent)[:, None] - jnp.arange(extent)[None, :] + middle
    picked = distance[:, :, None] == jnp.arange(length)[None, None, :]
    return jnp.sum(jnp.where(picked[None], taps[:, None, None, :], 0.0), axis=3)


def conv_xy(src_ref, t_ref, dst_ref, tx_ref, ty_ref, v, flip, count, chunk, taps, cols_out,
            finish=None):
    def tap(ref, k):
        return ref[v, taps - 1 - k] if flip else ref[v, k]

    def rows(c, carry):
        r0 = pl.multiple_of(c * chunk, chunk)
        acc = tap(tx_ref, 0) * src_ref[pl.ds(r0, chunk)]
        for a in range(1, taps):
            acc = acc + tap(tx_ref, a) * src_ref[pl.ds(r0 + a, chunk)]
        t_ref[...] = acc
        acc2 = tap(ty_ref, 0) * t_ref[:, pl.ds(0, cols_out), :]
        for b in range(1, taps):
            acc2 = acc2 + tap(ty_ref, b) * t_ref[:, pl.ds(b, cols_out), :]
        if finish is None:
            dst_ref[pl.ds(r0, chunk)] = acc2
        else:
            finish(pl.ds(r0, chunk), acc2)
        return carry

    lax.fori_loop(0, count // chunk, rows, 0)


def blur_views(field, taps_x, taps_y, fwd_z, views):
    rows_f, cols_f, depth = field.shape
    taps = taps_x.shape[1]
    rows_r = rows_f - (taps - 1)
    cols_r = cols_f - (taps - 1)
    chunk = 4
    deep = DEEP
    f32 = jnp.float32

    def kernel(tx_ref, ty_ref, field_ref, fz_ref, out_ref, q_ref, t1_ref):
        v = pl.program_id(0)
        conv_xy(field_ref, t1_ref, q_ref, tx_ref, ty_ref, v, False, rows_r, chunk, taps, cols_r)

        def depth_rows(c, carry):
            r0 = pl.multiple_of(c * deep, deep)
            flat = q_ref[pl.ds(r0, deep)].reshape(deep * cols_r, depth)
            blurred = jnp.dot(flat, fz_ref[0], precision=MATMUL, preferred_element_type=f32)
            out_ref[0, pl.ds(r0, deep)] = blurred.reshape(deep, cols_r, depth)
            return carry

        lax.fori_loop(0, rows_r // deep, depth_rows, 0)

    smem = pl.BlockSpec(memory_space=pltpu.SMEM)
    return pl.pallas_call(
        kernel,
        grid=(views,),
        in_specs=[
            smem,
            smem,
            pl.BlockSpec(field.shape, lambda v: (0, 0, 0)),
            pl.BlockSpec((1, depth, depth), lambda v: (v, 0, 0)),
        ],
        out_specs=pl.BlockSpec((1, rows_r, cols_r, depth), lambda v: (v, 0, 0, 0)),
        out_shape=jax.ShapeDtypeStruct((views, rows_r, cols_r, depth), f32),
        scratch_shapes=[
            pltpu.VMEM((rows_r, cols_r, depth), f32),
            pltpu.VMEM((chunk, cols_f, depth), f32),
        ],
        compiler_params=pltpu.CompilerParams(dimension_semantics=("arbitrary",)),
    )(taps_x, taps_y, field, fwd_z)


def rl_step(source, registered, estimate, weight, taps_x, taps_y, bg, fwd_z, adj_z, given):
    views, rows_r, cols_r, depth = registered.shape
    rows, cols = estimate.shape[:2]
    taps = taps_x.shape[1]
    cols_f = cols_r + taps - 1
    chunk = 4
    deep = DEEP
    f32 = jnp.float32

    def kernel(tx_ref, ty_ref, bg_ref, src_ref, reg_ref, est_ref, w_ref, fz_ref, az_ref,
               out_ref, q_ref, t1_ref, t2_ref, s_ref):
        v = pl.program_id(0)
        if not given:
            conv_xy(src_ref, t1_ref, q_ref, tx_ref, ty_ref, v, False, rows_r, chunk, taps, cols_r)

        def depth_rows(c, carry):
            r0 = pl.multiple_of(c * deep, deep)
            if given:
                blurred = src_ref[0, pl.ds(r0, deep)].reshape(deep * cols_r, depth)
            else:
                flat = q_ref[pl.ds(r0, deep)].reshape(deep * cols_r, depth)
                blurred = jnp.dot(flat, fz_ref[0], precision=MATMUL, preferred_element_type=f32)
            reg = reg_ref[0, pl.ds(r0, deep)].astype(f32).reshape(deep * cols_r, depth)
            ratio = reg / (blurred + bg_ref[v])
            back = jnp.dot(ratio, az_ref[0], precision=MATMUL, preferred_element_type=f32)
            q_ref[pl.ds(r0, deep)] = back.reshape(deep, cols_r, depth)
            return carry

        lax.fori_loop(0, rows_r // deep, depth_rows, 0)

        def finish(rs, acc2):
            @pl.when(v == 0)
            def _():
                s_ref[rs] = acc2

            @pl.when((v > 0) & (v < views - 1))
            def _():
                s_ref[rs] = s_ref[rs] + acc2

            @pl.when(v == views - 1)
            def _():
                out_ref[rs] = est_ref[rs] * (s_ref[rs] + acc2) / w_ref[rs]

        conv_xy(q_ref, t2_ref, None, tx_ref, ty_ref, v, True, rows, chunk, taps, cols, finish)

    smem = pl.BlockSpec(memory_space=pltpu.SMEM)
    whole3 = lambda shape: pl.BlockSpec(shape, lambda v: (0, 0, 0))
    per_view = pl.BlockSpec((1, rows_r, cols_r, depth), lambda v: (v, 0, 0, 0))
    return pl.pallas_call(
        kernel,
        grid=(views,),
        in_specs=[
            smem,
            smem,
            smem,
            per_view if given else whole3(source.shape),
            per_view,
            whole3(estimate.shape),
            whole3(weight.shape),
            pl.BlockSpec((1, depth, depth), lambda v: (v, 0, 0)),
            pl.BlockSpec((1, depth, depth), lambda v: (v, 0, 0)),
        ],
        out_specs=whole3(estimate.shape),
        out_shape=jax.ShapeDtypeStruct(estimate.shape, f32),
        scratch_shapes=[
            pltpu.VMEM((rows_r, cols_r, depth), f32),
            pltpu.VMEM((chunk, cols_f, depth), f32),
            pltpu.VMEM((chunk, cols_r, depth), f32),
            pltpu.VMEM((rows, cols, depth), f32),
        ],
        compiler_params=pltpu.CompilerParams(dimension_semantics=("arbitrary",)),
    )(taps_x, taps_y, bg, source, registered, estimate, weight, fwd_z, adj_z)


def local(views, offsets, background, psf_x, psf_y, psf_z, start):
    rows_x, rows_y, depth = start.shape
    nx = lax.axis_size("bx")
    ny = lax.axis_size("by")
    full_x = rows_x * nx
    full_y = rows_y * ny
    middle = (psf_x.shape[1] - 1) // 2
    h = middle
    ix = lax.axis_index("bx")
    iy = lax.axis_index("by")

    padded_start = halo_2d(start, 2 * h)

    taps_x = psf_x / jnp.sum(psf_x, axis=1, keepdims=True)
    taps_y = psf_y / jnp.sum(psf_y, axis=1, keepdims=True)
    taps_z = psf_z / jnp.sum(psf_z, axis=1, keepdims=True)
    fwd_x = band_rows(taps_x, rows_x + 2 * h)
    fwd_y = band_rows(taps_y, rows_y + 2 * h)
    fwd_z = depth_band(taps_z, depth)
    adj_x = band_rows(taps_x[:, ::-1], rows_x)
    adj_y = band_rows(taps_y[:, ::-1], rows_y)
    adj_z = jnp.swapaxes(fwd_z, 1, 2)

    pad_y = SHIFT + h
    vpad = jnp.pad(views, ((0, 0), (0, 0), (pad_y, pad_y), (0, 0)))
    cols = full_y + 2 * h
    shifted = jnp.stack(
        [
            lax.dynamic_slice_in_dim(vpad[w], SHIFT + offsets[w, 1], cols, axis=1)
            for w in range(V)
        ]
    )
    chunks = jnp.concatenate(
        [shifted[:, :, k * rows_y : k * rows_y + rows_y + 2 * h] for k in range(ny)], axis=2
    )
    padded_start, chunks = lax.optimization_barrier((padded_start, chunks))
    routed = lax.all_to_all(chunks, "by", split_axis=2, concat_axis=1, tiled=True)
    blurred = blur_views(padded_start, taps_x, taps_y, fwd_z, V)
    blurred, routed = lax.optimization_barrier((blurred, routed))

    reach = SHIFT + h
    prev_rows = (reach, h, reach, 0)
    next_rows = (0, reach, h, reach)
    prev_send = jnp.concatenate(
        [routed[w, rows_x - prev_rows[w] :] for w in range(V) if prev_rows[w]], axis=0
    )
    next_send = jnp.concatenate(
        [routed[w, : next_rows[w]] for w in range(V) if next_rows[w]], axis=0
    )
    prev_got = lax.ppermute(prev_send, "bx", shift_pairs(nx, 1))
    next_got = lax.ppermute(next_send, "bx", shift_pairs(nx, -1))

    base_x = ix * rows_x - h + jnp.arange(rows_x + 2 * h, dtype=jnp.int32)
    base_y = iy * rows_y - h + jnp.arange(rows_y + 2 * h, dtype=jnp.int32)
    inside_x = (base_x >= 0) & (base_x < full_x)
    inside_y = (base_y >= 0) & (base_y < full_y)
    inside = inside_x[:, None] & inside_y[None, :]

    registered = []
    at_prev = 0
    at_next = 0
    for w in range(V):
        parts = []
        if prev_rows[w]:
            parts.append(prev_got[at_prev : at_prev + prev_rows[w]])
            at_prev += prev_rows[w]
        parts.append(routed[w])
        if next_rows[w]:
            parts.append(next_got[at_next : at_next + next_rows[w]])
            at_next += next_rows[w]
        ext = jnp.concatenate(parts, axis=0)
        moved = lax.dynamic_slice_in_dim(
            ext, prev_rows[w] - h + offsets[w, 0], rows_x + 2 * h, axis=0
        )
        registered.append(jnp.where(inside[:, :, None], moved, jnp.zeros((), moved.dtype)))
    registered = jnp.stack(registered)

    cover_x = (
        (base_x[None, :] + offsets[:, 0:1] >= 0) & (base_x[None, :] + offsets[:, 0:1] < full_x)
    ) & inside_x[None, :]
    cover_y = (
        (base_y[None, :] + offsets[:, 1:2] >= 0) & (base_y[None, :] + offsets[:, 1:2] < full_y)
    ) & inside_y[None, :]
    weight_x = jnp.einsum("vij,vj->vi", adj_x, cover_x.astype(jnp.float32), precision=HIGHEST)
    weight_y = jnp.einsum("vij,vj->vi", adj_y, cover_y.astype(jnp.float32), precision=HIGHEST)
    weight_z = jnp.sum(adj_z, axis=1)
    weight = jnp.einsum("vx,vy,vz->xyz", weight_x, weight_y, weight_z, precision=HIGHEST)

    estimate = start
    for sweep in range(ITERS):
        if sweep == 0:
            source = blurred
        else:
            source = halo_2d(estimate, 2 * h)
        estimate = rl_step(source, registered, estimate, weight, taps_x, taps_y, background,
                           fwd_z, adj_z, sweep == 0)
    return estimate


def solution(mesh):
    return jax.shard_map(
        local,
        mesh=mesh,
        in_specs=(P(None, ("bx", "by"), None, None), P(), P(), P(), P(), P(), P("bx", "by", None)),
        out_specs=P("bx", "by", None),
        check_vma=False,
    )
```

```python
import jax
import jax.numpy as jnp
from jax import lax
from jax.sharding import PartitionSpec as P
from jax.experimental import pallas as pl
from jax.experimental.pallas import tpu as pltpu

V = 4
SHIFT = 16
ITERS = 2
HIGHEST = lax.Precision.HIGHEST
MATMUL = lax.Precision.HIGH
DEEP = 36


def shift_pairs(count, step):
    if step > 0:
        return [(i, i + step) for i in range(count - step)]
    return [(i - step, i) for i in range(count + step)]


def halo_2d(block, width):
    nx = lax.axis_size("bx")
    ny = lax.axis_size("by")
    low = block.astype(jnp.bfloat16)
    w = width
    up = lax.ppermute(low[-w:], "bx", shift_pairs(nx, 1))
    down = lax.ppermute(low[:w], "bx", shift_pairs(nx, -1))
    left = lax.ppermute(low[:, -w:], "by", shift_pairs(ny, 1))
    right = lax.ppermute(low[:, :w], "by", shift_pairs(ny, -1))

    def corner(part, dx, dy):
        pairs = []
        for i in range(nx):
            for j in range(ny):
                ti, tj = i + dx, j + dy
                if 0 <= ti < nx and 0 <= tj < ny:
                    pairs.append((i * ny + j, ti * ny + tj))
        return lax.ppermute(part, ("bx", "by"), pairs)

    up_left = corner(low[-w:, -w:], 1, 1)
    up_right = corner(low[-w:, :w], 1, -1)
    down_left = corner(low[:w, -w:], -1, 1)
    down_right = corner(low[:w, :w], -1, -1)
    f = block.dtype
    top = jnp.concatenate([up_left, up, up_right], axis=1).astype(f)
    mid = jnp.concatenate([left.astype(f), block, right.astype(f)], axis=1)
    bottom = jnp.concatenate([down_left, down, down_right], axis=1).astype(f)
    return jnp.concatenate([top, mid, bottom], axis=0)


def halo_rows_cols(block, width):
    nx = lax.axis_size("bx")
    ny = lax.axis_size("by")
    w = width
    f = block.dtype
    low = block.astype(jnp.bfloat16)
    up = lax.ppermute(low[-w:], "bx", shift_pairs(nx, 1))
    down = lax.ppermute(low[:w], "bx", shift_pairs(nx, -1))
    tall = jnp.concatenate([up, low, down], axis=0)
    left = lax.ppermute(tall[:, -w:], "by", shift_pairs(ny, 1))
    right = lax.ppermute(tall[:, :w], "by", shift_pairs(ny, -1))
    middle = jnp.concatenate([up.astype(f), block, down.astype(f)], axis=0)
    return jnp.concatenate([left.astype(f), middle, right.astype(f)], axis=1)


def band_rows(taps, extent):
    length = taps.shape[1]
    distance = jnp.arange(extent + length - 1)[None, :] - jnp.arange(extent)[:, None]
    picked = distance[:, :, None] == jnp.arange(length)[None, None, :]
    return jnp.sum(jnp.where(picked[None], taps[:, None, None, :], 0.0), axis=3)


def depth_band(taps, extent):
    length = taps.shape[1]
    middle = (length - 1) // 2
    distance = jnp.arange(extent)[:, None] - jnp.arange(extent)[None, :] + middle
    picked = distance[:, :, None] == jnp.arange(length)[None, None, :]
    return jnp.sum(jnp.where(picked[None], taps[:, None, None, :], 0.0), axis=3)


def rl_step(field, registered, estimate, weight, taps_x, taps_y, bg, fwd_z, adj_z):
    views, rows_r, cols_r, depth = registered.shape
    rows, cols = estimate.shape[:2]
    rows_f, cols_f = field.shape[:2]
    taps = taps_x.shape[1]
    chunk = 4
    deep = DEEP
    f32 = jnp.float32

    def kernel(tx_ref, ty_ref, bg_ref, field_ref, reg_ref, est_ref, w_ref, fz_ref, az_ref,
               out_ref, q_ref, t1_ref, t2_ref, s_ref):
        v = pl.program_id(0)

        def forward_rows(c, carry):
            r0 = pl.multiple_of(c * chunk, chunk)
            acc = tx_ref[v, 0] * field_ref[pl.ds(r0, chunk)]
            for a in range(1, taps):
                acc = acc + tx_ref[v, a] * field_ref[pl.ds(r0 + a, chunk)]
            t1_ref[...] = acc
            acc2 = ty_ref[v, 0] * t1_ref[:, pl.ds(0, cols_r), :]
            for b in range(1, taps):
                acc2 = acc2 + ty_ref[v, b] * t1_ref[:, pl.ds(b, cols_r), :]
            q_ref[pl.ds(r0, chunk)] = acc2
            return carry

        lax.fori_loop(0, rows_r // chunk, forward_rows, 0)

        def depth_rows(c, carry):
            r0 = pl.multiple_of(c * deep, deep)
            flat = q_ref[pl.ds(r0, deep)].reshape(deep * cols_r, depth)
            blurred = jnp.dot(flat, fz_ref[0], precision=MATMUL, preferred_element_type=f32)
            reg = reg_ref[0, pl.ds(r0, deep)].astype(f32).reshape(deep * cols_r, depth)
            ratio = reg / (blurred + bg_ref[v])
            back = jnp.dot(ratio, az_ref[0], precision=MATMUL, preferred_element_type=f32)
            q_ref[pl.ds(r0, deep)] = back.reshape(deep, cols_r, depth)
            return carry

        lax.fori_loop(0, rows_r // deep, depth_rows, 0)

        def adjoint_rows(c, carry):
            r0 = pl.multiple_of(c * chunk, chunk)
            acc = tx_ref[v, taps - 1] * q_ref[pl.ds(r0, chunk)]
            for a in range(1, taps):
                acc = acc + tx_ref[v, taps - 1 - a] * q_ref[pl.ds(r0 + a, chunk)]
            t2_ref[...] = acc
            acc2 = ty_ref[v, taps - 1] * t2_ref[:, pl.ds(0, cols), :]
            for b in range(1, taps):
                acc2 = acc2 + ty_ref[v, taps - 1 - b] * t2_ref[:, pl.ds(b, cols), :]
            rs = pl.ds(r0, chunk)

            @pl.when(v == 0)
            def _():
                s_ref[rs] = acc2

            @pl.when((v > 0) & (v < views - 1))
            def _():
                s_ref[rs] = s_ref[rs] + acc2

            @pl.when(v == views - 1)
            def _():
                out_ref[rs] = est_ref[rs] * (s_ref[rs] + acc2) / w_ref[rs]

            return carry

        lax.fori_loop(0, rows // chunk, adjoint_rows, 0)

    smem = pl.BlockSpec(memory_space=pltpu.SMEM)
    whole3 = lambda shape: pl.BlockSpec(shape, lambda v: (0, 0, 0))
    return pl.pallas_call(
        kernel,
        grid=(views,),
        in_specs=[
            smem,
            smem,
            smem,
            whole3(field.shape),
            pl.BlockSpec((1, rows_r, cols_r, depth), lambda v: (v, 0, 0, 0)),
            whole3(estimate.shape),
            whole3(weight.shape),
            pl.BlockSpec((1, depth, depth), lambda v: (v, 0, 0)),
            pl.BlockSpec((1, depth, depth), lambda v: (v, 0, 0)),
        ],
        out_specs=whole3(estimate.shape),
        out_shape=jax.ShapeDtypeStruct(estimate.shape, f32),
        scratch_shapes=[
            pltpu.VMEM((rows_r, cols_r, depth), f32),
            pltpu.VMEM((chunk, cols_f, depth), f32),
            pltpu.VMEM((chunk, cols_r, depth), f32),
            pltpu.VMEM((rows, cols, depth), f32),
        ],
        compiler_params=pltpu.CompilerParams(dimension_semantics=("arbitrary",)),
    )(taps_x, taps_y, bg, field, registered, estimate, weight, fwd_z, adj_z)


def local(views, offsets, background, psf_x, psf_y, psf_z, start):
    rows_x, rows_y, depth = start.shape
    nx = lax.axis_size("bx")
    ny = lax.axis_size("by")
    full_x = rows_x * nx
    full_y = rows_y * ny
    middle = (psf_x.shape[1] - 1) // 2
    h = middle
    ix = lax.axis_index("bx")
    iy = lax.axis_index("by")

    padded_start = halo_2d(start, 2 * h)

    pad_y = SHIFT + h
    vpad = jnp.pad(views, ((0, 0), (0, 0), (pad_y, pad_y), (0, 0)))
    cols = full_y + 2 * h
    shifted = jnp.stack(
        [
            lax.dynamic_slice_in_dim(vpad[w], SHIFT + offsets[w, 1], cols, axis=1)
            for w in range(V)
        ]
    )
    chunks = jnp.concatenate(
        [shifted[:, :, k * rows_y : k * rows_y + rows_y + 2 * h] for k in range(ny)], axis=2
    )
    routed = lax.all_to_all(chunks, "by", split_axis=2, concat_axis=1, tiled=True)

    reach = SHIFT + h
    prev_rows = (reach, h, reach, 0)
    next_rows = (0, reach, h, reach)
    prev_send = jnp.concatenate(
        [routed[w, rows_x - prev_rows[w] :] for w in range(V) if prev_rows[w]], axis=0
    )
    next_send = jnp.concatenate(
        [routed[w, : next_rows[w]] for w in range(V) if next_rows[w]], axis=0
    )
    prev_got = lax.ppermute(prev_send, "bx", shift_pairs(nx, 1))
    next_got = lax.ppermute(next_send, "bx", shift_pairs(nx, -1))

    base_x = ix * rows_x - h + jnp.arange(rows_x + 2 * h, dtype=jnp.int32)
    base_y = iy * rows_y - h + jnp.arange(rows_y + 2 * h, dtype=jnp.int32)
    inside_x = (base_x >= 0) & (base_x < full_x)
    inside_y = (base_y >= 0) & (base_y < full_y)
    inside = inside_x[:, None] & inside_y[None, :]

    registered = []
    at_prev = 0
    at_next = 0
    for w in range(V):
        parts = []
        if prev_rows[w]:
            parts.append(prev_got[at_prev : at_prev + prev_rows[w]])
            at_prev += prev_rows[w]
        parts.append(routed[w])
        if next_rows[w]:
            parts.append(next_got[at_next : at_next + next_rows[w]])
            at_next += next_rows[w]
        ext = jnp.concatenate(parts, axis=0)
        moved = lax.dynamic_slice_in_dim(
            ext, prev_rows[w] - h + offsets[w, 0], rows_x + 2 * h, axis=0
        )
        registered.append(jnp.where(inside[:, :, None], moved, jnp.zeros((), moved.dtype)))
    registered = jnp.stack(registered)

    taps_x = psf_x / jnp.sum(psf_x, axis=1, keepdims=True)
    taps_y = psf_y / jnp.sum(psf_y, axis=1, keepdims=True)
    taps_z = psf_z / jnp.sum(psf_z, axis=1, keepdims=True)
    fwd_x = band_rows(taps_x, rows_x + 2 * h)
    fwd_y = band_rows(taps_y, rows_y + 2 * h)
    fwd_z = depth_band(taps_z, depth)
    adj_x = band_rows(taps_x[:, ::-1], rows_x)
    adj_y = band_rows(taps_y[:, ::-1], rows_y)
    adj_z = jnp.swapaxes(fwd_z, 1, 2)

    cover_x = (
        (base_x[None, :] + offsets[:, 0:1] >= 0) & (base_x[None, :] + offsets[:, 0:1] < full_x)
    ) & inside_x[None, :]
    cover_y = (
        (base_y[None, :] + offsets[:, 1:2] >= 0) & (base_y[None, :] + offsets[:, 1:2] < full_y)
    ) & inside_y[None, :]
    weight_x = jnp.einsum("vij,vj->vi", adj_x, cover_x.astype(jnp.float32), precision=HIGHEST)
    weight_y = jnp.einsum("vij,vj->vi", adj_y, cover_y.astype(jnp.float32), precision=HIGHEST)
    weight_z = jnp.sum(adj_z, axis=1)
    weight = jnp.sum(
        weight_x[:, :, None, None] * weight_y[:, None, :, None] * weight_z[:, None, None, :], axis=0
    )

    estimate = start
    for sweep in range(ITERS):
        field = padded_start if sweep == 0 else halo_rows_cols(estimate, 2 * h)
        estimate = rl_step(field, registered, estimate, weight, taps_x, taps_y, background,
                           fwd_z, adj_z)
    return estimate


def solution(mesh):
    return jax.shard_map(
        local,
        mesh=mesh,
        in_specs=(P(None, ("bx", "by"), None, None), P(), P(), P(), P(), P(), P("bx", "by", None)),
        out_specs=P("bx", "by", None),
        check_vma=False,
    )
```

```python
import jax
import jax.numpy as jnp
from jax import lax
from jax.sharding import PartitionSpec as P
from jax.experimental import pallas as pl
from jax.experimental.pallas import tpu as pltpu

V = 4
SHIFT = 16
ITERS = 2
HIGHEST = lax.Precision.HIGHEST
MATMUL = lax.Precision.HIGH
DEEP = 36


def shift_pairs(count, step):
    if step > 0:
        return [(i, i + step) for i in range(count - step)]
    return [(i - step, i) for i in range(count + step)]


def halo_2d(block, width):
    nx = lax.axis_size("bx")
    ny = lax.axis_size("by")
    low = block.astype(jnp.bfloat16)
    w = width
    up = lax.ppermute(low[-w:], "bx", shift_pairs(nx, 1))
    down = lax.ppermute(low[:w], "bx", shift_pairs(nx, -1))
    left = lax.ppermute(low[:, -w:], "by", shift_pairs(ny, 1))
    right = lax.ppermute(low[:, :w], "by", shift_pairs(ny, -1))

    def corner(part, dx, dy):
        pairs = []
        for i in range(nx):
            for j in range(ny):
                ti, tj = i + dx, j + dy
                if 0 <= ti < nx and 0 <= tj < ny:
                    pairs.append((i * ny + j, ti * ny + tj))
        return lax.ppermute(part, ("bx", "by"), pairs)

    up_left = corner(low[-w:, -w:], 1, 1)
    up_right = corner(low[-w:, :w], 1, -1)
    down_left = corner(low[:w, -w:], -1, 1)
    down_right = corner(low[:w, :w], -1, -1)
    f = block.dtype
    top = jnp.concatenate([up_left, up, up_right], axis=1).astype(f)
    mid = jnp.concatenate([left.astype(f), block, right.astype(f)], axis=1)
    bottom = jnp.concatenate([down_left, down, down_right], axis=1).astype(f)
    return jnp.concatenate([top, mid, bottom], axis=0)


def halo_rows_cols(block, width):
    nx = lax.axis_size("bx")
    ny = lax.axis_size("by")
    w = width
    f = block.dtype
    low = block.astype(jnp.bfloat16)
    up = lax.ppermute(low[-w:], "bx", shift_pairs(nx, 1))
    down = lax.ppermute(low[:w], "bx", shift_pairs(nx, -1))
    tall = jnp.concatenate([up, low, down], axis=0)
    left = lax.ppermute(tall[:, -w:], "by", shift_pairs(ny, 1))
    right = lax.ppermute(tall[:, :w], "by", shift_pairs(ny, -1))
    middle = jnp.concatenate([up.astype(f), block, down.astype(f)], axis=0)
    return jnp.concatenate([left.astype(f), middle, right.astype(f)], axis=1)


def band_rows(taps, extent):
    length = taps.shape[1]
    distance = jnp.arange(extent + length - 1)[None, :] - jnp.arange(extent)[:, None]
    picked = distance[:, :, None] == jnp.arange(length)[None, None, :]
    return jnp.sum(jnp.where(picked[None], taps[:, None, None, :], 0.0), axis=3)


def depth_band(taps, extent):
    length = taps.shape[1]
    middle = (length - 1) // 2
    distance = jnp.arange(extent)[:, None] - jnp.arange(extent)[None, :] + middle
    picked = distance[:, :, None] == jnp.arange(length)[None, None, :]
    return jnp.sum(jnp.where(picked[None], taps[:, None, None, :], 0.0), axis=3)


def conv_xy(src_ref, t_ref, dst_ref, tx_ref, ty_ref, v, flip, count, chunk, taps, cols_out,
            finish=None):
    def tap(ref, k):
        return ref[v, taps - 1 - k] if flip else ref[v, k]

    def rows(c, carry):
        r0 = pl.multiple_of(c * chunk, chunk)
        acc = tap(tx_ref, 0) * src_ref[pl.ds(r0, chunk)]
        for a in range(1, taps):
            acc = acc + tap(tx_ref, a) * src_ref[pl.ds(r0 + a, chunk)]
        t_ref[...] = acc
        acc2 = tap(ty_ref, 0) * t_ref[:, pl.ds(0, cols_out), :]
        for b in range(1, taps):
            acc2 = acc2 + tap(ty_ref, b) * t_ref[:, pl.ds(b, cols_out), :]
        if finish is None:
            dst_ref[pl.ds(r0, chunk)] = acc2
        else:
            finish(pl.ds(r0, chunk), acc2)
        return carry

    lax.fori_loop(0, count // chunk, rows, 0)


def blur_views(field, taps_x, taps_y, fwd_z, views):
    rows_f, cols_f, depth = field.shape
    taps = taps_x.shape[1]
    rows_r = rows_f - (taps - 1)
    cols_r = cols_f - (taps - 1)
    chunk = 4
    deep = DEEP
    f32 = jnp.float32

    def kernel(tx_ref, ty_ref, field_ref, fz_ref, out_ref, q_ref, t1_ref):
        v = pl.program_id(0)
        conv_xy(field_ref, t1_ref, q_ref, tx_ref, ty_ref, v, False, rows_r, chunk, taps, cols_r)

        def depth_rows(c, carry):
            r0 = pl.multiple_of(c * deep, deep)
            flat = q_ref[pl.ds(r0, deep)].reshape(deep * cols_r, depth)
            blurred = jnp.dot(flat, fz_ref[0], precision=MATMUL, preferred_element_type=f32)
            out_ref[0, pl.ds(r0, deep)] = blurred.reshape(deep, cols_r, depth)
            return carry

        lax.fori_loop(0, rows_r // deep, depth_rows, 0)

    smem = pl.BlockSpec(memory_space=pltpu.SMEM)
    return pl.pallas_call(
        kernel,
        grid=(views,),
        in_specs=[
            smem,
            smem,
            pl.BlockSpec(field.shape, lambda v: (0, 0, 0)),
            pl.BlockSpec((1, depth, depth), lambda v: (v, 0, 0)),
        ],
        out_specs=pl.BlockSpec((1, rows_r, cols_r, depth), lambda v: (v, 0, 0, 0)),
        out_shape=jax.ShapeDtypeStruct((views, rows_r, cols_r, depth), f32),
        scratch_shapes=[
            pltpu.VMEM((rows_r, cols_r, depth), f32),
            pltpu.VMEM((chunk, cols_f, depth), f32),
        ],
        compiler_params=pltpu.CompilerParams(dimension_semantics=("arbitrary",)),
    )(taps_x, taps_y, field, fwd_z)


def rl_step(source, registered, estimate, weight, taps_x, taps_y, bg, fwd_z, adj_z, given):
    views, rows_r, cols_r, depth = registered.shape
    rows, cols = estimate.shape[:2]
    taps = taps_x.shape[1]
    cols_f = cols_r + taps - 1
    chunk = 4
    deep = DEEP
    f32 = jnp.float32

    def kernel(tx_ref, ty_ref, bg_ref, src_ref, reg_ref, est_ref, w_ref, fz_ref, az_ref,
               out_ref, q_ref, t1_ref, t2_ref, s_ref):
        v = pl.program_id(0)
        if not given:
            conv_xy(src_ref, t1_ref, q_ref, tx_ref, ty_ref, v, False, rows_r, chunk, taps, cols_r)

        def depth_rows(c, carry):
            r0 = pl.multiple_of(c * deep, deep)
            if given:
                blurred = src_ref[0, pl.ds(r0, deep)].reshape(deep * cols_r, depth)
            else:
                flat = q_ref[pl.ds(r0, deep)].reshape(deep * cols_r, depth)
                blurred = jnp.dot(flat, fz_ref[0], precision=MATMUL, preferred_element_type=f32)
            reg = reg_ref[0, pl.ds(r0, deep)].astype(f32).reshape(deep * cols_r, depth)
            ratio = reg / (blurred + bg_ref[v])
            back = jnp.dot(ratio, az_ref[0], precision=MATMUL, preferred_element_type=f32)
            q_ref[pl.ds(r0, deep)] = back.reshape(deep, cols_r, depth)
            return carry

        lax.fori_loop(0, rows_r // deep, depth_rows, 0)

        def finish(rs, acc2):
            @pl.when(v == 0)
            def _():
                s_ref[rs] = acc2

            @pl.when((v > 0) & (v < views - 1))
            def _():
                s_ref[rs] = s_ref[rs] + acc2

            @pl.when(v == views - 1)
            def _():
                out_ref[rs] = est_ref[rs] * (s_ref[rs] + acc2) / w_ref[rs]

        conv_xy(q_ref, t2_ref, None, tx_ref, ty_ref, v, True, rows, chunk, taps, cols, finish)

    smem = pl.BlockSpec(memory_space=pltpu.SMEM)
    whole3 = lambda shape: pl.BlockSpec(shape, lambda v: (0, 0, 0))
    per_view = pl.BlockSpec((1, rows_r, cols_r, depth), lambda v: (v, 0, 0, 0))
    return pl.pallas_call(
        kernel,
        grid=(views,),
        in_specs=[
            smem,
            smem,
            smem,
            per_view if given else whole3(source.shape),
            per_view,
            whole3(estimate.shape),
            whole3(weight.shape),
            pl.BlockSpec((1, depth, depth), lambda v: (v, 0, 0)),
            pl.BlockSpec((1, depth, depth), lambda v: (v, 0, 0)),
        ],
        out_specs=whole3(estimate.shape),
        out_shape=jax.ShapeDtypeStruct(estimate.shape, f32),
        scratch_shapes=[
            pltpu.VMEM((rows_r, cols_r, depth), f32),
            pltpu.VMEM((chunk, cols_f, depth), f32),
            pltpu.VMEM((chunk, cols_r, depth), f32),
            pltpu.VMEM((rows, cols, depth), f32),
        ],
        compiler_params=pltpu.CompilerParams(dimension_semantics=("arbitrary",)),
    )(taps_x, taps_y, bg, source, registered, estimate, weight, fwd_z, adj_z)


def local(views, offsets, background, psf_x, psf_y, psf_z, start):
    rows_x, rows_y, depth = start.shape
    nx = lax.axis_size("bx")
    ny = lax.axis_size("by")
    full_x = rows_x * nx
    full_y = rows_y * ny
    middle = (psf_x.shape[1] - 1) // 2
    h = middle
    ix = lax.axis_index("bx")
    iy = lax.axis_index("by")

    padded_start = halo_2d(start, 2 * h)

    taps_x = psf_x / jnp.sum(psf_x, axis=1, keepdims=True)
    taps_y = psf_y / jnp.sum(psf_y, axis=1, keepdims=True)
    taps_z = psf_z / jnp.sum(psf_z, axis=1, keepdims=True)
    fwd_x = band_rows(taps_x, rows_x + 2 * h)
    fwd_y = band_rows(taps_y, rows_y + 2 * h)
    fwd_z = depth_band(taps_z, depth)
    adj_x = band_rows(taps_x[:, ::-1], rows_x)
    adj_y = band_rows(taps_y[:, ::-1], rows_y)
    adj_z = jnp.swapaxes(fwd_z, 1, 2)

    pad_y = SHIFT + h
    vpad = jnp.pad(views, ((0, 0), (0, 0), (pad_y, pad_y), (0, 0)))
    cols = full_y + 2 * h
    shifted = jnp.stack(
        [
            lax.dynamic_slice_in_dim(vpad[w], SHIFT + offsets[w, 1], cols, axis=1)
            for w in range(V)
        ]
    )
    chunks = jnp.concatenate(
        [shifted[:, :, k * rows_y : k * rows_y + rows_y + 2 * h] for k in range(ny)], axis=2
    )
    routed = lax.all_to_all(chunks, "by", split_axis=2, concat_axis=1, tiled=True)

    reach = SHIFT + h
    prev_rows = (reach, h, reach, 0)
    next_rows = (0, reach, h, reach)
    prev_send = jnp.concatenate(
        [routed[w, rows_x - prev_rows[w] :] for w in range(V) if prev_rows[w]], axis=0
    )
    next_send = jnp.concatenate(
        [routed[w, : next_rows[w]] for w in range(V) if next_rows[w]], axis=0
    )
    prev_got = lax.ppermute(prev_send, "bx", shift_pairs(nx, 1))
    next_got = lax.ppermute(next_send, "bx", shift_pairs(nx, -1))
    blurred = blur_views(padded_start, taps_x, taps_y, fwd_z, V)
    blurred, prev_got, next_got = lax.optimization_barrier((blurred, prev_got, next_got))

    base_x = ix * rows_x - h + jnp.arange(rows_x + 2 * h, dtype=jnp.int32)
    base_y = iy * rows_y - h + jnp.arange(rows_y + 2 * h, dtype=jnp.int32)
    inside_x = (base_x >= 0) & (base_x < full_x)
    inside_y = (base_y >= 0) & (base_y < full_y)
    inside = inside_x[:, None] & inside_y[None, :]

    registered = []
    at_prev = 0
    at_next = 0
    for w in range(V):
        parts = []
        if prev_rows[w]:
            parts.append(prev_got[at_prev : at_prev + prev_rows[w]])
            at_prev += prev_rows[w]
        parts.append(routed[w])
        if next_rows[w]:
            parts.append(next_got[at_next : at_next + next_rows[w]])
            at_next += next_rows[w]
        ext = jnp.concatenate(parts, axis=0)
        moved = lax.dynamic_slice_in_dim(
            ext, prev_rows[w] - h + offsets[w, 0], rows_x + 2 * h, axis=0
        )
        registered.append(jnp.where(inside[:, :, None], moved, jnp.zeros((), moved.dtype)))
    registered = jnp.stack(registered)

    cover_x = (
        (base_x[None, :] + offsets[:, 0:1] >= 0) & (base_x[None, :] + offsets[:, 0:1] < full_x)
    ) & inside_x[None, :]
    cover_y = (
        (base_y[None, :] + offsets[:, 1:2] >= 0) & (base_y[None, :] + offsets[:, 1:2] < full_y)
    ) & inside_y[None, :]
    weight_x = jnp.einsum("vij,vj->vi", adj_x, cover_x.astype(jnp.float32), precision=HIGHEST)
    weight_y = jnp.einsum("vij,vj->vi", adj_y, cover_y.astype(jnp.float32), precision=HIGHEST)
    weight_z = jnp.sum(adj_z, axis=1)
    weight = jnp.sum(
        weight_x[:, :, None, None] * weight_y[:, None, :, None] * weight_z[:, None, None, :], axis=0
    )

    estimate = start
    for sweep in range(ITERS):
        if sweep == 0:
            source = blurred
        else:
            source = halo_rows_cols(estimate, 2 * h)
        estimate = rl_step(source, registered, estimate, weight, taps_x, taps_y, background,
                           fwd_z, adj_z, sweep == 0)
    return estimate


def solution(mesh):
    return jax.shard_map(
        local,
        mesh=mesh,
        in_specs=(P(None, ("bx", "by"), None, None), P(), P(), P(), P(), P(), P("bx", "by", None)),
        out_specs=P("bx", "by", None),
        check_vma=False,
    )
```

```python
import jax
import jax.numpy as jnp
from jax import lax
from jax.sharding import PartitionSpec as P
from jax.experimental import pallas as pl
from jax.experimental.pallas import tpu as pltpu

V = 4
SHIFT = 16
ITERS = 2
HIGHEST = lax.Precision.HIGHEST
MATMUL = lax.Precision.HIGH
DEEP = 36


def shift_pairs(count, step):
    if step > 0:
        return [(i, i + step) for i in range(count - step)]
    return [(i - step, i) for i in range(count + step)]


def halo_2d(block, width):
    nx = lax.axis_size("bx")
    ny = lax.axis_size("by")
    low = block.astype(jnp.bfloat16)
    w = width
    up = lax.ppermute(low[-w:], "bx", shift_pairs(nx, 1))
    down = lax.ppermute(low[:w], "bx", shift_pairs(nx, -1))
    left = lax.ppermute(low[:, -w:], "by", shift_pairs(ny, 1))
    right = lax.ppermute(low[:, :w], "by", shift_pairs(ny, -1))

    def corner(part, dx, dy):
        pairs = []
        for i in range(nx):
            for j in range(ny):
                ti, tj = i + dx, j + dy
                if 0 <= ti < nx and 0 <= tj < ny:
                    pairs.append((i * ny + j, ti * ny + tj))
        return lax.ppermute(part, ("bx", "by"), pairs)

    up_left = corner(low[-w:, -w:], 1, 1)
    up_right = corner(low[-w:, :w], 1, -1)
    down_left = corner(low[:w, -w:], -1, 1)
    down_right = corner(low[:w, :w], -1, -1)
    f = block.dtype
    top = jnp.concatenate([up_left, up, up_right], axis=1).astype(f)
    mid = jnp.concatenate([left.astype(f), block, right.astype(f)], axis=1)
    bottom = jnp.concatenate([down_left, down, down_right], axis=1).astype(f)
    return jnp.concatenate([top, mid, bottom], axis=0)


def halo_rows_cols(block, width):
    nx = lax.axis_size("bx")
    ny = lax.axis_size("by")
    w = width
    f = block.dtype
    low = block.astype(jnp.bfloat16)
    up = lax.ppermute(low[-w:], "bx", shift_pairs(nx, 1))
    down = lax.ppermute(low[:w], "bx", shift_pairs(nx, -1))
    tall = jnp.concatenate([up, low, down], axis=0)
    left = lax.ppermute(tall[:, -w:], "by", shift_pairs(ny, 1))
    right = lax.ppermute(tall[:, :w], "by", shift_pairs(ny, -1))
    middle = jnp.concatenate([up.astype(f), block, down.astype(f)], axis=0)
    return jnp.concatenate([left.astype(f), middle, right.astype(f)], axis=1)


def band_rows(taps, extent):
    length = taps.shape[1]
    distance = jnp.arange(extent + length - 1)[None, :] - jnp.arange(extent)[:, None]
    picked = distance[:, :, None] == jnp.arange(length)[None, None, :]
    return jnp.sum(jnp.where(picked[None], taps[:, None, None, :], 0.0), axis=3)


def depth_band(taps, extent):
    length = taps.shape[1]
    middle = (length - 1) // 2
    distance = jnp.arange(extent)[:, None] - jnp.arange(extent)[None, :] + middle
    picked = distance[:, :, None] == jnp.arange(length)[None, None, :]
    return jnp.sum(jnp.where(picked[None], taps[:, None, None, :], 0.0), axis=3)


def conv_xy(src_ref, t_ref, dst_ref, tx_ref, ty_ref, v, flip, count, chunk, taps, cols_out,
            finish=None):
    def tap(ref, k):
        return ref[v, taps - 1 - k] if flip else ref[v, k]

    def rows(c, carry):
        r0 = pl.multiple_of(c * chunk, chunk)
        acc = tap(tx_ref, 0) * src_ref[pl.ds(r0, chunk)]
        for a in range(1, taps):
            acc = acc + tap(tx_ref, a) * src_ref[pl.ds(r0 + a, chunk)]
        t_ref[...] = acc
        acc2 = tap(ty_ref, 0) * t_ref[:, pl.ds(0, cols_out), :]
        for b in range(1, taps):
            acc2 = acc2 + tap(ty_ref, b) * t_ref[:, pl.ds(b, cols_out), :]
        if finish is None:
            dst_ref[pl.ds(r0, chunk)] = acc2
        else:
            finish(pl.ds(r0, chunk), acc2)
        return carry

    lax.fori_loop(0, count // chunk, rows, 0)


def blur_views(field, taps_x, taps_y, fwd_z, views):
    rows_f, cols_f, depth = field.shape
    taps = taps_x.shape[1]
    rows_r = rows_f - (taps - 1)
    cols_r = cols_f - (taps - 1)
    chunk = 4
    deep = DEEP
    f32 = jnp.float32

    def kernel(tx_ref, ty_ref, field_ref, fz_ref, out_ref, q_ref, t1_ref):
        v = pl.program_id(0)
        conv_xy(field_ref, t1_ref, q_ref, tx_ref, ty_ref, v, False, rows_r, chunk, taps, cols_r)

        def depth_rows(c, carry):
            r0 = pl.multiple_of(c * deep, deep)
            flat = q_ref[pl.ds(r0, deep)].reshape(deep * cols_r, depth)
            blurred = jnp.dot(flat, fz_ref[0], precision=MATMUL, preferred_element_type=f32)
            out_ref[0, pl.ds(r0, deep)] = blurred.reshape(deep, cols_r, depth)
            return carry

        lax.fori_loop(0, rows_r // deep, depth_rows, 0)

    smem = pl.BlockSpec(memory_space=pltpu.SMEM)
    return pl.pallas_call(
        kernel,
        grid=(views,),
        in_specs=[
            smem,
            smem,
            pl.BlockSpec(field.shape, lambda v: (0, 0, 0)),
            pl.BlockSpec((1, depth, depth), lambda v: (v, 0, 0)),
        ],
        out_specs=pl.BlockSpec((1, rows_r, cols_r, depth), lambda v: (v, 0, 0, 0)),
        out_shape=jax.ShapeDtypeStruct((views, rows_r, cols_r, depth), f32),
        scratch_shapes=[
            pltpu.VMEM((rows_r, cols_r, depth), f32),
            pltpu.VMEM((chunk, cols_f, depth), f32),
        ],
        compiler_params=pltpu.CompilerParams(dimension_semantics=("arbitrary",)),
    )(taps_x, taps_y, field, fwd_z)


def rl_step(source, registered, estimate, weight, taps_x, taps_y, bg, fwd_z, adj_z, given):
    views, rows_r, cols_r, depth = registered.shape
    rows, cols = estimate.shape[:2]
    taps = taps_x.shape[1]
    cols_f = cols_r + taps - 1
    chunk = 4
    deep = DEEP
    f32 = jnp.float32

    def kernel(tx_ref, ty_ref, bg_ref, src_ref, reg_ref, est_ref, w_ref, fz_ref, az_ref,
               out_ref, q_ref, t1_ref, t2_ref, s_ref):
        v = pl.program_id(0)
        if not given:
            conv_xy(src_ref, t1_ref, q_ref, tx_ref, ty_ref, v, False, rows_r, chunk, taps, cols_r)

        def depth_rows(c, carry):
            r0 = pl.multiple_of(c * deep, deep)
            if given:
                blurred = src_ref[0, pl.ds(r0, deep)].reshape(deep * cols_r, depth)
            else:
                flat = q_ref[pl.ds(r0, deep)].reshape(deep * cols_r, depth)
                blurred = jnp.dot(flat, fz_ref[0], precision=MATMUL, preferred_element_type=f32)
            reg = reg_ref[0, pl.ds(r0, deep)].astype(f32).reshape(deep * cols_r, depth)
            ratio = reg / (blurred + bg_ref[v])
            back = jnp.dot(ratio, az_ref[0], precision=MATMUL, preferred_element_type=f32)
            q_ref[pl.ds(r0, deep)] = back.reshape(deep, cols_r, depth)
            return carry

        lax.fori_loop(0, rows_r // deep, depth_rows, 0)

        def finish(rs, acc2):
            @pl.when(v == 0)
            def _():
                s_ref[rs] = acc2

            @pl.when((v > 0) & (v < views - 1))
            def _():
                s_ref[rs] = s_ref[rs] + acc2

            @pl.when(v == views - 1)
            def _():
                out_ref[rs] = est_ref[rs] * (s_ref[rs] + acc2) / w_ref[rs]

        conv_xy(q_ref, t2_ref, None, tx_ref, ty_ref, v, True, rows, chunk, taps, cols, finish)

    smem = pl.BlockSpec(memory_space=pltpu.SMEM)
    whole3 = lambda shape: pl.BlockSpec(shape, lambda v: (0, 0, 0))
    per_view = pl.BlockSpec((1, rows_r, cols_r, depth), lambda v: (v, 0, 0, 0))
    return pl.pallas_call(
        kernel,
        grid=(views,),
        in_specs=[
            smem,
            smem,
            smem,
            per_view if given else whole3(source.shape),
            per_view,
            whole3(estimate.shape),
            whole3(weight.shape),
            pl.BlockSpec((1, depth, depth), lambda v: (v, 0, 0)),
            pl.BlockSpec((1, depth, depth), lambda v: (v, 0, 0)),
        ],
        out_specs=whole3(estimate.shape),
        out_shape=jax.ShapeDtypeStruct(estimate.shape, f32),
        scratch_shapes=[
            pltpu.VMEM((rows_r, cols_r, depth), f32),
            pltpu.VMEM((chunk, cols_f, depth), f32),
            pltpu.VMEM((chunk, cols_r, depth), f32),
            pltpu.VMEM((rows, cols, depth), f32),
        ],
        compiler_params=pltpu.CompilerParams(dimension_semantics=("arbitrary",)),
    )(taps_x, taps_y, bg, source, registered, estimate, weight, fwd_z, adj_z)


def local(views, offsets, background, psf_x, psf_y, psf_z, start):
    rows_x, rows_y, depth = start.shape
    nx = lax.axis_size("bx")
    ny = lax.axis_size("by")
    full_x = rows_x * nx
    full_y = rows_y * ny
    middle = (psf_x.shape[1] - 1) // 2
    h = middle
    ix = lax.axis_index("bx")
    iy = lax.axis_index("by")

    padded_start = halo_2d(start, 2 * h)

    taps_x = psf_x / jnp.sum(psf_x, axis=1, keepdims=True)
    taps_y = psf_y / jnp.sum(psf_y, axis=1, keepdims=True)
    taps_z = psf_z / jnp.sum(psf_z, axis=1, keepdims=True)
    fwd_x = band_rows(taps_x, rows_x + 2 * h)
    fwd_y = band_rows(taps_y, rows_y + 2 * h)
    fwd_z = depth_band(taps_z, depth)
    adj_x = band_rows(taps_x[:, ::-1], rows_x)
    adj_y = band_rows(taps_y[:, ::-1], rows_y)
    adj_z = jnp.swapaxes(fwd_z, 1, 2)

    pad_y = SHIFT + h
    vpad = jnp.pad(views, ((0, 0), (0, 0), (pad_y, pad_y), (0, 0)))
    cols = full_y + 2 * h
    shifted = jnp.stack(
        [
            lax.dynamic_slice_in_dim(vpad[w], SHIFT + offsets[w, 1], cols, axis=1)
            for w in range(V)
        ]
    )
    chunks = jnp.concatenate(
        [shifted[:, :, k * rows_y : k * rows_y + rows_y + 2 * h] for k in range(ny)], axis=2
    )
    routed = lax.all_to_all(chunks, "by", split_axis=2, concat_axis=1, tiled=True)
    padded_start, routed = lax.optimization_barrier((padded_start, routed))

    reach = SHIFT + h
    prev_rows = (reach, h, reach, 0)
    next_rows = (0, reach, h, reach)
    prev_send = jnp.concatenate(
        [routed[w, rows_x - prev_rows[w] :] for w in range(V) if prev_rows[w]], axis=0
    )
    next_send = jnp.concatenate(
        [routed[w, : next_rows[w]] for w in range(V) if next_rows[w]], axis=0
    )
    prev_got = lax.ppermute(prev_send, "bx", shift_pairs(nx, 1))
    next_got = lax.ppermute(next_send, "bx", shift_pairs(nx, -1))
    blurred = blur_views(padded_start, taps_x, taps_y, fwd_z, V)
    blurred, prev_got, next_got = lax.optimization_barrier((blurred, prev_got, next_got))

    base_x = ix * rows_x - h + jnp.arange(rows_x + 2 * h, dtype=jnp.int32)
    base_y = iy * rows_y - h + jnp.arange(rows_y + 2 * h, dtype=jnp.int32)
    inside_x = (base_x >= 0) & (base_x < full_x)
    inside_y = (base_y >= 0) & (base_y < full_y)
    inside = inside_x[:, None] & inside_y[None, :]

    registered = []
    at_prev = 0
    at_next = 0
    for w in range(V):
        parts = []
        if prev_rows[w]:
            parts.append(prev_got[at_prev : at_prev + prev_rows[w]])
            at_prev += prev_rows[w]
        parts.append(routed[w])
        if next_rows[w]:
            parts.append(next_got[at_next : at_next + next_rows[w]])
            at_next += next_rows[w]
        ext = jnp.concatenate(parts, axis=0)
        moved = lax.dynamic_slice_in_dim(
            ext, prev_rows[w] - h + offsets[w, 0], rows_x + 2 * h, axis=0
        )
        registered.append(jnp.where(inside[:, :, None], moved, jnp.zeros((), moved.dtype)))
    registered = jnp.stack(registered)

    cover_x = (
        (base_x[None, :] + offsets[:, 0:1] >= 0) & (base_x[None, :] + offsets[:, 0:1] < full_x)
    ) & inside_x[None, :]
    cover_y = (
        (base_y[None, :] + offsets[:, 1:2] >= 0) & (base_y[None, :] + offsets[:, 1:2] < full_y)
    ) & inside_y[None, :]
    weight_x = jnp.einsum("vij,vj->vi", adj_x, cover_x.astype(jnp.float32), precision=HIGHEST)
    weight_y = jnp.einsum("vij,vj->vi", adj_y, cover_y.astype(jnp.float32), precision=HIGHEST)
    weight_z = jnp.sum(adj_z, axis=1)
    weight = jnp.sum(
        weight_x[:, :, None, None] * weight_y[:, None, :, None] * weight_z[:, None, None, :], axis=0
    )

    estimate = start
    for sweep in range(ITERS):
        if sweep == 0:
            source = blurred
        else:
            source = halo_rows_cols(estimate, 2 * h)
        estimate = rl_step(source, registered, estimate, weight, taps_x, taps_y, background,
                           fwd_z, adj_z, sweep == 0)
    return estimate


def solution(mesh):
    return jax.shard_map(
        local,
        mesh=mesh,
        in_specs=(P(None, ("bx", "by"), None, None), P(), P(), P(), P(), P(), P("bx", "by", None)),
        out_specs=P("bx", "by", None),
        check_vma=False,
    )
```

```python
import jax
import jax.numpy as jnp
from jax import lax
from jax.sharding import PartitionSpec as P
from jax.experimental import pallas as pl
from jax.experimental.pallas import tpu as pltpu

V = 4
SHIFT = 16
ITERS = 2
HIGHEST = lax.Precision.HIGHEST
MATMUL = lax.Precision.HIGH
DEEP = 36


def shift_pairs(count, step):
    if step > 0:
        return [(i, i + step) for i in range(count - step)]
    return [(i - step, i) for i in range(count + step)]


def halo_2d(block, width):
    nx = lax.axis_size("bx")
    ny = lax.axis_size("by")
    low = block.astype(jnp.bfloat16)
    w = width
    up = lax.ppermute(low[-w:], "bx", shift_pairs(nx, 1))
    down = lax.ppermute(low[:w], "bx", shift_pairs(nx, -1))
    left = lax.ppermute(low[:, -w:], "by", shift_pairs(ny, 1))
    right = lax.ppermute(low[:, :w], "by", shift_pairs(ny, -1))

    def corner(part, dx, dy):
        pairs = []
        for i in range(nx):
            for j in range(ny):
                ti, tj = i + dx, j + dy
                if 0 <= ti < nx and 0 <= tj < ny:
                    pairs.append((i * ny + j, ti * ny + tj))
        return lax.ppermute(part, ("bx", "by"), pairs)

    up_left = corner(low[-w:, -w:], 1, 1)
    up_right = corner(low[-w:, :w], 1, -1)
    down_left = corner(low[:w, -w:], -1, 1)
    down_right = corner(low[:w, :w], -1, -1)
    f = block.dtype
    top = jnp.concatenate([up_left, up, up_right], axis=1).astype(f)
    mid = jnp.concatenate([left.astype(f), block, right.astype(f)], axis=1)
    bottom = jnp.concatenate([down_left, down, down_right], axis=1).astype(f)
    return jnp.concatenate([top, mid, bottom], axis=0)


def halo_rows_cols(block, width):
    nx = lax.axis_size("bx")
    ny = lax.axis_size("by")
    w = width
    f = block.dtype
    low = block.astype(jnp.bfloat16)
    up = lax.ppermute(low[-w:], "bx", shift_pairs(nx, 1))
    down = lax.ppermute(low[:w], "bx", shift_pairs(nx, -1))
    tall = jnp.concatenate([up, low, down], axis=0)
    left = lax.ppermute(tall[:, -w:], "by", shift_pairs(ny, 1))
    right = lax.ppermute(tall[:, :w], "by", shift_pairs(ny, -1))
    middle = jnp.concatenate([up.astype(f), block, down.astype(f)], axis=0)
    return jnp.concatenate([left.astype(f), middle, right.astype(f)], axis=1)


def band_rows(taps, extent):
    length = taps.shape[1]
    distance = jnp.arange(extent + length - 1)[None, :] - jnp.arange(extent)[:, None]
    picked = distance[:, :, None] == jnp.arange(length)[None, None, :]
    return jnp.sum(jnp.where(picked[None], taps[:, None, None, :], 0.0), axis=3)


def depth_band(taps, extent):
    length = taps.shape[1]
    middle = (length - 1) // 2
    distance = jnp.arange(extent)[:, None] - jnp.arange(extent)[None, :] + middle
    picked = distance[:, :, None] == jnp.arange(length)[None, None, :]
    return jnp.sum(jnp.where(picked[None], taps[:, None, None, :], 0.0), axis=3)


def conv_xy(src_ref, t_ref, dst_ref, tx_ref, ty_ref, v, flip, count, chunk, taps, cols_out,
            finish=None):
    def tap(ref, k):
        return ref[v, taps - 1 - k] if flip else ref[v, k]

    def rows(c, carry):
        r0 = pl.multiple_of(c * chunk, chunk)
        acc = tap(tx_ref, 0) * src_ref[pl.ds(r0, chunk)]
        for a in range(1, taps):
            acc = acc + tap(tx_ref, a) * src_ref[pl.ds(r0 + a, chunk)]
        t_ref[...] = acc
        acc2 = tap(ty_ref, 0) * t_ref[:, pl.ds(0, cols_out), :]
        for b in range(1, taps):
            acc2 = acc2 + tap(ty_ref, b) * t_ref[:, pl.ds(b, cols_out), :]
        if finish is None:
            dst_ref[pl.ds(r0, chunk)] = acc2
        else:
            finish(pl.ds(r0, chunk), acc2)
        return carry

    lax.fori_loop(0, count // chunk, rows, 0)


def blur_views(field, taps_x, taps_y, fwd_z, views):
    rows_f, cols_f, depth = field.shape
    taps = taps_x.shape[1]
    rows_r = rows_f - (taps - 1)
    cols_r = cols_f - (taps - 1)
    chunk = 4
    deep = DEEP
    f32 = jnp.float32

    def kernel(tx_ref, ty_ref, field_ref, fz_ref, out_ref, q_ref, t1_ref):
        v = pl.program_id(0)
        conv_xy(field_ref, t1_ref, q_ref, tx_ref, ty_ref, v, False, rows_r, chunk, taps, cols_r)

        def depth_rows(c, carry):
            r0 = pl.multiple_of(c * deep, deep)
            flat = q_ref[pl.ds(r0, deep)].reshape(deep * cols_r, depth)
            blurred = jnp.dot(flat, fz_ref[0], precision=MATMUL, preferred_element_type=f32)
            out_ref[0, pl.ds(r0, deep)] = blurred.reshape(deep, cols_r, depth)
            return carry

        lax.fori_loop(0, rows_r // deep, depth_rows, 0)

    smem = pl.BlockSpec(memory_space=pltpu.SMEM)
    return pl.pallas_call(
        kernel,
        grid=(views,),
        in_specs=[
            smem,
            smem,
            pl.BlockSpec(field.shape, lambda v: (0, 0, 0)),
            pl.BlockSpec((1, depth, depth), lambda v: (v, 0, 0)),
        ],
        out_specs=pl.BlockSpec((1, rows_r, cols_r, depth), lambda v: (v, 0, 0, 0)),
        out_shape=jax.ShapeDtypeStruct((views, rows_r, cols_r, depth), f32),
        scratch_shapes=[
            pltpu.VMEM((rows_r, cols_r, depth), f32),
            pltpu.VMEM((chunk, cols_f, depth), f32),
        ],
        compiler_params=pltpu.CompilerParams(dimension_semantics=("arbitrary",)),
    )(taps_x, taps_y, field, fwd_z)


def rl_step(source, registered, estimate, weight, taps_x, taps_y, bg, fwd_z, adj_z, given):
    views, rows_r, cols_r, depth = registered.shape
    rows, cols = estimate.shape[:2]
    taps = taps_x.shape[1]
    cols_f = cols_r + taps - 1
    chunk = 4
    deep = DEEP
    f32 = jnp.float32

    def kernel(tx_ref, ty_ref, bg_ref, src_ref, reg_ref, est_ref, w_ref, fz_ref, az_ref,
               out_ref, q_ref, t1_ref, t2_ref, s_ref):
        v = pl.program_id(0)
        if not given:
            conv_xy(src_ref, t1_ref, q_ref, tx_ref, ty_ref, v, False, rows_r, chunk, taps, cols_r)

        def depth_rows(c, carry):
            r0 = pl.multiple_of(c * deep, deep)
            if given:
                blurred = src_ref[0, pl.ds(r0, deep)].reshape(deep * cols_r, depth)
            else:
                flat = q_ref[pl.ds(r0, deep)].reshape(deep * cols_r, depth)
                blurred = jnp.dot(flat, fz_ref[0], precision=MATMUL, preferred_element_type=f32)
            reg = reg_ref[0, pl.ds(r0, deep)].astype(f32).reshape(deep * cols_r, depth)
            ratio = reg / (blurred + bg_ref[v])
            back = jnp.dot(ratio, az_ref[0], precision=MATMUL, preferred_element_type=f32)
            q_ref[pl.ds(r0, deep)] = back.reshape(deep, cols_r, depth)
            return carry

        lax.fori_loop(0, rows_r // deep, depth_rows, 0)

        def finish(rs, acc2):
            @pl.when(v == 0)
            def _():
                s_ref[rs] = acc2

            @pl.when((v > 0) & (v < views - 1))
            def _():
                s_ref[rs] = s_ref[rs] + acc2

            @pl.when(v == views - 1)
            def _():
                out_ref[rs] = est_ref[rs] * (s_ref[rs] + acc2) / w_ref[rs]

        conv_xy(q_ref, t2_ref, None, tx_ref, ty_ref, v, True, rows, chunk, taps, cols, finish)

    smem = pl.BlockSpec(memory_space=pltpu.SMEM)
    whole3 = lambda shape: pl.BlockSpec(shape, lambda v: (0, 0, 0))
    per_view = pl.BlockSpec((1, rows_r, cols_r, depth), lambda v: (v, 0, 0, 0))
    return pl.pallas_call(
        kernel,
        grid=(views,),
        in_specs=[
            smem,
            smem,
            smem,
            per_view if given else whole3(source.shape),
            per_view,
            whole3(estimate.shape),
            whole3(weight.shape),
            pl.BlockSpec((1, depth, depth), lambda v: (v, 0, 0)),
            pl.BlockSpec((1, depth, depth), lambda v: (v, 0, 0)),
        ],
        out_specs=whole3(estimate.shape),
        out_shape=jax.ShapeDtypeStruct(estimate.shape, f32),
        scratch_shapes=[
            pltpu.VMEM((rows_r, cols_r, depth), f32),
            pltpu.VMEM((chunk, cols_f, depth), f32),
            pltpu.VMEM((chunk, cols_r, depth), f32),
            pltpu.VMEM((rows, cols, depth), f32),
        ],
        compiler_params=pltpu.CompilerParams(dimension_semantics=("arbitrary",)),
    )(taps_x, taps_y, bg, source, registered, estimate, weight, fwd_z, adj_z)


def local(views, offsets, background, psf_x, psf_y, psf_z, start):
    rows_x, rows_y, depth = start.shape
    nx = lax.axis_size("bx")
    ny = lax.axis_size("by")
    full_x = rows_x * nx
    full_y = rows_y * ny
    middle = (psf_x.shape[1] - 1) // 2
    h = middle
    ix = lax.axis_index("bx")
    iy = lax.axis_index("by")

    padded_start = halo_2d(start, 2 * h)

    taps_x = psf_x / jnp.sum(psf_x, axis=1, keepdims=True)
    taps_y = psf_y / jnp.sum(psf_y, axis=1, keepdims=True)
    taps_z = psf_z / jnp.sum(psf_z, axis=1, keepdims=True)
    fwd_x = band_rows(taps_x, rows_x + 2 * h)
    fwd_y = band_rows(taps_y, rows_y + 2 * h)
    fwd_z = depth_band(taps_z, depth)
    adj_x = band_rows(taps_x[:, ::-1], rows_x)
    adj_y = band_rows(taps_y[:, ::-1], rows_y)
    adj_z = jnp.swapaxes(fwd_z, 1, 2)

    base_x = ix * rows_x - h + jnp.arange(rows_x + 2 * h, dtype=jnp.int32)
    base_y = iy * rows_y - h + jnp.arange(rows_y + 2 * h, dtype=jnp.int32)
    inside_x = (base_x >= 0) & (base_x < full_x)
    inside_y = (base_y >= 0) & (base_y < full_y)
    inside = inside_x[:, None] & inside_y[None, :]

    cover_x = (
        (base_x[None, :] + offsets[:, 0:1] >= 0) & (base_x[None, :] + offsets[:, 0:1] < full_x)
    ) & inside_x[None, :]
    cover_y = (
        (base_y[None, :] + offsets[:, 1:2] >= 0) & (base_y[None, :] + offsets[:, 1:2] < full_y)
    ) & inside_y[None, :]
    weight_x = jnp.einsum("vij,vj->vi", adj_x, cover_x.astype(jnp.float32), precision=HIGHEST)
    weight_y = jnp.einsum("vij,vj->vi", adj_y, cover_y.astype(jnp.float32), precision=HIGHEST)
    weight_z = jnp.sum(adj_z, axis=1)
    weight = jnp.sum(
        weight_x[:, :, None, None] * weight_y[:, None, :, None] * weight_z[:, None, None, :], axis=0
    )

    pad_y = SHIFT + h
    vpad = jnp.pad(views, ((0, 0), (0, 0), (pad_y, pad_y), (0, 0)))
    cols = full_y + 2 * h
    shifted = jnp.stack(
        [
            lax.dynamic_slice_in_dim(vpad[w], SHIFT + offsets[w, 1], cols, axis=1)
            for w in range(V)
        ]
    )
    chunks = jnp.concatenate(
        [shifted[:, :, k * rows_y : k * rows_y + rows_y + 2 * h] for k in range(ny)], axis=2
    )
    routed = lax.all_to_all(chunks, "by", split_axis=2, concat_axis=1, tiled=True)
    padded_start, weight, routed = lax.optimization_barrier((padded_start, weight, routed))

    reach = SHIFT + h
    prev_rows = (reach, h, reach, 0)
    next_rows = (0, reach, h, reach)
    prev_send = jnp.concatenate(
        [routed[w, rows_x - prev_rows[w] :] for w in range(V) if prev_rows[w]], axis=0
    )
    next_send = jnp.concatenate(
        [routed[w, : next_rows[w]] for w in range(V) if next_rows[w]], axis=0
    )
    prev_got = lax.ppermute(prev_send, "bx", shift_pairs(nx, 1))
    next_got = lax.ppermute(next_send, "bx", shift_pairs(nx, -1))
    blurred = blur_views(padded_start, taps_x, taps_y, fwd_z, V)
    blurred, prev_got, next_got = lax.optimization_barrier((blurred, prev_got, next_got))

    registered = []
    at_prev = 0
    at_next = 0
    for w in range(V):
        parts = []
        if prev_rows[w]:
            parts.append(prev_got[at_prev : at_prev + prev_rows[w]])
            at_prev += prev_rows[w]
        parts.append(routed[w])
        if next_rows[w]:
            parts.append(next_got[at_next : at_next + next_rows[w]])
            at_next += next_rows[w]
        ext = jnp.concatenate(parts, axis=0)
        moved = lax.dynamic_slice_in_dim(
            ext, prev_rows[w] - h + offsets[w, 0], rows_x + 2 * h, axis=0
        )
        registered.append(jnp.where(inside[:, :, None], moved.astype(jnp.float32), 0.0))
    registered = jnp.stack(registered)

    estimate = start
    for sweep in range(ITERS):
        if sweep == 0:
            source = blurred
        else:
            source = halo_rows_cols(estimate, 2 * h)
        estimate = rl_step(source, registered, estimate, weight, taps_x, taps_y, background,
                           fwd_z, adj_z, sweep == 0)
    return estimate


def solution(mesh):
    return jax.shard_map(
        local,
        mesh=mesh,
        in_specs=(P(None, ("bx", "by"), None, None), P(), P(), P(), P(), P(), P("bx", "by", None)),
        out_specs=P("bx", "by", None),
        check_vma=False,
    )
```

```python
import jax
import jax.numpy as jnp
from jax import lax
from jax.sharding import PartitionSpec as P
from jax.experimental import pallas as pl
from jax.experimental.pallas import tpu as pltpu

V = 4
SHIFT = 16
ITERS = 2
HIGHEST = lax.Precision.HIGHEST
MATMUL = lax.Precision.HIGH
DEEP = 36


def shift_pairs(count, step):
    if step > 0:
        return [(i, i + step) for i in range(count - step)]
    return [(i - step, i) for i in range(count + step)]


def halo_2d(block, width):
    nx = lax.axis_size("bx")
    ny = lax.axis_size("by")
    low = block.astype(jnp.bfloat16)
    w = width
    up = lax.ppermute(low[-w:], "bx", shift_pairs(nx, 1))
    down = lax.ppermute(low[:w], "bx", shift_pairs(nx, -1))
    left = lax.ppermute(low[:, -w:], "by", shift_pairs(ny, 1))
    right = lax.ppermute(low[:, :w], "by", shift_pairs(ny, -1))

    def corner(part, dx, dy):
        pairs = []
        for i in range(nx):
            for j in range(ny):
                ti, tj = i + dx, j + dy
                if 0 <= ti < nx and 0 <= tj < ny:
                    pairs.append((i * ny + j, ti * ny + tj))
        return lax.ppermute(part, ("bx", "by"), pairs)

    up_left = corner(low[-w:, -w:], 1, 1)
    up_right = corner(low[-w:, :w], 1, -1)
    down_left = corner(low[:w, -w:], -1, 1)
    down_right = corner(low[:w, :w], -1, -1)
    f = block.dtype
    top = jnp.concatenate([up_left, up, up_right], axis=1).astype(f)
    mid = jnp.concatenate([left.astype(f), block, right.astype(f)], axis=1)
    bottom = jnp.concatenate([down_left, down, down_right], axis=1).astype(f)
    return jnp.concatenate([top, mid, bottom], axis=0)


def halo_rows_cols(block, width):
    nx = lax.axis_size("bx")
    ny = lax.axis_size("by")
    w = width
    f = block.dtype
    low = block.astype(jnp.bfloat16)
    up = lax.ppermute(low[-w:], "bx", shift_pairs(nx, 1))
    down = lax.ppermute(low[:w], "bx", shift_pairs(nx, -1))
    tall = jnp.concatenate([up, low, down], axis=0)
    left = lax.ppermute(tall[:, -w:], "by", shift_pairs(ny, 1))
    right = lax.ppermute(tall[:, :w], "by", shift_pairs(ny, -1))
    middle = jnp.concatenate([up.astype(f), block, down.astype(f)], axis=0)
    return jnp.concatenate([left.astype(f), middle, right.astype(f)], axis=1)


def band_rows(taps, extent):
    length = taps.shape[1]
    distance = jnp.arange(extent + length - 1)[None, :] - jnp.arange(extent)[:, None]
    picked = distance[:, :, None] == jnp.arange(length)[None, None, :]
    return jnp.sum(jnp.where(picked[None], taps[:, None, None, :], 0.0), axis=3)


def depth_band(taps, extent):
    length = taps.shape[1]
    middle = (length - 1) // 2
    distance = jnp.arange(extent)[:, None] - jnp.arange(extent)[None, :] + middle
    picked = distance[:, :, None] == jnp.arange(length)[None, None, :]
    return jnp.sum(jnp.where(picked[None], taps[:, None, None, :], 0.0), axis=3)


def conv_xy(src_ref, t_ref, dst_ref, tx_ref, ty_ref, v, flip, count, chunk, taps, cols_out,
            finish=None):
    def tap(ref, k):
        return ref[v, taps - 1 - k] if flip else ref[v, k]

    def rows(c, carry):
        r0 = pl.multiple_of(c * chunk, chunk)
        acc = tap(tx_ref, 0) * src_ref[pl.ds(r0, chunk)]
        for a in range(1, taps):
            acc = acc + tap(tx_ref, a) * src_ref[pl.ds(r0 + a, chunk)]
        t_ref[...] = acc
        acc2 = tap(ty_ref, 0) * t_ref[:, pl.ds(0, cols_out), :]
        for b in range(1, taps):
            acc2 = acc2 + tap(ty_ref, b) * t_ref[:, pl.ds(b, cols_out), :]
        if finish is None:
            dst_ref[pl.ds(r0, chunk)] = acc2
        else:
            finish(pl.ds(r0, chunk), acc2)
        return carry

    lax.fori_loop(0, count // chunk, rows, 0)


def blur_views(field, taps_x, taps_y, fwd_z, views):
    rows_f, cols_f, depth = field.shape
    taps = taps_x.shape[1]
    rows_r = rows_f - (taps - 1)
    cols_r = cols_f - (taps - 1)
    chunk = 2
    deep = DEEP
    f32 = jnp.float32

    def kernel(tx_ref, ty_ref, field_ref, fz_ref, out_ref, q_ref, t1_ref):
        v = pl.program_id(0)
        conv_xy(field_ref, t1_ref, q_ref, tx_ref, ty_ref, v, False, rows_r, chunk, taps, cols_r)

        def depth_rows(c, carry):
            r0 = pl.multiple_of(c * deep, deep)
            flat = q_ref[pl.ds(r0, deep)].reshape(deep * cols_r, depth)
            blurred = jnp.dot(flat, fz_ref[0], precision=MATMUL, preferred_element_type=f32)
            out_ref[0, pl.ds(r0, deep)] = blurred.reshape(deep, cols_r, depth)
            return carry

        lax.fori_loop(0, rows_r // deep, depth_rows, 0)

    smem = pl.BlockSpec(memory_space=pltpu.SMEM)
    return pl.pallas_call(
        kernel,
        grid=(views,),
        in_specs=[
            smem,
            smem,
            pl.BlockSpec(field.shape, lambda v: (0, 0, 0)),
            pl.BlockSpec((1, depth, depth), lambda v: (v, 0, 0)),
        ],
        out_specs=pl.BlockSpec((1, rows_r, cols_r, depth), lambda v: (v, 0, 0, 0)),
        out_shape=jax.ShapeDtypeStruct((views, rows_r, cols_r, depth), f32),
        scratch_shapes=[
            pltpu.VMEM((rows_r, cols_r, depth), f32),
            pltpu.VMEM((chunk, cols_f, depth), f32),
        ],
        compiler_params=pltpu.CompilerParams(dimension_semantics=("arbitrary",)),
    )(taps_x, taps_y, field, fwd_z)


def rl_step(source, registered, estimate, weight, taps_x, taps_y, bg, fwd_z, adj_z, given):
    views, rows_r, cols_r, depth = registered.shape
    rows, cols = estimate.shape[:2]
    taps = taps_x.shape[1]
    cols_f = cols_r + taps - 1
    chunk = 2
    deep = DEEP
    f32 = jnp.float32

    def kernel(tx_ref, ty_ref, bg_ref, src_ref, reg_ref, est_ref, w_ref, fz_ref, az_ref,
               out_ref, q_ref, t1_ref, t2_ref, s_ref):
        v = pl.program_id(0)
        if not given:
            conv_xy(src_ref, t1_ref, q_ref, tx_ref, ty_ref, v, False, rows_r, chunk, taps, cols_r)

        def depth_rows(c, carry):
            r0 = pl.multiple_of(c * deep, deep)
            if given:
                blurred = src_ref[0, pl.ds(r0, deep)].reshape(deep * cols_r, depth)
            else:
                flat = q_ref[pl.ds(r0, deep)].reshape(deep * cols_r, depth)
                blurred = jnp.dot(flat, fz_ref[0], precision=MATMUL, preferred_element_type=f32)
            reg = reg_ref[0, pl.ds(r0, deep)].astype(f32).reshape(deep * cols_r, depth)
            ratio = reg / (blurred + bg_ref[v])
            back = jnp.dot(ratio, az_ref[0], precision=MATMUL, preferred_element_type=f32)
            q_ref[pl.ds(r0, deep)] = back.reshape(deep, cols_r, depth)
            return carry

        lax.fori_loop(0, rows_r // deep, depth_rows, 0)

        def finish(rs, acc2):
            @pl.when(v == 0)
            def _():
                s_ref[rs] = acc2

            @pl.when((v > 0) & (v < views - 1))
            def _():
                s_ref[rs] = s_ref[rs] + acc2

            @pl.when(v == views - 1)
            def _():
                out_ref[rs] = est_ref[rs] * (s_ref[rs] + acc2) / w_ref[rs]

        conv_xy(q_ref, t2_ref, None, tx_ref, ty_ref, v, True, rows, chunk, taps, cols, finish)

    smem = pl.BlockSpec(memory_space=pltpu.SMEM)
    whole3 = lambda shape: pl.BlockSpec(shape, lambda v: (0, 0, 0))
    per_view = pl.BlockSpec((1, rows_r, cols_r, depth), lambda v: (v, 0, 0, 0))
    return pl.pallas_call(
        kernel,
        grid=(views,),
        in_specs=[
            smem,
            smem,
            smem,
            per_view if given else whole3(source.shape),
            per_view,
            whole3(estimate.shape),
            whole3(weight.shape),
            pl.BlockSpec((1, depth, depth), lambda v: (v, 0, 0)),
            pl.BlockSpec((1, depth, depth), lambda v: (v, 0, 0)),
        ],
        out_specs=whole3(estimate.shape),
        out_shape=jax.ShapeDtypeStruct(estimate.shape, f32),
        scratch_shapes=[
            pltpu.VMEM((rows_r, cols_r, depth), f32),
            pltpu.VMEM((chunk, cols_f, depth), f32),
            pltpu.VMEM((chunk, cols_r, depth), f32),
            pltpu.VMEM((rows, cols, depth), f32),
        ],
        compiler_params=pltpu.CompilerParams(dimension_semantics=("arbitrary",)),
    )(taps_x, taps_y, bg, source, registered, estimate, weight, fwd_z, adj_z)


def local(views, offsets, background, psf_x, psf_y, psf_z, start):
    rows_x, rows_y, depth = start.shape
    nx = lax.axis_size("bx")
    ny = lax.axis_size("by")
    full_x = rows_x * nx
    full_y = rows_y * ny
    middle = (psf_x.shape[1] - 1) // 2
    h = middle
    ix = lax.axis_index("bx")
    iy = lax.axis_index("by")

    padded_start = halo_2d(start, 2 * h)

    taps_x = psf_x / jnp.sum(psf_x, axis=1, keepdims=True)
    taps_y = psf_y / jnp.sum(psf_y, axis=1, keepdims=True)
    taps_z = psf_z / jnp.sum(psf_z, axis=1, keepdims=True)
    fwd_x = band_rows(taps_x, rows_x + 2 * h)
    fwd_y = band_rows(taps_y, rows_y + 2 * h)
    fwd_z = depth_band(taps_z, depth)
    adj_x = band_rows(taps_x[:, ::-1], rows_x)
    adj_y = band_rows(taps_y[:, ::-1], rows_y)
    adj_z = jnp.swapaxes(fwd_z, 1, 2)

    base_x = ix * rows_x - h + jnp.arange(rows_x + 2 * h, dtype=jnp.int32)
    base_y = iy * rows_y - h + jnp.arange(rows_y + 2 * h, dtype=jnp.int32)
    inside_x = (base_x >= 0) & (base_x < full_x)
    inside_y = (base_y >= 0) & (base_y < full_y)
    inside = inside_x[:, None] & inside_y[None, :]

    cover_x = (
        (base_x[None, :] + offsets[:, 0:1] >= 0) & (base_x[None, :] + offsets[:, 0:1] < full_x)
    ) & inside_x[None, :]
    cover_y = (
        (base_y[None, :] + offsets[:, 1:2] >= 0) & (base_y[None, :] + offsets[:, 1:2] < full_y)
    ) & inside_y[None, :]
    weight_x = jnp.einsum("vij,vj->vi", adj_x, cover_x.astype(jnp.float32), precision=HIGHEST)
    weight_y = jnp.einsum("vij,vj->vi", adj_y, cover_y.astype(jnp.float32), precision=HIGHEST)
    weight_z = jnp.sum(adj_z, axis=1)
    weight = jnp.sum(
        weight_x[:, :, None, None] * weight_y[:, None, :, None] * weight_z[:, None, None, :], axis=0
    )

    pad_y = SHIFT + h
    vpad = jnp.pad(views, ((0, 0), (0, 0), (pad_y, pad_y), (0, 0)))
    cols = full_y + 2 * h
    shifted = jnp.stack(
        [
            lax.dynamic_slice_in_dim(vpad[w], SHIFT + offsets[w, 1], cols, axis=1)
            for w in range(V)
        ]
    )
    chunks = jnp.concatenate(
        [shifted[:, :, k * rows_y : k * rows_y + rows_y + 2 * h] for k in range(ny)], axis=2
    )
    routed = lax.all_to_all(chunks, "by", split_axis=2, concat_axis=1, tiled=True)
    padded_start, weight, routed = lax.optimization_barrier((padded_start, weight, routed))

    reach = SHIFT + h
    prev_rows = (reach, h, reach, 0)
    next_rows = (0, reach, h, reach)
    prev_send = jnp.concatenate(
        [routed[w, rows_x - prev_rows[w] :] for w in range(V) if prev_rows[w]], axis=0
    )
    next_send = jnp.concatenate(
        [routed[w, : next_rows[w]] for w in range(V) if next_rows[w]], axis=0
    )
    prev_got = lax.ppermute(prev_send, "bx", shift_pairs(nx, 1))
    next_got = lax.ppermute(next_send, "bx", shift_pairs(nx, -1))
    blurred = blur_views(padded_start, taps_x, taps_y, fwd_z, V)
    blurred, prev_got, next_got = lax.optimization_barrier((blurred, prev_got, next_got))

    registered = []
    at_prev = 0
    at_next = 0
    for w in range(V):
        parts = []
        if prev_rows[w]:
            parts.append(prev_got[at_prev : at_prev + prev_rows[w]])
            at_prev += prev_rows[w]
        parts.append(routed[w])
        if next_rows[w]:
            parts.append(next_got[at_next : at_next + next_rows[w]])
            at_next += next_rows[w]
        ext = jnp.concatenate(parts, axis=0)
        moved = lax.dynamic_slice_in_dim(
            ext, prev_rows[w] - h + offsets[w, 0], rows_x + 2 * h, axis=0
        )
        registered.append(jnp.where(inside[:, :, None], moved.astype(jnp.float32), 0.0))
    registered = jnp.stack(registered)

    estimate = start
    for sweep in range(ITERS):
        if sweep == 0:
            source = blurred
        else:
            source = halo_rows_cols(estimate, 2 * h)
        estimate = rl_step(source, registered, estimate, weight, taps_x, taps_y, background,
                           fwd_z, adj_z, sweep == 0)
    return estimate


def solution(mesh):
    return jax.shard_map(
        local,
        mesh=mesh,
        in_specs=(P(None, ("bx", "by"), None, None), P(), P(), P(), P(), P(), P("bx", "by", None)),
        out_specs=P("bx", "by", None),
        check_vma=False,
    )
```

```python
import jax
import jax.numpy as jnp
from jax import lax
from jax.sharding import PartitionSpec as P
from jax.experimental import pallas as pl
from jax.experimental.pallas import tpu as pltpu

V = 4
SHIFT = 16
ITERS = 2
HIGHEST = lax.Precision.HIGHEST
MATMUL = lax.Precision.HIGH
DEEP = 72


def shift_pairs(count, step):
    if step > 0:
        return [(i, i + step) for i in range(count - step)]
    return [(i - step, i) for i in range(count + step)]


def halo_2d(block, width):
    nx = lax.axis_size("bx")
    ny = lax.axis_size("by")
    low = block.astype(jnp.bfloat16)
    w = width
    up = lax.ppermute(low[-w:], "bx", shift_pairs(nx, 1))
    down = lax.ppermute(low[:w], "bx", shift_pairs(nx, -1))
    left = lax.ppermute(low[:, -w:], "by", shift_pairs(ny, 1))
    right = lax.ppermute(low[:, :w], "by", shift_pairs(ny, -1))

    def corner(part, dx, dy):
        pairs = []
        for i in range(nx):
            for j in range(ny):
                ti, tj = i + dx, j + dy
                if 0 <= ti < nx and 0 <= tj < ny:
                    pairs.append((i * ny + j, ti * ny + tj))
        return lax.ppermute(part, ("bx", "by"), pairs)

    up_left = corner(low[-w:, -w:], 1, 1)
    up_right = corner(low[-w:, :w], 1, -1)
    down_left = corner(low[:w, -w:], -1, 1)
    down_right = corner(low[:w, :w], -1, -1)
    f = block.dtype
    top = jnp.concatenate([up_left, up, up_right], axis=1).astype(f)
    mid = jnp.concatenate([left.astype(f), block, right.astype(f)], axis=1)
    bottom = jnp.concatenate([down_left, down, down_right], axis=1).astype(f)
    return jnp.concatenate([top, mid, bottom], axis=0)


def halo_rows_cols(block, width):
    nx = lax.axis_size("bx")
    ny = lax.axis_size("by")
    w = width
    f = block.dtype
    low = block.astype(jnp.bfloat16)
    up = lax.ppermute(low[-w:], "bx", shift_pairs(nx, 1))
    down = lax.ppermute(low[:w], "bx", shift_pairs(nx, -1))
    tall = jnp.concatenate([up, low, down], axis=0)
    left = lax.ppermute(tall[:, -w:], "by", shift_pairs(ny, 1))
    right = lax.ppermute(tall[:, :w], "by", shift_pairs(ny, -1))
    middle = jnp.concatenate([up.astype(f), block, down.astype(f)], axis=0)
    return jnp.concatenate([left.astype(f), middle, right.astype(f)], axis=1)


def band_rows(taps, extent):
    length = taps.shape[1]
    distance = jnp.arange(extent + length - 1)[None, :] - jnp.arange(extent)[:, None]
    picked = distance[:, :, None] == jnp.arange(length)[None, None, :]
    return jnp.sum(jnp.where(picked[None], taps[:, None, None, :], 0.0), axis=3)


def depth_band(taps, extent):
    length = taps.shape[1]
    middle = (length - 1) // 2
    distance = jnp.arange(extent)[:, None] - jnp.arange(extent)[None, :] + middle
    picked = distance[:, :, None] == jnp.arange(length)[None, None, :]
    return jnp.sum(jnp.where(picked[None], taps[:, None, None, :], 0.0), axis=3)


def conv_xy(src_ref, t_ref, dst_ref, tx_ref, ty_ref, v, flip, count, chunk, taps, cols_out,
            finish=None):
    def tap(ref, k):
        return ref[v, taps - 1 - k] if flip else ref[v, k]

    def rows(c, carry):
        r0 = pl.multiple_of(c * chunk, chunk)
        acc = tap(tx_ref, 0) * src_ref[pl.ds(r0, chunk)]
        for a in range(1, taps):
            acc = acc + tap(tx_ref, a) * src_ref[pl.ds(r0 + a, chunk)]
        t_ref[...] = acc
        acc2 = tap(ty_ref, 0) * t_ref[:, pl.ds(0, cols_out), :]
        for b in range(1, taps):
            acc2 = acc2 + tap(ty_ref, b) * t_ref[:, pl.ds(b, cols_out), :]
        if finish is None:
            dst_ref[pl.ds(r0, chunk)] = acc2
        else:
            finish(pl.ds(r0, chunk), acc2)
        return carry

    lax.fori_loop(0, count // chunk, rows, 0)


def blur_views(field, taps_x, taps_y, fwd_z, views):
    rows_f, cols_f, depth = field.shape
    taps = taps_x.shape[1]
    rows_r = rows_f - (taps - 1)
    cols_r = cols_f - (taps - 1)
    chunk = 2
    deep = DEEP
    f32 = jnp.float32

    def kernel(tx_ref, ty_ref, field_ref, fz_ref, out_ref, q_ref, t1_ref):
        v = pl.program_id(0)
        conv_xy(field_ref, t1_ref, q_ref, tx_ref, ty_ref, v, False, rows_r, chunk, taps, cols_r)

        def depth_rows(c, carry):
            r0 = pl.multiple_of(c * deep, deep)
            flat = q_ref[pl.ds(r0, deep)].reshape(deep * cols_r, depth)
            blurred = jnp.dot(flat, fz_ref[0], precision=MATMUL, preferred_element_type=f32)
            out_ref[0, pl.ds(r0, deep)] = blurred.reshape(deep, cols_r, depth)
            return carry

        lax.fori_loop(0, rows_r // deep, depth_rows, 0)

    smem = pl.BlockSpec(memory_space=pltpu.SMEM)
    return pl.pallas_call(
        kernel,
        grid=(views,),
        in_specs=[
            smem,
            smem,
            pl.BlockSpec(field.shape, lambda v: (0, 0, 0)),
            pl.BlockSpec((1, depth, depth), lambda v: (v, 0, 0)),
        ],
        out_specs=pl.BlockSpec((1, rows_r, cols_r, depth), lambda v: (v, 0, 0, 0)),
        out_shape=jax.ShapeDtypeStruct((views, rows_r, cols_r, depth), f32),
        scratch_shapes=[
            pltpu.VMEM((rows_r, cols_r, depth), f32),
            pltpu.VMEM((chunk, cols_f, depth), f32),
        ],
        compiler_params=pltpu.CompilerParams(dimension_semantics=("arbitrary",)),
    )(taps_x, taps_y, field, fwd_z)


def rl_step(source, registered, estimate, weight, taps_x, taps_y, bg, fwd_z, adj_z, given):
    views, rows_r, cols_r, depth = registered.shape
    rows, cols = estimate.shape[:2]
    taps = taps_x.shape[1]
    cols_f = cols_r + taps - 1
    chunk = 2
    deep = DEEP
    f32 = jnp.float32

    def kernel(tx_ref, ty_ref, bg_ref, src_ref, reg_ref, est_ref, w_ref, fz_ref, az_ref,
               out_ref, q_ref, t1_ref, t2_ref, s_ref):
        v = pl.program_id(0)
        if not given:
            conv_xy(src_ref, t1_ref, q_ref, tx_ref, ty_ref, v, False, rows_r, chunk, taps, cols_r)

        def depth_rows(c, carry):
            r0 = pl.multiple_of(c * deep, deep)
            if given:
                blurred = src_ref[0, pl.ds(r0, deep)].reshape(deep * cols_r, depth)
            else:
                flat = q_ref[pl.ds(r0, deep)].reshape(deep * cols_r, depth)
                blurred = jnp.dot(flat, fz_ref[0], precision=MATMUL, preferred_element_type=f32)
            reg = reg_ref[0, pl.ds(r0, deep)].astype(f32).reshape(deep * cols_r, depth)
            ratio = reg / (blurred + bg_ref[v])
            back = jnp.dot(ratio, az_ref[0], precision=MATMUL, preferred_element_type=f32)
            q_ref[pl.ds(r0, deep)] = back.reshape(deep, cols_r, depth)
            return carry

        lax.fori_loop(0, rows_r // deep, depth_rows, 0)

        def finish(rs, acc2):
            @pl.when(v == 0)
            def _():
                s_ref[rs] = acc2

            @pl.when((v > 0) & (v < views - 1))
            def _():
                s_ref[rs] = s_ref[rs] + acc2

            @pl.when(v == views - 1)
            def _():
                out_ref[rs] = est_ref[rs] * (s_ref[rs] + acc2) / w_ref[rs]

        conv_xy(q_ref, t2_ref, None, tx_ref, ty_ref, v, True, rows, chunk, taps, cols, finish)

    smem = pl.BlockSpec(memory_space=pltpu.SMEM)
    whole3 = lambda shape: pl.BlockSpec(shape, lambda v: (0, 0, 0))
    per_view = pl.BlockSpec((1, rows_r, cols_r, depth), lambda v: (v, 0, 0, 0))
    return pl.pallas_call(
        kernel,
        grid=(views,),
        in_specs=[
            smem,
            smem,
            smem,
            per_view if given else whole3(source.shape),
            per_view,
            whole3(estimate.shape),
            whole3(weight.shape),
            pl.BlockSpec((1, depth, depth), lambda v: (v, 0, 0)),
            pl.BlockSpec((1, depth, depth), lambda v: (v, 0, 0)),
        ],
        out_specs=whole3(estimate.shape),
        out_shape=jax.ShapeDtypeStruct(estimate.shape, f32),
        scratch_shapes=[
            pltpu.VMEM((rows_r, cols_r, depth), f32),
            pltpu.VMEM((chunk, cols_f, depth), f32),
            pltpu.VMEM((chunk, cols_r, depth), f32),
            pltpu.VMEM((rows, cols, depth), f32),
        ],
        compiler_params=pltpu.CompilerParams(dimension_semantics=("arbitrary",)),
    )(taps_x, taps_y, bg, source, registered, estimate, weight, fwd_z, adj_z)


def local(views, offsets, background, psf_x, psf_y, psf_z, start):
    rows_x, rows_y, depth = start.shape
    nx = lax.axis_size("bx")
    ny = lax.axis_size("by")
    full_x = rows_x * nx
    full_y = rows_y * ny
    middle = (psf_x.shape[1] - 1) // 2
    h = middle
    ix = lax.axis_index("bx")
    iy = lax.axis_index("by")

    padded_start = halo_2d(start, 2 * h)

    taps_x = psf_x / jnp.sum(psf_x, axis=1, keepdims=True)
    taps_y = psf_y / jnp.sum(psf_y, axis=1, keepdims=True)
    taps_z = psf_z / jnp.sum(psf_z, axis=1, keepdims=True)
    fwd_x = band_rows(taps_x, rows_x + 2 * h)
    fwd_y = band_rows(taps_y, rows_y + 2 * h)
    fwd_z = depth_band(taps_z, depth)
    adj_x = band_rows(taps_x[:, ::-1], rows_x)
    adj_y = band_rows(taps_y[:, ::-1], rows_y)
    adj_z = jnp.swapaxes(fwd_z, 1, 2)

    base_x = ix * rows_x - h + jnp.arange(rows_x + 2 * h, dtype=jnp.int32)
    base_y = iy * rows_y - h + jnp.arange(rows_y + 2 * h, dtype=jnp.int32)
    inside_x = (base_x >= 0) & (base_x < full_x)
    inside_y = (base_y >= 0) & (base_y < full_y)
    inside = inside_x[:, None] & inside_y[None, :]

    cover_x = (
        (base_x[None, :] + offsets[:, 0:1] >= 0) & (base_x[None, :] + offsets[:, 0:1] < full_x)
    ) & inside_x[None, :]
    cover_y = (
        (base_y[None, :] + offsets[:, 1:2] >= 0) & (base_y[None, :] + offsets[:, 1:2] < full_y)
    ) & inside_y[None, :]
    weight_x = jnp.einsum("vij,vj->vi", adj_x, cover_x.astype(jnp.float32), precision=HIGHEST)
    weight_y = jnp.einsum("vij,vj->vi", adj_y, cover_y.astype(jnp.float32), precision=HIGHEST)
    weight_z = jnp.sum(adj_z, axis=1)
    weight = jnp.sum(
        weight_x[:, :, None, None] * weight_y[:, None, :, None] * weight_z[:, None, None, :], axis=0
    )

    pad_y = SHIFT + h
    vpad = jnp.pad(views, ((0, 0), (0, 0), (pad_y, pad_y), (0, 0)))
    cols = full_y + 2 * h
    shifted = jnp.stack(
        [
            lax.dynamic_slice_in_dim(vpad[w], SHIFT + offsets[w, 1], cols, axis=1)
            for w in range(V)
        ]
    )
    chunks = jnp.concatenate(
        [shifted[:, :, k * rows_y : k * rows_y + rows_y + 2 * h] for k in range(ny)], axis=2
    )
    routed = lax.all_to_all(chunks, "by", split_axis=2, concat_axis=1, tiled=True)
    padded_start, weight, routed = lax.optimization_barrier((padded_start, weight, routed))

    reach = SHIFT + h
    prev_rows = (reach, h, reach, 0)
    next_rows = (0, reach, h, reach)
    prev_send = jnp.concatenate(
        [routed[w, rows_x - prev_rows[w] :] for w in range(V) if prev_rows[w]], axis=0
    )
    next_send = jnp.concatenate(
        [routed[w, : next_rows[w]] for w in range(V) if next_rows[w]], axis=0
    )
    prev_got = lax.ppermute(prev_send, "bx", shift_pairs(nx, 1))
    next_got = lax.ppermute(next_send, "bx", shift_pairs(nx, -1))
    blurred = blur_views(padded_start, taps_x, taps_y, fwd_z, V)
    blurred, prev_got, next_got = lax.optimization_barrier((blurred, prev_got, next_got))

    registered = []
    at_prev = 0
    at_next = 0
    for w in range(V):
        parts = []
        if prev_rows[w]:
            parts.append(prev_got[at_prev : at_prev + prev_rows[w]])
            at_prev += prev_rows[w]
        parts.append(routed[w])
        if next_rows[w]:
            parts.append(next_got[at_next : at_next + next_rows[w]])
            at_next += next_rows[w]
        ext = jnp.concatenate(parts, axis=0)
        moved = lax.dynamic_slice_in_dim(
            ext, prev_rows[w] - h + offsets[w, 0], rows_x + 2 * h, axis=0
        )
        registered.append(jnp.where(inside[:, :, None], moved.astype(jnp.float32), 0.0))
    registered = jnp.stack(registered)

    estimate = start
    for sweep in range(ITERS):
        if sweep == 0:
            source = blurred
        else:
            source = halo_rows_cols(estimate, 2 * h)
        estimate = rl_step(source, registered, estimate, weight, taps_x, taps_y, background,
                           fwd_z, adj_z, sweep == 0)
    return estimate


def solution(mesh):
    return jax.shard_map(
        local,
        mesh=mesh,
        in_specs=(P(None, ("bx", "by"), None, None), P(), P(), P(), P(), P(), P("bx", "by", None)),
        out_specs=P("bx", "by", None),
        check_vma=False,
    )
```

```python
import jax
import jax.numpy as jnp
from jax import lax
from jax.sharding import PartitionSpec as P
from jax.experimental import pallas as pl
from jax.experimental.pallas import tpu as pltpu

V = 4
SHIFT = 16
ITERS = 2
HIGHEST = lax.Precision.HIGHEST
MATMUL = lax.Precision.HIGH
DEEP = 72


def shift_pairs(count, step):
    if step > 0:
        return [(i, i + step) for i in range(count - step)]
    return [(i - step, i) for i in range(count + step)]


def halo_2d(block, width):
    nx = lax.axis_size("bx")
    ny = lax.axis_size("by")
    low = block.astype(jnp.bfloat16)
    w = width
    up = lax.ppermute(low[-w:], "bx", shift_pairs(nx, 1))
    down = lax.ppermute(low[:w], "bx", shift_pairs(nx, -1))
    left = lax.ppermute(low[:, -w:], "by", shift_pairs(ny, 1))
    right = lax.ppermute(low[:, :w], "by", shift_pairs(ny, -1))

    def corner(part, dx, dy):
        pairs = []
        for i in range(nx):
            for j in range(ny):
                ti, tj = i + dx, j + dy
                if 0 <= ti < nx and 0 <= tj < ny:
                    pairs.append((i * ny + j, ti * ny + tj))
        return lax.ppermute(part, ("bx", "by"), pairs)

    up_left = corner(low[-w:, -w:], 1, 1)
    up_right = corner(low[-w:, :w], 1, -1)
    down_left = corner(low[:w, -w:], -1, 1)
    down_right = corner(low[:w, :w], -1, -1)
    f = block.dtype
    top = jnp.concatenate([up_left, up, up_right], axis=1).astype(f)
    mid = jnp.concatenate([left.astype(f), block, right.astype(f)], axis=1)
    bottom = jnp.concatenate([down_left, down, down_right], axis=1).astype(f)
    return jnp.concatenate([top, mid, bottom], axis=0)


def halo_rows_cols(block, width):
    nx = lax.axis_size("bx")
    ny = lax.axis_size("by")
    w = width
    f = block.dtype
    low = block.astype(jnp.bfloat16)
    up = lax.ppermute(low[-w:], "bx", shift_pairs(nx, 1))
    down = lax.ppermute(low[:w], "bx", shift_pairs(nx, -1))
    tall = jnp.concatenate([up, low, down], axis=0)
    left = lax.ppermute(tall[:, -w:], "by", shift_pairs(ny, 1))
    right = lax.ppermute(tall[:, :w], "by", shift_pairs(ny, -1))
    middle = jnp.concatenate([up.astype(f), block, down.astype(f)], axis=0)
    return jnp.concatenate([left.astype(f), middle, right.astype(f)], axis=1)


def band_rows(taps, extent):
    length = taps.shape[1]
    distance = jnp.arange(extent + length - 1)[None, :] - jnp.arange(extent)[:, None]
    picked = distance[:, :, None] == jnp.arange(length)[None, None, :]
    return jnp.sum(jnp.where(picked[None], taps[:, None, None, :], 0.0), axis=3)


def depth_band(taps, extent):
    length = taps.shape[1]
    middle = (length - 1) // 2
    distance = jnp.arange(extent)[:, None] - jnp.arange(extent)[None, :] + middle
    picked = distance[:, :, None] == jnp.arange(length)[None, None, :]
    return jnp.sum(jnp.where(picked[None], taps[:, None, None, :], 0.0), axis=3)


def conv_xy(src_ref, t_ref, dst_ref, tx_ref, ty_ref, v, flip, count, chunk, taps, cols_out,
            finish=None):
    def tap(ref, k):
        return ref[v, taps - 1 - k] if flip else ref[v, k]

    def rows(c, carry):
        r0 = pl.multiple_of(c * chunk, chunk)
        acc = tap(tx_ref, 0) * src_ref[pl.ds(r0, chunk)]
        for a in range(1, taps):
            acc = acc + tap(tx_ref, a) * src_ref[pl.ds(r0 + a, chunk)]
        t_ref[...] = acc
        acc2 = tap(ty_ref, 0) * t_ref[:, pl.ds(0, cols_out), :]
        for b in range(1, taps):
            acc2 = acc2 + tap(ty_ref, b) * t_ref[:, pl.ds(b, cols_out), :]
        if finish is None:
            dst_ref[pl.ds(r0, chunk)] = acc2
        else:
            finish(pl.ds(r0, chunk), acc2)
        return carry

    lax.fori_loop(0, count // chunk, rows, 0, unroll=2)


def blur_views(field, taps_x, taps_y, fwd_z, views):
    rows_f, cols_f, depth = field.shape
    taps = taps_x.shape[1]
    rows_r = rows_f - (taps - 1)
    cols_r = cols_f - (taps - 1)
    chunk = 2
    deep = DEEP
    f32 = jnp.float32

    def kernel(tx_ref, ty_ref, field_ref, fz_ref, out_ref, q_ref, t1_ref):
        v = pl.program_id(0)
        conv_xy(field_ref, t1_ref, q_ref, tx_ref, ty_ref, v, False, rows_r, chunk, taps, cols_r)

        def depth_rows(c, carry):
            r0 = pl.multiple_of(c * deep, deep)
            flat = q_ref[pl.ds(r0, deep)].reshape(deep * cols_r, depth)
            blurred = jnp.dot(flat, fz_ref[0], precision=MATMUL, preferred_element_type=f32)
            out_ref[0, pl.ds(r0, deep)] = blurred.reshape(deep, cols_r, depth)
            return carry

        lax.fori_loop(0, rows_r // deep, depth_rows, 0)

    smem = pl.BlockSpec(memory_space=pltpu.SMEM)
    return pl.pallas_call(
        kernel,
        grid=(views,),
        in_specs=[
            smem,
            smem,
            pl.BlockSpec(field.shape, lambda v: (0, 0, 0)),
            pl.BlockSpec((1, depth, depth), lambda v: (v, 0, 0)),
        ],
        out_specs=pl.BlockSpec((1, rows_r, cols_r, depth), lambda v: (v, 0, 0, 0)),
        out_shape=jax.ShapeDtypeStruct((views, rows_r, cols_r, depth), f32),
        scratch_shapes=[
            pltpu.VMEM((rows_r, cols_r, depth), f32),
            pltpu.VMEM((chunk, cols_f, depth), f32),
        ],
        compiler_params=pltpu.CompilerParams(dimension_semantics=("arbitrary",)),
    )(taps_x, taps_y, field, fwd_z)


def rl_step(source, registered, estimate, weight, taps_x, taps_y, bg, fwd_z, adj_z, given):
    views, rows_r, cols_r, depth = registered.shape
    rows, cols = estimate.shape[:2]
    taps = taps_x.shape[1]
    cols_f = cols_r + taps - 1
    chunk = 2
    deep = DEEP
    f32 = jnp.float32

    def kernel(tx_ref, ty_ref, bg_ref, src_ref, reg_ref, est_ref, w_ref, fz_ref, az_ref,
               out_ref, q_ref, t1_ref, t2_ref, s_ref):
        v = pl.program_id(0)
        if not given:
            conv_xy(src_ref, t1_ref, q_ref, tx_ref, ty_ref, v, False, rows_r, chunk, taps, cols_r)

        def depth_rows(c, carry):
            r0 = pl.multiple_of(c * deep, deep)
            if given:
                blurred = src_ref[0, pl.ds(r0, deep)].reshape(deep * cols_r, depth)
            else:
                flat = q_ref[pl.ds(r0, deep)].reshape(deep * cols_r, depth)
                blurred = jnp.dot(flat, fz_ref[0], precision=MATMUL, preferred_element_type=f32)
            reg = reg_ref[0, pl.ds(r0, deep)].astype(f32).reshape(deep * cols_r, depth)
            ratio = reg / (blurred + bg_ref[v])
            back = jnp.dot(ratio, az_ref[0], precision=MATMUL, preferred_element_type=f32)
            q_ref[pl.ds(r0, deep)] = back.reshape(deep, cols_r, depth)
            return carry

        lax.fori_loop(0, rows_r // deep, depth_rows, 0)

        def finish(rs, acc2):
            @pl.when(v == 0)
            def _():
                s_ref[rs] = acc2

            @pl.when((v > 0) & (v < views - 1))
            def _():
                s_ref[rs] = s_ref[rs] + acc2

            @pl.when(v == views - 1)
            def _():
                out_ref[rs] = est_ref[rs] * (s_ref[rs] + acc2) / w_ref[rs]

        conv_xy(q_ref, t2_ref, None, tx_ref, ty_ref, v, True, rows, chunk, taps, cols, finish)

    smem = pl.BlockSpec(memory_space=pltpu.SMEM)
    whole3 = lambda shape: pl.BlockSpec(shape, lambda v: (0, 0, 0))
    per_view = pl.BlockSpec((1, rows_r, cols_r, depth), lambda v: (v, 0, 0, 0))
    return pl.pallas_call(
        kernel,
        grid=(views,),
        in_specs=[
            smem,
            smem,
            smem,
            per_view if given else whole3(source.shape),
            per_view,
            whole3(estimate.shape),
            whole3(weight.shape),
            pl.BlockSpec((1, depth, depth), lambda v: (v, 0, 0)),
            pl.BlockSpec((1, depth, depth), lambda v: (v, 0, 0)),
        ],
        out_specs=whole3(estimate.shape),
        out_shape=jax.ShapeDtypeStruct(estimate.shape, f32),
        scratch_shapes=[
            pltpu.VMEM((rows_r, cols_r, depth), f32),
            pltpu.VMEM((chunk, cols_f, depth), f32),
            pltpu.VMEM((chunk, cols_r, depth), f32),
            pltpu.VMEM((rows, cols, depth), f32),
        ],
        compiler_params=pltpu.CompilerParams(dimension_semantics=("arbitrary",)),
    )(taps_x, taps_y, bg, source, registered, estimate, weight, fwd_z, adj_z)


def local(views, offsets, background, psf_x, psf_y, psf_z, start):
    rows_x, rows_y, depth = start.shape
    nx = lax.axis_size("bx")
    ny = lax.axis_size("by")
    full_x = rows_x * nx
    full_y = rows_y * ny
    middle = (psf_x.shape[1] - 1) // 2
    h = middle
    ix = lax.axis_index("bx")
    iy = lax.axis_index("by")

    padded_start = halo_2d(start, 2 * h)

    taps_x = psf_x / jnp.sum(psf_x, axis=1, keepdims=True)
    taps_y = psf_y / jnp.sum(psf_y, axis=1, keepdims=True)
    taps_z = psf_z / jnp.sum(psf_z, axis=1, keepdims=True)
    fwd_x = band_rows(taps_x, rows_x + 2 * h)
    fwd_y = band_rows(taps_y, rows_y + 2 * h)
    fwd_z = depth_band(taps_z, depth)
    adj_x = band_rows(taps_x[:, ::-1], rows_x)
    adj_y = band_rows(taps_y[:, ::-1], rows_y)
    adj_z = jnp.swapaxes(fwd_z, 1, 2)

    base_x = ix * rows_x - h + jnp.arange(rows_x + 2 * h, dtype=jnp.int32)
    base_y = iy * rows_y - h + jnp.arange(rows_y + 2 * h, dtype=jnp.int32)
    inside_x = (base_x >= 0) & (base_x < full_x)
    inside_y = (base_y >= 0) & (base_y < full_y)
    inside = inside_x[:, None] & inside_y[None, :]

    cover_x = (
        (base_x[None, :] + offsets[:, 0:1] >= 0) & (base_x[None, :] + offsets[:, 0:1] < full_x)
    ) & inside_x[None, :]
    cover_y = (
        (base_y[None, :] + offsets[:, 1:2] >= 0) & (base_y[None, :] + offsets[:, 1:2] < full_y)
    ) & inside_y[None, :]
    weight_x = jnp.einsum("vij,vj->vi", adj_x, cover_x.astype(jnp.float32), precision=HIGHEST)
    weight_y = jnp.einsum("vij,vj->vi", adj_y, cover_y.astype(jnp.float32), precision=HIGHEST)
    weight_z = jnp.sum(adj_z, axis=1)
    weight = jnp.sum(
        weight_x[:, :, None, None] * weight_y[:, None, :, None] * weight_z[:, None, None, :], axis=0
    )

    pad_y = SHIFT + h
    vpad = jnp.pad(views, ((0, 0), (0, 0), (pad_y, pad_y), (0, 0)))
    cols = full_y + 2 * h
    shifted = jnp.stack(
        [
            lax.dynamic_slice_in_dim(vpad[w], SHIFT + offsets[w, 1], cols, axis=1)
            for w in range(V)
        ]
    )
    chunks = jnp.concatenate(
        [shifted[:, :, k * rows_y : k * rows_y + rows_y + 2 * h] for k in range(ny)], axis=2
    )
    routed = lax.all_to_all(chunks, "by", split_axis=2, concat_axis=1, tiled=True)
    padded_start, weight, routed = lax.optimization_barrier((padded_start, weight, routed))

    reach = SHIFT + h
    prev_rows = (reach, h, reach, 0)
    next_rows = (0, reach, h, reach)
    prev_send = jnp.concatenate(
        [routed[w, rows_x - prev_rows[w] :] for w in range(V) if prev_rows[w]], axis=0
    )
    next_send = jnp.concatenate(
        [routed[w, : next_rows[w]] for w in range(V) if next_rows[w]], axis=0
    )
    prev_got = lax.ppermute(prev_send, "bx", shift_pairs(nx, 1))
    next_got = lax.ppermute(next_send, "bx", shift_pairs(nx, -1))
    blurred = blur_views(padded_start, taps_x, taps_y, fwd_z, V)
    blurred, prev_got, next_got = lax.optimization_barrier((blurred, prev_got, next_got))

    registered = []
    at_prev = 0
    at_next = 0
    for w in range(V):
        parts = []
        if prev_rows[w]:
            parts.append(prev_got[at_prev : at_prev + prev_rows[w]])
            at_prev += prev_rows[w]
        parts.append(routed[w])
        if next_rows[w]:
            parts.append(next_got[at_next : at_next + next_rows[w]])
            at_next += next_rows[w]
        ext = jnp.concatenate(parts, axis=0)
        moved = lax.dynamic_slice_in_dim(
            ext, prev_rows[w] - h + offsets[w, 0], rows_x + 2 * h, axis=0
        )
        registered.append(jnp.where(inside[:, :, None], moved.astype(jnp.float32), 0.0))
    registered = jnp.stack(registered)

    estimate = start
    for sweep in range(ITERS):
        if sweep == 0:
            source = blurred
        else:
            source = halo_rows_cols(estimate, 2 * h)
        estimate = rl_step(source, registered, estimate, weight, taps_x, taps_y, background,
                           fwd_z, adj_z, sweep == 0)
    return estimate


def solution(mesh):
    return jax.shard_map(
        local,
        mesh=mesh,
        in_specs=(P(None, ("bx", "by"), None, None), P(), P(), P(), P(), P(), P("bx", "by", None)),
        out_specs=P("bx", "by", None),
        check_vma=False,
    )
```

```python
import jax
import jax.numpy as jnp
from jax import lax
from jax.sharding import PartitionSpec as P
from jax.experimental import pallas as pl
from jax.experimental.pallas import tpu as pltpu

V = 4
SHIFT = 16
ITERS = 2
HIGHEST = lax.Precision.HIGHEST
MATMUL = lax.Precision.HIGH
DEEP = 72


def shift_pairs(count, step):
    if step > 0:
        return [(i, i + step) for i in range(count - step)]
    return [(i - step, i) for i in range(count + step)]


def halo_2d(block, width):
    nx = lax.axis_size("bx")
    ny = lax.axis_size("by")
    low = block.astype(jnp.bfloat16)
    w = width
    up = lax.ppermute(low[-w:], "bx", shift_pairs(nx, 1))
    down = lax.ppermute(low[:w], "bx", shift_pairs(nx, -1))
    left = lax.ppermute(low[:, -w:], "by", shift_pairs(ny, 1))
    right = lax.ppermute(low[:, :w], "by", shift_pairs(ny, -1))

    def corner(part, dx, dy):
        pairs = []
        for i in range(nx):
            for j in range(ny):
                ti, tj = i + dx, j + dy
                if 0 <= ti < nx and 0 <= tj < ny:
                    pairs.append((i * ny + j, ti * ny + tj))
        return lax.ppermute(part, ("bx", "by"), pairs)

    up_left = corner(low[-w:, -w:], 1, 1)
    up_right = corner(low[-w:, :w], 1, -1)
    down_left = corner(low[:w, -w:], -1, 1)
    down_right = corner(low[:w, :w], -1, -1)
    f = block.dtype
    top = jnp.concatenate([up_left, up, up_right], axis=1).astype(f)
    mid = jnp.concatenate([left.astype(f), block, right.astype(f)], axis=1)
    bottom = jnp.concatenate([down_left, down, down_right], axis=1).astype(f)
    return jnp.concatenate([top, mid, bottom], axis=0)


def halo_rows_cols(block, width):
    nx = lax.axis_size("bx")
    ny = lax.axis_size("by")
    w = width
    f = block.dtype
    low = block.astype(jnp.bfloat16)
    up = lax.ppermute(low[-w:], "bx", shift_pairs(nx, 1))
    down = lax.ppermute(low[:w], "bx", shift_pairs(nx, -1))
    tall = jnp.concatenate([up, low, down], axis=0)
    left = lax.ppermute(tall[:, -w:], "by", shift_pairs(ny, 1))
    right = lax.ppermute(tall[:, :w], "by", shift_pairs(ny, -1))
    middle = jnp.concatenate([up.astype(f), block, down.astype(f)], axis=0)
    return jnp.concatenate([left.astype(f), middle, right.astype(f)], axis=1)


def band_rows(taps, extent):
    length = taps.shape[1]
    distance = jnp.arange(extent + length - 1)[None, :] - jnp.arange(extent)[:, None]
    picked = distance[:, :, None] == jnp.arange(length)[None, None, :]
    return jnp.sum(jnp.where(picked[None], taps[:, None, None, :], 0.0), axis=3)


def depth_band(taps, extent):
    length = taps.shape[1]
    middle = (length - 1) // 2
    distance = jnp.arange(extent)[:, None] - jnp.arange(extent)[None, :] + middle
    picked = distance[:, :, None] == jnp.arange(length)[None, None, :]
    return jnp.sum(jnp.where(picked[None], taps[:, None, None, :], 0.0), axis=3)


def conv_xy(src_ref, t_ref, dst_ref, tx_ref, ty_ref, v, flip, count, chunk, taps, cols_out,
            finish=None):
    def tap(ref, k):
        return ref[v, taps - 1 - k] if flip else ref[v, k]

    def rows(c, carry):
        r0 = pl.multiple_of(c * chunk, chunk)
        acc = tap(tx_ref, 0) * src_ref[pl.ds(r0, chunk)]
        for a in range(1, taps):
            acc = acc + tap(tx_ref, a) * src_ref[pl.ds(r0 + a, chunk)]
        t_ref[...] = acc
        acc2 = tap(ty_ref, 0) * t_ref[:, pl.ds(0, cols_out), :]
        for b in range(1, taps):
            acc2 = acc2 + tap(ty_ref, b) * t_ref[:, pl.ds(b, cols_out), :]
        if finish is None:
            dst_ref[pl.ds(r0, chunk)] = acc2
        else:
            finish(pl.ds(r0, chunk), acc2)
        return carry

    lax.fori_loop(0, count // chunk, rows, 0, unroll=2)


def blur_views(field, taps_x, taps_y, fwd_z, views):
    rows_f, cols_f, depth = field.shape
    taps = taps_x.shape[1]
    rows_r = rows_f - (taps - 1)
    cols_r = cols_f - (taps - 1)
    chunk = 2
    deep = DEEP
    f32 = jnp.float32

    def kernel(tx_ref, ty_ref, field_ref, fz_ref, out_ref, q_ref, t1_ref):
        v = pl.program_id(0)
        conv_xy(field_ref, t1_ref, q_ref, tx_ref, ty_ref, v, False, rows_r, chunk, taps, cols_r)

        def depth_rows(c, carry):
            r0 = pl.multiple_of(c * deep, deep)
            flat = q_ref[pl.ds(r0, deep)].reshape(deep * cols_r, depth)
            blurred = jnp.dot(flat, fz_ref[0], precision=MATMUL, preferred_element_type=f32)
            out_ref[0, pl.ds(r0, deep)] = blurred.reshape(deep, cols_r, depth)
            return carry

        lax.fori_loop(0, rows_r // deep, depth_rows, 0)

    smem = pl.BlockSpec(memory_space=pltpu.SMEM)
    return pl.pallas_call(
        kernel,
        grid=(views,),
        in_specs=[
            smem,
            smem,
            pl.BlockSpec(field.shape, lambda v: (0, 0, 0)),
            pl.BlockSpec((1, depth, depth), lambda v: (v, 0, 0)),
        ],
        out_specs=pl.BlockSpec((1, rows_r, cols_r, depth), lambda v: (v, 0, 0, 0)),
        out_shape=jax.ShapeDtypeStruct((views, rows_r, cols_r, depth), f32),
        scratch_shapes=[
            pltpu.VMEM((rows_r, cols_r, depth), f32),
            pltpu.VMEM((chunk, cols_f, depth), f32),
        ],
        compiler_params=pltpu.CompilerParams(dimension_semantics=("arbitrary",)),
    )(taps_x, taps_y, field, fwd_z)


def rl_step(source, registered, estimate, weight, taps_x, taps_y, bg, fwd_z, adj_z, given):
    views, rows_r, cols_r, depth = registered.shape
    rows, cols = estimate.shape[:2]
    taps = taps_x.shape[1]
    cols_f = cols_r + taps - 1
    chunk = 2
    deep = DEEP
    f32 = jnp.float32

    def kernel(tx_ref, ty_ref, bg_ref, src_ref, reg_ref, est_ref, w_ref, fz_ref, az_ref,
               out_ref, q_ref, t1_ref, t2_ref, s_ref):
        v = pl.program_id(0)
        if not given:
            conv_xy(src_ref, t1_ref, q_ref, tx_ref, ty_ref, v, False, rows_r, chunk, taps, cols_r)

        def depth_rows(c, carry):
            r0 = pl.multiple_of(c * deep, deep)
            if given:
                blurred = src_ref[0, pl.ds(r0, deep)].reshape(deep * cols_r, depth)
            else:
                flat = q_ref[pl.ds(r0, deep)].reshape(deep * cols_r, depth)
                blurred = jnp.dot(flat, fz_ref[0], precision=MATMUL, preferred_element_type=f32)
            reg = reg_ref[0, pl.ds(r0, deep)].astype(f32).reshape(deep * cols_r, depth)
            ratio = reg / (blurred + bg_ref[v])
            back = jnp.dot(ratio, az_ref[0], precision=MATMUL, preferred_element_type=f32)
            q_ref[pl.ds(r0, deep)] = back.reshape(deep, cols_r, depth)
            return carry

        lax.fori_loop(0, rows_r // deep, depth_rows, 0)

        def finish(rs, acc2):
            @pl.when(v == 0)
            def _():
                s_ref[rs] = acc2

            @pl.when((v > 0) & (v < views - 1))
            def _():
                s_ref[rs] = s_ref[rs] + acc2

            @pl.when(v == views - 1)
            def _():
                out_ref[rs] = est_ref[rs] * (s_ref[rs] + acc2) / w_ref[rs]

        conv_xy(q_ref, t2_ref, None, tx_ref, ty_ref, v, True, rows, chunk, taps, cols, finish)

    smem = pl.BlockSpec(memory_space=pltpu.SMEM)
    whole3 = lambda shape: pl.BlockSpec(shape, lambda v: (0, 0, 0))
    per_view = pl.BlockSpec((1, rows_r, cols_r, depth), lambda v: (v, 0, 0, 0))
    return pl.pallas_call(
        kernel,
        grid=(views,),
        in_specs=[
            smem,
            smem,
            smem,
            per_view if given else whole3(source.shape),
            per_view,
            whole3(estimate.shape),
            whole3(weight.shape),
            pl.BlockSpec((1, depth, depth), lambda v: (v, 0, 0)),
            pl.BlockSpec((1, depth, depth), lambda v: (v, 0, 0)),
        ],
        out_specs=whole3(estimate.shape),
        out_shape=jax.ShapeDtypeStruct(estimate.shape, f32),
        scratch_shapes=[
            pltpu.VMEM((rows_r, cols_r, depth), f32),
            pltpu.VMEM((chunk, cols_f, depth), f32),
            pltpu.VMEM((chunk, cols_r, depth), f32),
            pltpu.VMEM((rows, cols, depth), f32),
        ],
        compiler_params=pltpu.CompilerParams(dimension_semantics=("arbitrary",)),
    )(taps_x, taps_y, bg, source, registered, estimate, weight, fwd_z, adj_z)


def local(views, offsets, background, psf_x, psf_y, psf_z, start):
    rows_x, rows_y, depth = start.shape
    nx = lax.axis_size("bx")
    ny = lax.axis_size("by")
    full_x = rows_x * nx
    full_y = rows_y * ny
    middle = (psf_x.shape[1] - 1) // 2
    h = middle
    ix = lax.axis_index("bx")
    iy = lax.axis_index("by")

    padded_start = halo_rows_cols(start, 2 * h)

    taps_x = psf_x / jnp.sum(psf_x, axis=1, keepdims=True)
    taps_y = psf_y / jnp.sum(psf_y, axis=1, keepdims=True)
    taps_z = psf_z / jnp.sum(psf_z, axis=1, keepdims=True)
    fwd_x = band_rows(taps_x, rows_x + 2 * h)
    fwd_y = band_rows(taps_y, rows_y + 2 * h)
    fwd_z = depth_band(taps_z, depth)
    adj_x = band_rows(taps_x[:, ::-1], rows_x)
    adj_y = band_rows(taps_y[:, ::-1], rows_y)
    adj_z = jnp.swapaxes(fwd_z, 1, 2)

    base_x = ix * rows_x - h + jnp.arange(rows_x + 2 * h, dtype=jnp.int32)
    base_y = iy * rows_y - h + jnp.arange(rows_y + 2 * h, dtype=jnp.int32)
    inside_x = (base_x >= 0) & (base_x < full_x)
    inside_y = (base_y >= 0) & (base_y < full_y)
    inside = inside_x[:, None] & inside_y[None, :]

    cover_x = (
        (base_x[None, :] + offsets[:, 0:1] >= 0) & (base_x[None, :] + offsets[:, 0:1] < full_x)
    ) & inside_x[None, :]
    cover_y = (
        (base_y[None, :] + offsets[:, 1:2] >= 0) & (base_y[None, :] + offsets[:, 1:2] < full_y)
    ) & inside_y[None, :]
    weight_x = jnp.einsum("vij,vj->vi", adj_x, cover_x.astype(jnp.float32), precision=HIGHEST)
    weight_y = jnp.einsum("vij,vj->vi", adj_y, cover_y.astype(jnp.float32), precision=HIGHEST)
    weight_z = jnp.sum(adj_z, axis=1)
    weight = jnp.sum(
        weight_x[:, :, None, None] * weight_y[:, None, :, None] * weight_z[:, None, None, :], axis=0
    )

    pad_y = SHIFT + h
    vpad = jnp.pad(views, ((0, 0), (0, 0), (pad_y, pad_y), (0, 0)))
    cols = full_y + 2 * h
    shifted = jnp.stack(
        [
            lax.dynamic_slice_in_dim(vpad[w], SHIFT + offsets[w, 1], cols, axis=1)
            for w in range(V)
        ]
    )
    chunks = jnp.concatenate(
        [shifted[:, :, k * rows_y : k * rows_y + rows_y + 2 * h] for k in range(ny)], axis=2
    )
    routed = lax.all_to_all(chunks, "by", split_axis=2, concat_axis=1, tiled=True)
    padded_start, weight, routed = lax.optimization_barrier((padded_start, weight, routed))

    reach = SHIFT + h
    prev_rows = (reach, h, reach, 0)
    next_rows = (0, reach, h, reach)
    prev_send = jnp.concatenate(
        [routed[w, rows_x - prev_rows[w] :] for w in range(V) if prev_rows[w]], axis=0
    )
    next_send = jnp.concatenate(
        [routed[w, : next_rows[w]] for w in range(V) if next_rows[w]], axis=0
    )
    prev_got = lax.ppermute(prev_send, "bx", shift_pairs(nx, 1))
    next_got = lax.ppermute(next_send, "bx", shift_pairs(nx, -1))
    blurred = blur_views(padded_start, taps_x, taps_y, fwd_z, V)
    blurred, prev_got, next_got = lax.optimization_barrier((blurred, prev_got, next_got))

    registered = []
    at_prev = 0
    at_next = 0
    for w in range(V):
        parts = []
        if prev_rows[w]:
            parts.append(prev_got[at_prev : at_prev + prev_rows[w]])
            at_prev += prev_rows[w]
        parts.append(routed[w])
        if next_rows[w]:
            parts.append(next_got[at_next : at_next + next_rows[w]])
            at_next += next_rows[w]
        ext = jnp.concatenate(parts, axis=0)
        moved = lax.dynamic_slice_in_dim(
            ext, prev_rows[w] - h + offsets[w, 0], rows_x + 2 * h, axis=0
        )
        registered.append(jnp.where(inside[:, :, None], moved.astype(jnp.float32), 0.0))
    registered = jnp.stack(registered)

    estimate = start
    for sweep in range(ITERS):
        if sweep == 0:
            source = blurred
        else:
            source = halo_rows_cols(estimate, 2 * h)
        estimate = rl_step(source, registered, estimate, weight, taps_x, taps_y, background,
                           fwd_z, adj_z, sweep == 0)
    return estimate


def solution(mesh):
    return jax.shard_map(
        local,
        mesh=mesh,
        in_specs=(P(None, ("bx", "by"), None, None), P(), P(), P(), P(), P(), P("bx", "by", None)),
        out_specs=P("bx", "by", None),
        check_vma=False,
    )
```

```python
import functools

import jax
import jax.numpy as jnp
from jax import lax
from jax.sharding import PartitionSpec as P
from jax.experimental import pallas as pl
from jax.experimental.pallas import tpu as pltpu

V = 4
SHIFT = 16
ITERS = 2
HIGHEST = lax.Precision.HIGHEST
MATMUL = lax.Precision.HIGH
DEEP = 36


def shift_pairs(count, step):
    if step > 0:
        return [(i, i + step) for i in range(count - step)]
    return [(i - step, i) for i in range(count + step)]


def halo_2d(block, width):
    nx = lax.axis_size("bx")
    ny = lax.axis_size("by")
    low = block.astype(jnp.bfloat16)
    w = width
    up = lax.ppermute(low[-w:], "bx", shift_pairs(nx, 1))
    down = lax.ppermute(low[:w], "bx", shift_pairs(nx, -1))
    left = lax.ppermute(low[:, -w:], "by", shift_pairs(ny, 1))
    right = lax.ppermute(low[:, :w], "by", shift_pairs(ny, -1))

    def corner(part, dx, dy):
        pairs = []
        for i in range(nx):
            for j in range(ny):
                ti, tj = i + dx, j + dy
                if 0 <= ti < nx and 0 <= tj < ny:
                    pairs.append((i * ny + j, ti * ny + tj))
        return lax.ppermute(part, ("bx", "by"), pairs)

    up_left = corner(low[-w:, -w:], 1, 1)
    up_right = corner(low[-w:, :w], 1, -1)
    down_left = corner(low[:w, -w:], -1, 1)
    down_right = corner(low[:w, :w], -1, -1)
    f = block.dtype
    top = jnp.concatenate([up_left, up, up_right], axis=1).astype(f)
    mid = jnp.concatenate([left.astype(f), block, right.astype(f)], axis=1)
    bottom = jnp.concatenate([down_left, down, down_right], axis=1).astype(f)
    return jnp.concatenate([top, mid, bottom], axis=0)


def halo_rows_cols(block, width):
    nx = lax.axis_size("bx")
    ny = lax.axis_size("by")
    w = width
    f = block.dtype
    low = block.astype(jnp.bfloat16)
    up = lax.ppermute(low[-w:], "bx", shift_pairs(nx, 1))
    down = lax.ppermute(low[:w], "bx", shift_pairs(nx, -1))
    tall = jnp.concatenate([up, low, down], axis=0)
    left = lax.ppermute(tall[:, -w:], "by", shift_pairs(ny, 1))
    right = lax.ppermute(tall[:, :w], "by", shift_pairs(ny, -1))
    middle = jnp.concatenate([up.astype(f), block, down.astype(f)], axis=0)
    return jnp.concatenate([left.astype(f), middle, right.astype(f)], axis=1)


def band_rows(taps, extent):
    length = taps.shape[1]
    distance = jnp.arange(extent + length - 1)[None, :] - jnp.arange(extent)[:, None]
    picked = distance[:, :, None] == jnp.arange(length)[None, None, :]
    return jnp.sum(jnp.where(picked[None], taps[:, None, None, :], 0.0), axis=3)


def depth_band(taps, extent):
    length = taps.shape[1]
    middle = (length - 1) // 2
    distance = jnp.arange(extent)[:, None] - jnp.arange(extent)[None, :] + middle
    picked = distance[:, :, None] == jnp.arange(length)[None, None, :]
    return jnp.sum(jnp.where(picked[None], taps[:, None, None, :], 0.0), axis=3)


def conv_xy(src_ref, t_ref, dst_ref, tx_ref, ty_ref, v, flip, count, chunk, taps, cols_out,
            finish=None):
    def tap(ref, k):
        return ref[v, taps - 1 - k] if flip else ref[v, k]

    def rows(c, carry):
        r0 = pl.multiple_of(c * chunk, chunk)
        acc = tap(tx_ref, 0) * src_ref[pl.ds(r0, chunk)]
        for a in range(1, taps):
            acc = acc + tap(tx_ref, a) * src_ref[pl.ds(r0 + a, chunk)]
        t_ref[...] = acc
        acc2 = tap(ty_ref, 0) * t_ref[:, pl.ds(0, cols_out), :]
        for b in range(1, taps):
            acc2 = acc2 + tap(ty_ref, b) * t_ref[:, pl.ds(b, cols_out), :]
        if finish is None:
            dst_ref[pl.ds(r0, chunk)] = acc2
        else:
            finish(pl.ds(r0, chunk), acc2)
        return carry

    lax.fori_loop(0, count // chunk, rows, 0, unroll=2)


def blur_views(field, taps_x, taps_y, fwd_z, views):
    rows_f, cols_f, depth = field.shape
    taps = taps_x.shape[1]
    rows_r = rows_f - (taps - 1)
    cols_r = cols_f - (taps - 1)
    chunk = 2
    deep = DEEP
    f32 = jnp.float32

    def kernel(tx_ref, ty_ref, field_ref, fz_ref, out_ref, q_ref, t1_ref):
        v = pl.program_id(0)
        conv_xy(field_ref, t1_ref, q_ref, tx_ref, ty_ref, v, False, rows_r, chunk, taps, cols_r)

        def depth_rows(c, carry):
            r0 = pl.multiple_of(c * deep, deep)
            flat = q_ref[pl.ds(r0, deep)].reshape(deep * cols_r, depth)
            blurred = jnp.dot(flat, fz_ref[0], precision=MATMUL, preferred_element_type=f32)
            out_ref[0, pl.ds(r0, deep)] = blurred.reshape(deep, cols_r, depth)
            return carry

        lax.fori_loop(0, rows_r // deep, depth_rows, 0)

    smem = pl.BlockSpec(memory_space=pltpu.SMEM)
    return pl.pallas_call(
        kernel,
        grid=(views,),
        in_specs=[
            smem,
            smem,
            pl.BlockSpec(field.shape, lambda v: (0, 0, 0)),
            pl.BlockSpec((1, depth, depth), lambda v: (v, 0, 0)),
        ],
        out_specs=pl.BlockSpec((1, rows_r, cols_r, depth), lambda v: (v, 0, 0, 0)),
        out_shape=jax.ShapeDtypeStruct((views, rows_r, cols_r, depth), f32),
        scratch_shapes=[
            pltpu.VMEM((rows_r, cols_r, depth), f32),
            pltpu.VMEM((chunk, cols_f, depth), f32),
        ],
        compiler_params=pltpu.CompilerParams(dimension_semantics=("arbitrary",)),
    )(taps_x, taps_y, field, fwd_z)


def rl_step(source, registered, estimate, weight, taps_x, taps_y, bg, fwd_z, adj_z, given):
    views = len(registered)
    rows_r, cols_r, depth = registered[0].shape
    rows, cols = estimate.shape[:2]
    taps = taps_x.shape[1]
    cols_f = cols_r + taps - 1
    chunk = 2
    deep = DEEP
    f32 = jnp.float32

    def kernel(tx_ref, ty_ref, bg_ref, src_ref, *refs):
        reg_refs = refs[:views]
        est_ref, w_ref, fz_ref, az_ref, out_ref, q_ref, t1_ref, t2_ref, s_ref = refs[views:]
        v = pl.program_id(0)
        if not given:
            conv_xy(src_ref, t1_ref, q_ref, tx_ref, ty_ref, v, False, rows_r, chunk, taps, cols_r)

        def depth_rows(reg_ref, c, carry):
            r0 = pl.multiple_of(c * deep, deep)
            if given:
                blurred = src_ref[0, pl.ds(r0, deep)].reshape(deep * cols_r, depth)
            else:
                flat = q_ref[pl.ds(r0, deep)].reshape(deep * cols_r, depth)
                blurred = jnp.dot(flat, fz_ref[0], precision=MATMUL, preferred_element_type=f32)
            reg = reg_ref[pl.ds(r0, deep)].astype(f32).reshape(deep * cols_r, depth)
            ratio = reg / (blurred + bg_ref[v])
            back = jnp.dot(ratio, az_ref[0], precision=MATMUL, preferred_element_type=f32)
            q_ref[pl.ds(r0, deep)] = back.reshape(deep, cols_r, depth)
            return carry

        for w in range(views):
            @pl.when(v == w)
            def _():
                lax.fori_loop(0, rows_r // deep, functools.partial(depth_rows, reg_refs[w]), 0)

        def finish(rs, acc2):
            @pl.when(v == 0)
            def _():
                s_ref[rs] = acc2

            @pl.when((v > 0) & (v < views - 1))
            def _():
                s_ref[rs] = s_ref[rs] + acc2

            @pl.when(v == views - 1)
            def _():
                out_ref[rs] = est_ref[rs] * (s_ref[rs] + acc2) / w_ref[rs]

        conv_xy(q_ref, t2_ref, None, tx_ref, ty_ref, v, True, rows, chunk, taps, cols, finish)

    smem = pl.BlockSpec(memory_space=pltpu.SMEM)
    whole3 = lambda shape: pl.BlockSpec(shape, lambda v: (0, 0, 0))
    per_view = pl.BlockSpec((1, rows_r, cols_r, depth), lambda v: (v, 0, 0, 0))
    return pl.pallas_call(
        kernel,
        grid=(views,),
        in_specs=[
            smem,
            smem,
            smem,
            per_view if given else whole3(source.shape),
            *[whole3(r.shape) for r in registered],
            whole3(estimate.shape),
            whole3(weight.shape),
            pl.BlockSpec((1, depth, depth), lambda v: (v, 0, 0)),
            pl.BlockSpec((1, depth, depth), lambda v: (v, 0, 0)),
        ],
        out_specs=whole3(estimate.shape),
        out_shape=jax.ShapeDtypeStruct(estimate.shape, f32),
        scratch_shapes=[
            pltpu.VMEM((rows_r, cols_r, depth), f32),
            pltpu.VMEM((chunk, cols_f, depth), f32),
            pltpu.VMEM((chunk, cols_r, depth), f32),
            pltpu.VMEM((rows, cols, depth), f32),
        ],
        compiler_params=pltpu.CompilerParams(dimension_semantics=("arbitrary",)),
    )(taps_x, taps_y, bg, source, *registered, estimate, weight, fwd_z, adj_z)


def local(views, offsets, background, psf_x, psf_y, psf_z, start):
    rows_x, rows_y, depth = start.shape
    nx = lax.axis_size("bx")
    ny = lax.axis_size("by")
    full_x = rows_x * nx
    full_y = rows_y * ny
    middle = (psf_x.shape[1] - 1) // 2
    h = middle
    ix = lax.axis_index("bx")
    iy = lax.axis_index("by")

    padded_start = halo_rows_cols(start, 2 * h)

    taps_x = psf_x / jnp.sum(psf_x, axis=1, keepdims=True)
    taps_y = psf_y / jnp.sum(psf_y, axis=1, keepdims=True)
    taps_z = psf_z / jnp.sum(psf_z, axis=1, keepdims=True)
    fwd_x = band_rows(taps_x, rows_x + 2 * h)
    fwd_y = band_rows(taps_y, rows_y + 2 * h)
    fwd_z = depth_band(taps_z, depth)
    adj_x = band_rows(taps_x[:, ::-1], rows_x)
    adj_y = band_rows(taps_y[:, ::-1], rows_y)
    adj_z = jnp.swapaxes(fwd_z, 1, 2)

    base_x = ix * rows_x - h + jnp.arange(rows_x + 2 * h, dtype=jnp.int32)
    base_y = iy * rows_y - h + jnp.arange(rows_y + 2 * h, dtype=jnp.int32)
    inside_x = (base_x >= 0) & (base_x < full_x)
    inside_y = (base_y >= 0) & (base_y < full_y)
    inside = inside_x[:, None] & inside_y[None, :]

    cover_x = (
        (base_x[None, :] + offsets[:, 0:1] >= 0) & (base_x[None, :] + offsets[:, 0:1] < full_x)
    ) & inside_x[None, :]
    cover_y = (
        (base_y[None, :] + offsets[:, 1:2] >= 0) & (base_y[None, :] + offsets[:, 1:2] < full_y)
    ) & inside_y[None, :]
    weight_x = jnp.einsum("vij,vj->vi", adj_x, cover_x.astype(jnp.float32), precision=HIGHEST)
    weight_y = jnp.einsum("vij,vj->vi", adj_y, cover_y.astype(jnp.float32), precision=HIGHEST)
    weight_z = jnp.sum(adj_z, axis=1)
    weight = jnp.sum(
        weight_x[:, :, None, None] * weight_y[:, None, :, None] * weight_z[:, None, None, :], axis=0
    )

    pad_y = SHIFT + h
    vpad = jnp.pad(views, ((0, 0), (0, 0), (pad_y, pad_y), (0, 0)))
    cols = full_y + 2 * h
    shifted = jnp.stack(
        [
            lax.dynamic_slice_in_dim(vpad[w], SHIFT + offsets[w, 1], cols, axis=1)
            for w in range(V)
        ]
    )
    chunks = jnp.concatenate(
        [shifted[:, :, k * rows_y : k * rows_y + rows_y + 2 * h] for k in range(ny)], axis=2
    )
    routed = lax.all_to_all(chunks, "by", split_axis=2, concat_axis=1, tiled=True)
    padded_start, weight, routed = lax.optimization_barrier((padded_start, weight, routed))

    reach = SHIFT + h
    prev_rows = (reach, h, reach, 0)
    next_rows = (0, reach, h, reach)
    prev_send = jnp.concatenate(
        [routed[w, rows_x - prev_rows[w] :] for w in range(V) if prev_rows[w]], axis=0
    )
    next_send = jnp.concatenate(
        [routed[w, : next_rows[w]] for w in range(V) if next_rows[w]], axis=0
    )
    prev_got = lax.ppermute(prev_send, "bx", shift_pairs(nx, 1))
    next_got = lax.ppermute(next_send, "bx", shift_pairs(nx, -1))
    blurred = blur_views(padded_start, taps_x, taps_y, fwd_z, V)
    blurred, prev_got, next_got = lax.optimization_barrier((blurred, prev_got, next_got))

    registered = []
    at_prev = 0
    at_next = 0
    for w in range(V):
        parts = []
        if prev_rows[w]:
            parts.append(prev_got[at_prev : at_prev + prev_rows[w]])
            at_prev += prev_rows[w]
        parts.append(routed[w])
        if next_rows[w]:
            parts.append(next_got[at_next : at_next + next_rows[w]])
            at_next += next_rows[w]
        ext = jnp.concatenate(parts, axis=0)
        moved = lax.dynamic_slice_in_dim(
            ext, prev_rows[w] - h + offsets[w, 0], rows_x + 2 * h, axis=0
        )
        registered.append(jnp.where(inside[:, :, None], moved.astype(jnp.float32), 0.0))

    estimate = start
    for sweep in range(ITERS):
        if sweep == 0:
            source = blurred
        else:
            source = halo_rows_cols(estimate, 2 * h)
        estimate = rl_step(source, registered, estimate, weight, taps_x, taps_y, background,
                           fwd_z, adj_z, sweep == 0)
    return estimate


def solution(mesh):
    return jax.shard_map(
        local,
        mesh=mesh,
        in_specs=(P(None, ("bx", "by"), None, None), P(), P(), P(), P(), P(), P("bx", "by", None)),
        out_specs=P("bx", "by", None),
        check_vma=False,
    )
```

```python
import jax
import jax.numpy as jnp
from jax import lax
from jax.sharding import PartitionSpec as P
from jax.experimental import pallas as pl
from jax.experimental.pallas import tpu as pltpu

V = 4
SHIFT = 16
ITERS = 2
HIGHEST = lax.Precision.HIGHEST
MATMUL = lax.Precision.HIGH
DEEP = 72


def shift_pairs(count, step):
    if step > 0:
        return [(i, i + step) for i in range(count - step)]
    return [(i - step, i) for i in range(count + step)]


def halo_2d(block, width):
    nx = lax.axis_size("bx")
    ny = lax.axis_size("by")
    low = block.astype(jnp.bfloat16)
    w = width
    up = lax.ppermute(low[-w:], "bx", shift_pairs(nx, 1))
    down = lax.ppermute(low[:w], "bx", shift_pairs(nx, -1))
    left = lax.ppermute(low[:, -w:], "by", shift_pairs(ny, 1))
    right = lax.ppermute(low[:, :w], "by", shift_pairs(ny, -1))

    def corner(part, dx, dy):
        pairs = []
        for i in range(nx):
            for j in range(ny):
                ti, tj = i + dx, j + dy
                if 0 <= ti < nx and 0 <= tj < ny:
                    pairs.append((i * ny + j, ti * ny + tj))
        return lax.ppermute(part, ("bx", "by"), pairs)

    up_left = corner(low[-w:, -w:], 1, 1)
    up_right = corner(low[-w:, :w], 1, -1)
    down_left = corner(low[:w, -w:], -1, 1)
    down_right = corner(low[:w, :w], -1, -1)
    f = block.dtype
    top = jnp.concatenate([up_left, up, up_right], axis=1).astype(f)
    mid = jnp.concatenate([left.astype(f), block, right.astype(f)], axis=1)
    bottom = jnp.concatenate([down_left, down, down_right], axis=1).astype(f)
    return jnp.concatenate([top, mid, bottom], axis=0)


def halo_rows_cols(block, width):
    nx = lax.axis_size("bx")
    ny = lax.axis_size("by")
    w = width
    f = block.dtype
    low = block.astype(jnp.bfloat16)
    up = lax.ppermute(low[-w:], "bx", shift_pairs(nx, 1))
    down = lax.ppermute(low[:w], "bx", shift_pairs(nx, -1))
    tall = jnp.concatenate([up, low, down], axis=0)
    left = lax.ppermute(tall[:, -w:], "by", shift_pairs(ny, 1))
    right = lax.ppermute(tall[:, :w], "by", shift_pairs(ny, -1))
    middle = jnp.concatenate([up.astype(f), block, down.astype(f)], axis=0)
    return jnp.concatenate([left.astype(f), middle, right.astype(f)], axis=1)


def band_rows(taps, extent):
    length = taps.shape[1]
    distance = jnp.arange(extent + length - 1)[None, :] - jnp.arange(extent)[:, None]
    picked = distance[:, :, None] == jnp.arange(length)[None, None, :]
    return jnp.sum(jnp.where(picked[None], taps[:, None, None, :], 0.0), axis=3)


def depth_band(taps, extent):
    length = taps.shape[1]
    middle = (length - 1) // 2
    distance = jnp.arange(extent)[:, None] - jnp.arange(extent)[None, :] + middle
    picked = distance[:, :, None] == jnp.arange(length)[None, None, :]
    return jnp.sum(jnp.where(picked[None], taps[:, None, None, :], 0.0), axis=3)


def conv_xy(src_ref, t_ref, dst_ref, tx_ref, ty_ref, v, flip, count, chunk, taps, cols_out,
            finish=None):
    def tap(ref, k):
        return ref[v, taps - 1 - k] if flip else ref[v, k]

    def rows(c, carry):
        r0 = pl.multiple_of(c * chunk, chunk)
        acc = tap(tx_ref, 0) * src_ref[pl.ds(r0, chunk)]
        for a in range(1, taps):
            acc = acc + tap(tx_ref, a) * src_ref[pl.ds(r0 + a, chunk)]
        t_ref[...] = acc
        acc2 = tap(ty_ref, 0) * t_ref[:, pl.ds(0, cols_out), :]
        for b in range(1, taps):
            acc2 = acc2 + tap(ty_ref, b) * t_ref[:, pl.ds(b, cols_out), :]
        if finish is None:
            dst_ref[pl.ds(r0, chunk)] = acc2
        else:
            finish(pl.ds(r0, chunk), acc2)
        return carry

    lax.fori_loop(0, count // chunk, rows, 0, unroll=4)


def blur_views(field, taps_x, taps_y, fwd_z, views):
    rows_f, cols_f, depth = field.shape
    taps = taps_x.shape[1]
    rows_r = rows_f - (taps - 1)
    cols_r = cols_f - (taps - 1)
    chunk = 2
    deep = DEEP
    f32 = jnp.float32

    def kernel(tx_ref, ty_ref, field_ref, fz_ref, out_ref, q_ref, t1_ref):
        v = pl.program_id(0)
        conv_xy(field_ref, t1_ref, q_ref, tx_ref, ty_ref, v, False, rows_r, chunk, taps, cols_r)

        def depth_rows(c, carry):
            r0 = pl.multiple_of(c * deep, deep)
            flat = q_ref[pl.ds(r0, deep)].reshape(deep * cols_r, depth)
            blurred = jnp.dot(flat, fz_ref[0], precision=MATMUL, preferred_element_type=f32)
            out_ref[0, pl.ds(r0, deep)] = blurred.reshape(deep, cols_r, depth)
            return carry

        lax.fori_loop(0, rows_r // deep, depth_rows, 0)

    smem = pl.BlockSpec(memory_space=pltpu.SMEM)
    return pl.pallas_call(
        kernel,
        grid=(views,),
        in_specs=[
            smem,
            smem,
            pl.BlockSpec(field.shape, lambda v: (0, 0, 0)),
            pl.BlockSpec((1, depth, depth), lambda v: (v, 0, 0)),
        ],
        out_specs=pl.BlockSpec((1, rows_r, cols_r, depth), lambda v: (v, 0, 0, 0)),
        out_shape=jax.ShapeDtypeStruct((views, rows_r, cols_r, depth), f32),
        scratch_shapes=[
            pltpu.VMEM((rows_r, cols_r, depth), f32),
            pltpu.VMEM((chunk, cols_f, depth), f32),
        ],
        compiler_params=pltpu.CompilerParams(dimension_semantics=("arbitrary",)),
    )(taps_x, taps_y, field, fwd_z)


def rl_step(source, registered, estimate, weight, taps_x, taps_y, bg, fwd_z, adj_z, given):
    views, rows_r, cols_r, depth = registered.shape
    rows, cols = estimate.shape[:2]
    taps = taps_x.shape[1]
    cols_f = cols_r + taps - 1
    chunk = 2
    deep = DEEP
    f32 = jnp.float32

    def kernel(tx_ref, ty_ref, bg_ref, src_ref, reg_ref, est_ref, w_ref, fz_ref, az_ref,
               out_ref, q_ref, t1_ref, t2_ref, s_ref):
        v = pl.program_id(0)
        if not given:
            conv_xy(src_ref, t1_ref, q_ref, tx_ref, ty_ref, v, False, rows_r, chunk, taps, cols_r)

        def depth_rows(c, carry):
            r0 = pl.multiple_of(c * deep, deep)
            if given:
                blurred = src_ref[0, pl.ds(r0, deep)].reshape(deep * cols_r, depth)
            else:
                flat = q_ref[pl.ds(r0, deep)].reshape(deep * cols_r, depth)
                blurred = jnp.dot(flat, fz_ref[0], precision=MATMUL, preferred_element_type=f32)
            reg = reg_ref[0, pl.ds(r0, deep)].astype(f32).reshape(deep * cols_r, depth)
            ratio = reg / (blurred + bg_ref[v])
            back = jnp.dot(ratio, az_ref[0], precision=MATMUL, preferred_element_type=f32)
            q_ref[pl.ds(r0, deep)] = back.reshape(deep, cols_r, depth)
            return carry

        lax.fori_loop(0, rows_r // deep, depth_rows, 0)

        def finish(rs, acc2):
            @pl.when(v == 0)
            def _():
                s_ref[rs] = acc2

            @pl.when((v > 0) & (v < views - 1))
            def _():
                s_ref[rs] = s_ref[rs] + acc2

            @pl.when(v == views - 1)
            def _():
                out_ref[rs] = est_ref[rs] * (s_ref[rs] + acc2) / w_ref[rs]

        conv_xy(q_ref, t2_ref, None, tx_ref, ty_ref, v, True, rows, chunk, taps, cols, finish)

    smem = pl.BlockSpec(memory_space=pltpu.SMEM)
    whole3 = lambda shape: pl.BlockSpec(shape, lambda v: (0, 0, 0))
    per_view = pl.BlockSpec((1, rows_r, cols_r, depth), lambda v: (v, 0, 0, 0))
    return pl.pallas_call(
        kernel,
        grid=(views,),
        in_specs=[
            smem,
            smem,
            smem,
            per_view if given else whole3(source.shape),
            per_view,
            whole3(estimate.shape),
            whole3(weight.shape),
            pl.BlockSpec((1, depth, depth), lambda v: (v, 0, 0)),
            pl.BlockSpec((1, depth, depth), lambda v: (v, 0, 0)),
        ],
        out_specs=whole3(estimate.shape),
        out_shape=jax.ShapeDtypeStruct(estimate.shape, f32),
        scratch_shapes=[
            pltpu.VMEM((rows_r, cols_r, depth), f32),
            pltpu.VMEM((chunk, cols_f, depth), f32),
            pltpu.VMEM((chunk, cols_r, depth), f32),
            pltpu.VMEM((rows, cols, depth), f32),
        ],
        compiler_params=pltpu.CompilerParams(dimension_semantics=("arbitrary",)),
    )(taps_x, taps_y, bg, source, registered, estimate, weight, fwd_z, adj_z)


def local(views, offsets, background, psf_x, psf_y, psf_z, start):
    rows_x, rows_y, depth = start.shape
    nx = lax.axis_size("bx")
    ny = lax.axis_size("by")
    full_x = rows_x * nx
    full_y = rows_y * ny
    middle = (psf_x.shape[1] - 1) // 2
    h = middle
    ix = lax.axis_index("bx")
    iy = lax.axis_index("by")

    padded_start = halo_rows_cols(start, 2 * h)

    taps_x = psf_x / jnp.sum(psf_x, axis=1, keepdims=True)
    taps_y = psf_y / jnp.sum(psf_y, axis=1, keepdims=True)
    taps_z = psf_z / jnp.sum(psf_z, axis=1, keepdims=True)
    fwd_x = band_rows(taps_x, rows_x + 2 * h)
    fwd_y = band_rows(taps_y, rows_y + 2 * h)
    fwd_z = depth_band(taps_z, depth)
    adj_x = band_rows(taps_x[:, ::-1], rows_x)
    adj_y = band_rows(taps_y[:, ::-1], rows_y)
    adj_z = jnp.swapaxes(fwd_z, 1, 2)

    base_x = ix * rows_x - h + jnp.arange(rows_x + 2 * h, dtype=jnp.int32)
    base_y = iy * rows_y - h + jnp.arange(rows_y + 2 * h, dtype=jnp.int32)
    inside_x = (base_x >= 0) & (base_x < full_x)
    inside_y = (base_y >= 0) & (base_y < full_y)
    inside = inside_x[:, None] & inside_y[None, :]

    cover_x = (
        (base_x[None, :] + offsets[:, 0:1] >= 0) & (base_x[None, :] + offsets[:, 0:1] < full_x)
    ) & inside_x[None, :]
    cover_y = (
        (base_y[None, :] + offsets[:, 1:2] >= 0) & (base_y[None, :] + offsets[:, 1:2] < full_y)
    ) & inside_y[None, :]
    weight_x = jnp.einsum("vij,vj->vi", adj_x, cover_x.astype(jnp.float32), precision=HIGHEST)
    weight_y = jnp.einsum("vij,vj->vi", adj_y, cover_y.astype(jnp.float32), precision=HIGHEST)
    weight_z = jnp.sum(adj_z, axis=1)
    weight = jnp.sum(
        weight_x[:, :, None, None] * weight_y[:, None, :, None] * weight_z[:, None, None, :], axis=0
    )

    pad_y = SHIFT + h
    vpad = jnp.pad(views, ((0, 0), (0, 0), (pad_y, pad_y), (0, 0)))
    cols = full_y + 2 * h
    shifted = jnp.stack(
        [
            lax.dynamic_slice_in_dim(vpad[w], SHIFT + offsets[w, 1], cols, axis=1)
            for w in range(V)
        ]
    )
    chunks = jnp.concatenate(
        [shifted[:, :, k * rows_y : k * rows_y + rows_y + 2 * h] for k in range(ny)], axis=2
    )
    routed = lax.all_to_all(chunks, "by", split_axis=2, concat_axis=1, tiled=True)
    padded_start, weight, routed = lax.optimization_barrier((padded_start, weight, routed))

    reach = SHIFT + h
    prev_rows = (reach, h, reach, 0)
    next_rows = (0, reach, h, reach)
    prev_send = jnp.concatenate(
        [routed[w, rows_x - prev_rows[w] :] for w in range(V) if prev_rows[w]], axis=0
    )
    next_send = jnp.concatenate(
        [routed[w, : next_rows[w]] for w in range(V) if next_rows[w]], axis=0
    )
    prev_got = lax.ppermute(prev_send, "bx", shift_pairs(nx, 1))
    next_got = lax.ppermute(next_send, "bx", shift_pairs(nx, -1))
    blurred = blur_views(padded_start, taps_x, taps_y, fwd_z, V)
    blurred, prev_got, next_got = lax.optimization_barrier((blurred, prev_got, next_got))

    registered = []
    at_prev = 0
    at_next = 0
    for w in range(V):
        parts = []
        if prev_rows[w]:
            parts.append(prev_got[at_prev : at_prev + prev_rows[w]])
            at_prev += prev_rows[w]
        parts.append(routed[w])
        if next_rows[w]:
            parts.append(next_got[at_next : at_next + next_rows[w]])
            at_next += next_rows[w]
        ext = jnp.concatenate(parts, axis=0)
        moved = lax.dynamic_slice_in_dim(
            ext, prev_rows[w] - h + offsets[w, 0], rows_x + 2 * h, axis=0
        )
        registered.append(jnp.where(inside[:, :, None], moved.astype(jnp.float32), 0.0))
    registered = jnp.stack(registered)

    estimate = start
    for sweep in range(ITERS):
        if sweep == 0:
            source = blurred
        else:
            source = halo_rows_cols(estimate, 2 * h)
        estimate = rl_step(source, registered, estimate, weight, taps_x, taps_y, background,
                           fwd_z, adj_z, sweep == 0)
    return estimate


def solution(mesh):
    return jax.shard_map(
        local,
        mesh=mesh,
        in_specs=(P(None, ("bx", "by"), None, None), P(), P(), P(), P(), P(), P("bx", "by", None)),
        out_specs=P("bx", "by", None),
        check_vma=False,
    )
```

```python
import jax
import jax.numpy as jnp
from jax import lax
from jax.sharding import PartitionSpec as P
from jax.experimental import pallas as pl
from jax.experimental.pallas import tpu as pltpu

V = 4
SHIFT = 16
ITERS = 2
HIGHEST = lax.Precision.HIGHEST
MATMUL = lax.Precision.HIGH
DEEP = 72


def shift_pairs(count, step):
    if step > 0:
        return [(i, i + step) for i in range(count - step)]
    return [(i - step, i) for i in range(count + step)]


def halo_2d(block, width):
    nx = lax.axis_size("bx")
    ny = lax.axis_size("by")
    low = block.astype(jnp.bfloat16)
    w = width
    up = lax.ppermute(low[-w:], "bx", shift_pairs(nx, 1))
    down = lax.ppermute(low[:w], "bx", shift_pairs(nx, -1))
    left = lax.ppermute(low[:, -w:], "by", shift_pairs(ny, 1))
    right = lax.ppermute(low[:, :w], "by", shift_pairs(ny, -1))

    def corner(part, dx, dy):
        pairs = []
        for i in range(nx):
            for j in range(ny):
                ti, tj = i + dx, j + dy
                if 0 <= ti < nx and 0 <= tj < ny:
                    pairs.append((i * ny + j, ti * ny + tj))
        return lax.ppermute(part, ("bx", "by"), pairs)

    up_left = corner(low[-w:, -w:], 1, 1)
    up_right = corner(low[-w:, :w], 1, -1)
    down_left = corner(low[:w, -w:], -1, 1)
    down_right = corner(low[:w, :w], -1, -1)
    f = block.dtype
    top = jnp.concatenate([up_left, up, up_right], axis=1).astype(f)
    mid = jnp.concatenate([left.astype(f), block, right.astype(f)], axis=1)
    bottom = jnp.concatenate([down_left, down, down_right], axis=1).astype(f)
    return jnp.concatenate([top, mid, bottom], axis=0)


def halo_rows_cols(block, width):
    nx = lax.axis_size("bx")
    ny = lax.axis_size("by")
    w = width
    f = block.dtype
    low = block.astype(jnp.bfloat16)
    up = lax.ppermute(low[-w:], "bx", shift_pairs(nx, 1))
    down = lax.ppermute(low[:w], "bx", shift_pairs(nx, -1))
    tall = jnp.concatenate([up, low, down], axis=0)
    left = lax.ppermute(tall[:, -w:], "by", shift_pairs(ny, 1))
    right = lax.ppermute(tall[:, :w], "by", shift_pairs(ny, -1))
    middle = jnp.concatenate([up.astype(f), block, down.astype(f)], axis=0)
    return jnp.concatenate([left.astype(f), middle, right.astype(f)], axis=1)


def band_rows(taps, extent):
    length = taps.shape[1]
    distance = jnp.arange(extent + length - 1)[None, :] - jnp.arange(extent)[:, None]
    picked = distance[:, :, None] == jnp.arange(length)[None, None, :]
    return jnp.sum(jnp.where(picked[None], taps[:, None, None, :], 0.0), axis=3)


def depth_band(taps, extent):
    length = taps.shape[1]
    middle = (length - 1) // 2
    distance = jnp.arange(extent)[:, None] - jnp.arange(extent)[None, :] + middle
    picked = distance[:, :, None] == jnp.arange(length)[None, None, :]
    return jnp.sum(jnp.where(picked[None], taps[:, None, None, :], 0.0), axis=3)


def conv_xy(src_ref, t_ref, dst_ref, tx_ref, ty_ref, v, flip, count, chunk, taps, cols_out,
            finish=None):
    def tap(ref, k):
        return ref[v, taps - 1 - k] if flip else ref[v, k]

    def rows(c, carry):
        r0 = pl.multiple_of(c * chunk, chunk)
        acc = tap(tx_ref, 0) * src_ref[pl.ds(r0, chunk)]
        for a in range(1, taps):
            acc = acc + tap(tx_ref, a) * src_ref[pl.ds(r0 + a, chunk)]
        t_ref[...] = acc
        acc2 = tap(ty_ref, 0) * t_ref[:, pl.ds(0, cols_out), :]
        for b in range(1, taps):
            acc2 = acc2 + tap(ty_ref, b) * t_ref[:, pl.ds(b, cols_out), :]
        if finish is None:
            dst_ref[pl.ds(r0, chunk)] = acc2
        else:
            finish(pl.ds(r0, chunk), acc2)
        return carry

    lax.fori_loop(0, count // chunk, rows, 0, unroll=4)


def blur_views(field, taps_x, taps_y, fwd_z, views):
    rows_f, cols_f, depth = field.shape
    taps = taps_x.shape[1]
    rows_r = rows_f - (taps - 1)
    cols_r = cols_f - (taps - 1)
    chunk = 2
    deep = DEEP
    f32 = jnp.float32

    def kernel(tx_ref, ty_ref, field_ref, fz_ref, out_ref, q_ref, t1_ref):
        v = pl.program_id(0)
        conv_xy(field_ref, t1_ref, q_ref, tx_ref, ty_ref, v, False, rows_r, chunk, taps, cols_r)

        def depth_rows(c, carry):
            r0 = pl.multiple_of(c * deep, deep)
            flat = q_ref[pl.ds(r0, deep)].reshape(deep * cols_r, depth)
            blurred = jnp.dot(flat, fz_ref[0], precision=MATMUL, preferred_element_type=f32)
            out_ref[0, pl.ds(r0, deep)] = blurred.reshape(deep, cols_r, depth)
            return carry

        lax.fori_loop(0, rows_r // deep, depth_rows, 0)

    smem = pl.BlockSpec(memory_space=pltpu.SMEM)
    return pl.pallas_call(
        kernel,
        grid=(views,),
        in_specs=[
            smem,
            smem,
            pl.BlockSpec(field.shape, lambda v: (0, 0, 0)),
            pl.BlockSpec((1, depth, depth), lambda v: (v, 0, 0)),
        ],
        out_specs=pl.BlockSpec((1, rows_r, cols_r, depth), lambda v: (v, 0, 0, 0)),
        out_shape=jax.ShapeDtypeStruct((views, rows_r, cols_r, depth), f32),
        scratch_shapes=[
            pltpu.VMEM((rows_r, cols_r, depth), f32),
            pltpu.VMEM((chunk, cols_f, depth), f32),
        ],
        compiler_params=pltpu.CompilerParams(dimension_semantics=("arbitrary",)),
    )(taps_x, taps_y, field, fwd_z)


def rl_step(source, registered, estimate, weight, taps_x, taps_y, bg, fwd_z, adj_z, given):
    views, rows_r, cols_r, depth = registered.shape
    rows, cols = estimate.shape[:2]
    taps = taps_x.shape[1]
    cols_f = cols_r + taps - 1
    chunk = 2
    deep = DEEP
    f32 = jnp.float32

    def kernel(tx_ref, ty_ref, bg_ref, src_ref, reg_ref, est_ref, w_ref, fz_ref, az_ref,
               out_ref, q_ref, t1_ref, t2_ref, s_ref):
        v = pl.program_id(0)
        if not given:
            conv_xy(src_ref, t1_ref, q_ref, tx_ref, ty_ref, v, False, rows_r, chunk, taps, cols_r)

        def depth_rows(c, carry):
            r0 = pl.multiple_of(c * deep, deep)
            if given:
                blurred = src_ref[0, pl.ds(r0, deep)].reshape(deep * cols_r, depth)
            else:
                flat = q_ref[pl.ds(r0, deep)].reshape(deep * cols_r, depth)
                blurred = jnp.dot(flat, fz_ref[0], precision=MATMUL, preferred_element_type=f32)
            reg = reg_ref[0, pl.ds(r0, deep)].astype(f32).reshape(deep * cols_r, depth)
            ratio = reg / (blurred + bg_ref[v])
            back = jnp.dot(ratio, az_ref[0], precision=MATMUL, preferred_element_type=f32)
            q_ref[pl.ds(r0, deep)] = back.reshape(deep, cols_r, depth)
            return carry

        lax.fori_loop(0, rows_r // deep, depth_rows, 0)

        def finish(rs, acc2):
            @pl.when(v == 0)
            def _():
                s_ref[rs] = acc2

            @pl.when((v > 0) & (v < views - 1))
            def _():
                s_ref[rs] = s_ref[rs] + acc2

            @pl.when(v == views - 1)
            def _():
                out_ref[rs] = est_ref[rs] * (s_ref[rs] + acc2) / w_ref[rs]

        conv_xy(q_ref, t2_ref, None, tx_ref, ty_ref, v, True, rows, chunk, taps, cols, finish)

    smem = pl.BlockSpec(memory_space=pltpu.SMEM)
    whole3 = lambda shape: pl.BlockSpec(shape, lambda v: (0, 0, 0))
    per_view = pl.BlockSpec((1, rows_r, cols_r, depth), lambda v: (v, 0, 0, 0))
    return pl.pallas_call(
        kernel,
        grid=(views,),
        in_specs=[
            smem,
            smem,
            smem,
            per_view if given else whole3(source.shape),
            per_view,
            whole3(estimate.shape),
            whole3(weight.shape),
            pl.BlockSpec((1, depth, depth), lambda v: (v, 0, 0)),
            pl.BlockSpec((1, depth, depth), lambda v: (v, 0, 0)),
        ],
        out_specs=whole3(estimate.shape),
        out_shape=jax.ShapeDtypeStruct(estimate.shape, f32),
        scratch_shapes=[
            pltpu.VMEM((rows_r, cols_r, depth), f32),
            pltpu.VMEM((chunk, cols_f, depth), f32),
            pltpu.VMEM((chunk, cols_r, depth), f32),
            pltpu.VMEM((rows, cols, depth), f32),
        ],
        compiler_params=pltpu.CompilerParams(dimension_semantics=("arbitrary",)),
    )(taps_x, taps_y, bg, source, registered, estimate, weight, fwd_z, adj_z)


def local(views, offsets, background, psf_x, psf_y, psf_z, start):
    rows_x, rows_y, depth = start.shape
    nx = lax.axis_size("bx")
    ny = lax.axis_size("by")
    full_x = rows_x * nx
    full_y = rows_y * ny
    middle = (psf_x.shape[1] - 1) // 2
    h = middle
    ix = lax.axis_index("bx")
    iy = lax.axis_index("by")

    padded_start = halo_rows_cols(start, 2 * h)

    taps_x = psf_x / jnp.sum(psf_x, axis=1, keepdims=True)
    taps_y = psf_y / jnp.sum(psf_y, axis=1, keepdims=True)
    taps_z = psf_z / jnp.sum(psf_z, axis=1, keepdims=True)
    fwd_x = band_rows(taps_x, rows_x + 2 * h)
    fwd_y = band_rows(taps_y, rows_y + 2 * h)
    fwd_z = depth_band(taps_z, depth)
    adj_x = band_rows(taps_x[:, ::-1], rows_x)
    adj_y = band_rows(taps_y[:, ::-1], rows_y)
    adj_z = jnp.swapaxes(fwd_z, 1, 2)

    base_x = ix * rows_x - h + jnp.arange(rows_x + 2 * h, dtype=jnp.int32)
    base_y = iy * rows_y - h + jnp.arange(rows_y + 2 * h, dtype=jnp.int32)
    inside_x = (base_x >= 0) & (base_x < full_x)
    inside_y = (base_y >= 0) & (base_y < full_y)
    inside = inside_x[:, None] & inside_y[None, :]

    cover_x = (
        (base_x[None, :] + offsets[:, 0:1] >= 0) & (base_x[None, :] + offsets[:, 0:1] < full_x)
    ) & inside_x[None, :]
    cover_y = (
        (base_y[None, :] + offsets[:, 1:2] >= 0) & (base_y[None, :] + offsets[:, 1:2] < full_y)
    ) & inside_y[None, :]
    weight_x = jnp.einsum("vij,vj->vi", adj_x, cover_x.astype(jnp.float32), precision=HIGHEST)
    weight_y = jnp.einsum("vij,vj->vi", adj_y, cover_y.astype(jnp.float32), precision=HIGHEST)
    weight_z = jnp.sum(adj_z, axis=1)
    weight = jnp.sum(
        weight_x[:, :, None, None] * weight_y[:, None, :, None] * weight_z[:, None, None, :], axis=0
    )

    pad_y = SHIFT + h
    vpad = jnp.pad(views, ((0, 0), (0, 0), (pad_y, pad_y), (0, 0)))
    cols = full_y + 2 * h
    shifted = jnp.stack(
        [
            lax.dynamic_slice_in_dim(vpad[w], SHIFT + offsets[w, 1], cols, axis=1)
            for w in range(V)
        ]
    )
    chunks = jnp.stack(
        [shifted[:, :, k * rows_y : k * rows_y + rows_y + 2 * h] for k in range(ny)], axis=0
    )
    got = lax.all_to_all(chunks, "by", split_axis=0, concat_axis=0, tiled=True)
    routed = jnp.swapaxes(got, 0, 1).reshape(V, rows_x, rows_y + 2 * h, depth)
    padded_start, weight, routed = lax.optimization_barrier((padded_start, weight, routed))

    reach = SHIFT + h
    prev_rows = (reach, h, reach, 0)
    next_rows = (0, reach, h, reach)
    prev_send = jnp.concatenate(
        [routed[w, rows_x - prev_rows[w] :] for w in range(V) if prev_rows[w]], axis=0
    )
    next_send = jnp.concatenate(
        [routed[w, : next_rows[w]] for w in range(V) if next_rows[w]], axis=0
    )
    prev_got = lax.ppermute(prev_send, "bx", shift_pairs(nx, 1))
    next_got = lax.ppermute(next_send, "bx", shift_pairs(nx, -1))
    blurred = blur_views(padded_start, taps_x, taps_y, fwd_z, V)
    blurred, prev_got, next_got = lax.optimization_barrier((blurred, prev_got, next_got))

    registered = []
    at_prev = 0
    at_next = 0
    for w in range(V):
        parts = []
        if prev_rows[w]:
            parts.append(prev_got[at_prev : at_prev + prev_rows[w]])
            at_prev += prev_rows[w]
        parts.append(routed[w])
        if next_rows[w]:
            parts.append(next_got[at_next : at_next + next_rows[w]])
            at_next += next_rows[w]
        ext = jnp.concatenate(parts, axis=0)
        moved = lax.dynamic_slice_in_dim(
            ext, prev_rows[w] - h + offsets[w, 0], rows_x + 2 * h, axis=0
        )
        registered.append(jnp.where(inside[:, :, None], moved.astype(jnp.float32), 0.0))
    registered = jnp.stack(registered)

    estimate = start
    for sweep in range(ITERS):
        if sweep == 0:
            source = blurred
        else:
            source = halo_rows_cols(estimate, 2 * h)
        estimate = rl_step(source, registered, estimate, weight, taps_x, taps_y, background,
                           fwd_z, adj_z, sweep == 0)
    return estimate


def solution(mesh):
    return jax.shard_map(
        local,
        mesh=mesh,
        in_specs=(P(None, ("bx", "by"), None, None), P(), P(), P(), P(), P(), P("bx", "by", None)),
        out_specs=P("bx", "by", None),
        check_vma=False,
    )
```

```python
import jax
import jax.numpy as jnp
from jax import lax
from jax.sharding import PartitionSpec as P
from jax.experimental import pallas as pl
from jax.experimental.pallas import tpu as pltpu

V = 4
SHIFT = 16
ITERS = 2
HIGHEST = lax.Precision.HIGHEST
MATMUL = lax.Precision.HIGH
DEEP = 72


def shift_pairs(count, step):
    if step > 0:
        return [(i, i + step) for i in range(count - step)]
    return [(i - step, i) for i in range(count + step)]


def halo_2d(block, width):
    nx = lax.axis_size("bx")
    ny = lax.axis_size("by")
    low = block.astype(jnp.bfloat16)
    w = width
    up = lax.ppermute(low[-w:], "bx", shift_pairs(nx, 1))
    down = lax.ppermute(low[:w], "bx", shift_pairs(nx, -1))
    left = lax.ppermute(low[:, -w:], "by", shift_pairs(ny, 1))
    right = lax.ppermute(low[:, :w], "by", shift_pairs(ny, -1))

    def corner(part, dx, dy):
        pairs = []
        for i in range(nx):
            for j in range(ny):
                ti, tj = i + dx, j + dy
                if 0 <= ti < nx and 0 <= tj < ny:
                    pairs.append((i * ny + j, ti * ny + tj))
        return lax.ppermute(part, ("bx", "by"), pairs)

    up_left = corner(low[-w:, -w:], 1, 1)
    up_right = corner(low[-w:, :w], 1, -1)
    down_left = corner(low[:w, -w:], -1, 1)
    down_right = corner(low[:w, :w], -1, -1)
    f = block.dtype
    top = jnp.concatenate([up_left, up, up_right], axis=1).astype(f)
    mid = jnp.concatenate([left.astype(f), block, right.astype(f)], axis=1)
    bottom = jnp.concatenate([down_left, down, down_right], axis=1).astype(f)
    return jnp.concatenate([top, mid, bottom], axis=0)


def halo_rows_cols(block, width):
    nx = lax.axis_size("bx")
    ny = lax.axis_size("by")
    w = width
    f = block.dtype
    low = jnp.bfloat16
    up = lax.ppermute(block[-w:].astype(low), "bx", shift_pairs(nx, 1))
    down = lax.ppermute(block[:w].astype(low), "bx", shift_pairs(nx, -1))
    tall_right = jnp.concatenate([up[:, -w:], block[:, -w:].astype(low), down[:, -w:]], axis=0)
    tall_left = jnp.concatenate([up[:, :w], block[:, :w].astype(low), down[:, :w]], axis=0)
    left = lax.ppermute(tall_right, "by", shift_pairs(ny, 1))
    right = lax.ppermute(tall_left, "by", shift_pairs(ny, -1))
    middle = jnp.concatenate([up.astype(f), block, down.astype(f)], axis=0)
    return jnp.concatenate([left.astype(f), middle, right.astype(f)], axis=1)


def band_rows(taps, extent):
    length = taps.shape[1]
    distance = jnp.arange(extent + length - 1)[None, :] - jnp.arange(extent)[:, None]
    picked = distance[:, :, None] == jnp.arange(length)[None, None, :]
    return jnp.sum(jnp.where(picked[None], taps[:, None, None, :], 0.0), axis=3)


def depth_band(taps, extent):
    length = taps.shape[1]
    middle = (length - 1) // 2
    distance = jnp.arange(extent)[:, None] - jnp.arange(extent)[None, :] + middle
    picked = distance[:, :, None] == jnp.arange(length)[None, None, :]
    return jnp.sum(jnp.where(picked[None], taps[:, None, None, :], 0.0), axis=3)


def conv_xy(src_ref, t_ref, dst_ref, tx_ref, ty_ref, v, flip, count, chunk, taps, cols_out,
            finish=None):
    def tap(ref, k):
        return ref[v, taps - 1 - k] if flip else ref[v, k]

    def rows(c, carry):
        r0 = pl.multiple_of(c * chunk, chunk)
        acc = tap(tx_ref, 0) * src_ref[pl.ds(r0, chunk)]
        for a in range(1, taps):
            acc = acc + tap(tx_ref, a) * src_ref[pl.ds(r0 + a, chunk)]
        t_ref[...] = acc
        acc2 = tap(ty_ref, 0) * t_ref[:, pl.ds(0, cols_out), :]
        for b in range(1, taps):
            acc2 = acc2 + tap(ty_ref, b) * t_ref[:, pl.ds(b, cols_out), :]
        if finish is None:
            dst_ref[pl.ds(r0, chunk)] = acc2
        else:
            finish(pl.ds(r0, chunk), acc2)
        return carry

    lax.fori_loop(0, count // chunk, rows, 0, unroll=4)


def blur_views(field, taps_x, taps_y, fwd_z, views):
    rows_f, cols_f, depth = field.shape
    taps = taps_x.shape[1]
    rows_r = rows_f - (taps - 1)
    cols_r = cols_f - (taps - 1)
    chunk = 2
    deep = DEEP
    f32 = jnp.float32

    def kernel(tx_ref, ty_ref, field_ref, fz_ref, out_ref, q_ref, t1_ref):
        v = pl.program_id(0)
        conv_xy(field_ref, t1_ref, q_ref, tx_ref, ty_ref, v, False, rows_r, chunk, taps, cols_r)

        def depth_rows(c, carry):
            r0 = pl.multiple_of(c * deep, deep)
            flat = q_ref[pl.ds(r0, deep)].reshape(deep * cols_r, depth)
            blurred = jnp.dot(flat, fz_ref[0], precision=MATMUL, preferred_element_type=f32)
            out_ref[0, pl.ds(r0, deep)] = blurred.reshape(deep, cols_r, depth)
            return carry

        lax.fori_loop(0, rows_r // deep, depth_rows, 0)

    smem = pl.BlockSpec(memory_space=pltpu.SMEM)
    return pl.pallas_call(
        kernel,
        grid=(views,),
        in_specs=[
            smem,
            smem,
            pl.BlockSpec(field.shape, lambda v: (0, 0, 0)),
            pl.BlockSpec((1, depth, depth), lambda v: (v, 0, 0)),
        ],
        out_specs=pl.BlockSpec((1, rows_r, cols_r, depth), lambda v: (v, 0, 0, 0)),
        out_shape=jax.ShapeDtypeStruct((views, rows_r, cols_r, depth), f32),
        scratch_shapes=[
            pltpu.VMEM((rows_r, cols_r, depth), f32),
            pltpu.VMEM((chunk, cols_f, depth), f32),
        ],
        compiler_params=pltpu.CompilerParams(dimension_semantics=("arbitrary",)),
    )(taps_x, taps_y, field, fwd_z)


def rl_step(source, registered, estimate, weight, taps_x, taps_y, bg, fwd_z, adj_z, given):
    views, rows_r, cols_r, depth = registered.shape
    rows, cols = estimate.shape[:2]
    taps = taps_x.shape[1]
    cols_f = cols_r + taps - 1
    chunk = 2
    deep = DEEP
    f32 = jnp.float32

    def kernel(tx_ref, ty_ref, bg_ref, src_ref, reg_ref, est_ref, w_ref, fz_ref, az_ref,
               out_ref, q_ref, t1_ref, t2_ref, s_ref):
        v = pl.program_id(0)
        if not given:
            conv_xy(src_ref, t1_ref, q_ref, tx_ref, ty_ref, v, False, rows_r, chunk, taps, cols_r)

        def depth_rows(c, carry):
            r0 = pl.multiple_of(c * deep, deep)
            if given:
                blurred = src_ref[0, pl.ds(r0, deep)].reshape(deep * cols_r, depth)
            else:
                flat = q_ref[pl.ds(r0, deep)].reshape(deep * cols_r, depth)
                blurred = jnp.dot(flat, fz_ref[0], precision=MATMUL, preferred_element_type=f32)
            reg = reg_ref[0, pl.ds(r0, deep)].astype(f32).reshape(deep * cols_r, depth)
            ratio = reg / (blurred + bg_ref[v])
            back = jnp.dot(ratio, az_ref[0], precision=MATMUL, preferred_element_type=f32)
            q_ref[pl.ds(r0, deep)] = back.reshape(deep, cols_r, depth)
            return carry

        lax.fori_loop(0, rows_r // deep, depth_rows, 0)

        def finish(rs, acc2):
            @pl.when(v == 0)
            def _():
                s_ref[rs] = acc2

            @pl.when((v > 0) & (v < views - 1))
            def _():
                s_ref[rs] = s_ref[rs] + acc2

            @pl.when(v == views - 1)
            def _():
                out_ref[rs] = est_ref[rs] * (s_ref[rs] + acc2) / w_ref[rs]

        conv_xy(q_ref, t2_ref, None, tx_ref, ty_ref, v, True, rows, chunk, taps, cols, finish)

    smem = pl.BlockSpec(memory_space=pltpu.SMEM)
    whole3 = lambda shape: pl.BlockSpec(shape, lambda v: (0, 0, 0))
    per_view = pl.BlockSpec((1, rows_r, cols_r, depth), lambda v: (v, 0, 0, 0))
    return pl.pallas_call(
        kernel,
        grid=(views,),
        in_specs=[
            smem,
            smem,
            smem,
            per_view if given else whole3(source.shape),
            per_view,
            whole3(estimate.shape),
            whole3(weight.shape),
            pl.BlockSpec((1, depth, depth), lambda v: (v, 0, 0)),
            pl.BlockSpec((1, depth, depth), lambda v: (v, 0, 0)),
        ],
        out_specs=whole3(estimate.shape),
        out_shape=jax.ShapeDtypeStruct(estimate.shape, f32),
        scratch_shapes=[
            pltpu.VMEM((rows_r, cols_r, depth), f32),
            pltpu.VMEM((chunk, cols_f, depth), f32),
            pltpu.VMEM((chunk, cols_r, depth), f32),
            pltpu.VMEM((rows, cols, depth), f32),
        ],
        compiler_params=pltpu.CompilerParams(dimension_semantics=("arbitrary",)),
    )(taps_x, taps_y, bg, source, registered, estimate, weight, fwd_z, adj_z)


def local(views, offsets, background, psf_x, psf_y, psf_z, start):
    rows_x, rows_y, depth = start.shape
    nx = lax.axis_size("bx")
    ny = lax.axis_size("by")
    full_x = rows_x * nx
    full_y = rows_y * ny
    middle = (psf_x.shape[1] - 1) // 2
    h = middle
    ix = lax.axis_index("bx")
    iy = lax.axis_index("by")

    padded_start = halo_rows_cols(start, 2 * h)

    taps_x = psf_x / jnp.sum(psf_x, axis=1, keepdims=True)
    taps_y = psf_y / jnp.sum(psf_y, axis=1, keepdims=True)
    taps_z = psf_z / jnp.sum(psf_z, axis=1, keepdims=True)
    fwd_x = band_rows(taps_x, rows_x + 2 * h)
    fwd_y = band_rows(taps_y, rows_y + 2 * h)
    fwd_z = depth_band(taps_z, depth)
    adj_x = band_rows(taps_x[:, ::-1], rows_x)
    adj_y = band_rows(taps_y[:, ::-1], rows_y)
    adj_z = jnp.swapaxes(fwd_z, 1, 2)

    base_x = ix * rows_x - h + jnp.arange(rows_x + 2 * h, dtype=jnp.int32)
    base_y = iy * rows_y - h + jnp.arange(rows_y + 2 * h, dtype=jnp.int32)
    inside_x = (base_x >= 0) & (base_x < full_x)
    inside_y = (base_y >= 0) & (base_y < full_y)
    inside = inside_x[:, None] & inside_y[None, :]

    cover_x = (
        (base_x[None, :] + offsets[:, 0:1] >= 0) & (base_x[None, :] + offsets[:, 0:1] < full_x)
    ) & inside_x[None, :]
    cover_y = (
        (base_y[None, :] + offsets[:, 1:2] >= 0) & (base_y[None, :] + offsets[:, 1:2] < full_y)
    ) & inside_y[None, :]
    weight_x = jnp.einsum("vij,vj->vi", adj_x, cover_x.astype(jnp.float32), precision=HIGHEST)
    weight_y = jnp.einsum("vij,vj->vi", adj_y, cover_y.astype(jnp.float32), precision=HIGHEST)
    weight_z = jnp.sum(adj_z, axis=1)
    weight = jnp.sum(
        weight_x[:, :, None, None] * weight_y[:, None, :, None] * weight_z[:, None, None, :], axis=0
    )

    pad_y = SHIFT + h
    vpad = jnp.pad(views, ((0, 0), (0, 0), (pad_y, pad_y), (0, 0)))
    cols = full_y + 2 * h
    shifted = jnp.stack(
        [
            lax.dynamic_slice_in_dim(vpad[w], SHIFT + offsets[w, 1], cols, axis=1)
            for w in range(V)
        ]
    )
    chunks = jnp.stack(
        [shifted[:, :, k * rows_y : k * rows_y + rows_y + 2 * h] for k in range(ny)], axis=0
    )
    got = lax.all_to_all(chunks, "by", split_axis=0, concat_axis=0, tiled=True)
    routed = jnp.swapaxes(got, 0, 1).reshape(V, rows_x, rows_y + 2 * h, depth)
    padded_start, weight, routed = lax.optimization_barrier((padded_start, weight, routed))

    reach = SHIFT + h
    prev_rows = (reach, h, reach, 0)
    next_rows = (0, reach, h, reach)
    prev_send = jnp.concatenate(
        [routed[w, rows_x - prev_rows[w] :] for w in range(V) if prev_rows[w]], axis=0
    )
    next_send = jnp.concatenate(
        [routed[w, : next_rows[w]] for w in range(V) if next_rows[w]], axis=0
    )
    prev_got = lax.ppermute(prev_send, "bx", shift_pairs(nx, 1))
    next_got = lax.ppermute(next_send, "bx", shift_pairs(nx, -1))
    blurred = blur_views(padded_start, taps_x, taps_y, fwd_z, V)
    blurred, prev_got, next_got = lax.optimization_barrier((blurred, prev_got, next_got))

    registered = []
    at_prev = 0
    at_next = 0
    for w in range(V):
        parts = []
        if prev_rows[w]:
            parts.append(prev_got[at_prev : at_prev + prev_rows[w]])
            at_prev += prev_rows[w]
        parts.append(routed[w])
        if next_rows[w]:
            parts.append(next_got[at_next : at_next + next_rows[w]])
            at_next += next_rows[w]
        ext = jnp.concatenate(parts, axis=0)
        moved = lax.dynamic_slice_in_dim(
            ext, prev_rows[w] - h + offsets[w, 0], rows_x + 2 * h, axis=0
        )
        registered.append(jnp.where(inside[:, :, None], moved.astype(jnp.float32), 0.0))
    registered = jnp.stack(registered)

    estimate = start
    for sweep in range(ITERS):
        if sweep == 0:
            source = blurred
        else:
            source = halo_rows_cols(estimate, 2 * h)
        estimate = rl_step(source, registered, estimate, weight, taps_x, taps_y, background,
                           fwd_z, adj_z, sweep == 0)
    return estimate


def solution(mesh):
    return jax.shard_map(
        local,
        mesh=mesh,
        in_specs=(P(None, ("bx", "by"), None, None), P(), P(), P(), P(), P(), P("bx", "by", None)),
        out_specs=P("bx", "by", None),
        check_vma=False,
    )
```
